32 devices in a mesh: leaf: 16 (over z, x, core), site: 2 (over y).
Axes of the slice: x: 2, y: 2, z: 4, core: 2. Of those that a mesh axis runs over, the one named last changes fastest.
Arguments:
- tips: float32 [128, 64, 256], P('leaf', None, 'site'), as said below
- parents: int32 [224], P('leaf'), may hold values from 8 to 14, as said below
- branch_lengths: float32 [224], P('leaf'), may hold values from 0.02 to 0.6
- top_parents: int32 [30], replicated, may hold values from 16 to 30, as said below
- top_lengths: float32 [30], replicated, may hold values from 0.02 to 0.6
- weights: int32 [256], P('site'), may hold values from 1 to 16
- eig_vectors: float32 [64, 64], replicated, as said below
- eig_inverse: float32 [64, 64], replicated, as said below
- eig_values: float32 [64], replicated, as said below
- labeled_rates: float32 [64, 64], replicated, as said below
- root_freq: float32 [64], replicated, as said below
Outputs:
- local_counts: float32 [224], P('leaf')
- top_counts: float32 [30], replicated
- site_loglik: float32 [256], P('site')
The draws below stay inside these ranges and needn't reach their ends.
Inputs may be any that keep to these rules, and one draw needn't show every extreme that they name: `parents`: within each block of 14 entries (one subtree) the entries form a binary tree: every entry is larger than its own position in the block, every internal node 8 to 14 is named by exactly two entries. `top_parents`: A binary tree over the subtrees: every entry is larger than its own position, every node 16 to 2 * 16 - 2 is named by exactly two entries. `tips`: Positive. eig_vectors diag(eig_values) eig_inverse is a reversible rate matrix Q on the first 61 states with stationary frequencies root_freq and mean rate 1, and eig_inverse eig_vectors is the identity; rows, columns and eigenvalues past 61 are those of the identity and 0. `eig_inverse`: the inverse of eig_vectors, as above. `eig_values`: eigenvalues of Q, at most 0. `labeled_rates`: Off-diagonal rates of Q for a symmetric set of counted state pairs, 0 elsewhere. `root_freq`: positive on the first 61 states, 0 past them, summing to 1.
All inputs are finite; a program needn't handle non-finite values.
Results may differ from the reference program's by a relative error of at most 0.0003.
Values sent between devices are 32-bit elements; how exact they have to be, the bound alone decides.
No kernel may reach another device: no remote copies, remote signals or barrier semaphores. Data moves between devices by JAX's collectives and lax.ppermute only.
A program may use at most 64 MiB of HBM per device.

```python
import math
import jax
import jax.numpy as jnp
from jax import lax

STATES = 64
CODONS = 61
LEAVES_DEV = 8
TAXA = 128
SITES = 256
BR_DEV = 14
BRANCHES = 224
TOP_BR = 30
N_LEAF = 16


def random_tree(seed_key, leaf_count):
    active = jnp.arange(leaf_count, dtype=jnp.int32)
    parent = jnp.zeros((2 * leaf_count - 2,), jnp.int32)

    def merge_step(counter, state_triple):
        active, parent, seed_key = state_triple
        seed_key, first_key, second_key = jax.random.split(seed_key, 3)
        remaining = leaf_count - counter
        first = jax.random.randint(first_key, (), 0, remaining)
        second = jax.random.randint(second_key, (), 0, remaining - 1)
        second = second + (second >= first).astype(jnp.int32)
        newest = (leaf_count + counter).astype(jnp.int32)
        parent = parent.at[active[first]].set(newest).at[active[second]].set(newest)
        lowest = jnp.minimum(first, second)
        highest = jnp.maximum(first, second)
        last_node = active[remaining - 1]
        active = active.at[lowest].set(newest)
        active = active.at[highest].set(last_node)
        return (active, parent, seed_key)
    _, parent, _ = lax.fori_loop(0, leaf_count - 1, merge_step, (active, parent, seed_key))
    return parent


def draw_parents(key, part):
    groups = BRANCHES // BR_DEV
    indices = jnp.arange(groups, dtype=jnp.int32)
    forest = jax.vmap(lambda group: random_tree(jax.random.fold_in(key, 1000 + group), LEAVES_DEV))(indices)
    return forest.reshape(BRANCHES)


def draw_top_parents(key, part):
    return random_tree(jax.random.fold_in(key, 3), TOP_BR // 2 + 1)


def draw_tips(key, part):
    states_key, noise_key = jax.random.split(jax.random.fold_in(key, 5))
    observed = jax.random.randint(states_key, (TAXA, SITES), 0, CODONS)
    noise_draw = jax.random.uniform(noise_key, (TAXA, STATES, SITES), jnp.float32)
    observed_hot = (observed[:, None, :] == jnp.arange(STATES)[None, :, None]).astype(jnp.float32)
    return (0.02 + 0.1 * noise_draw + observed_hot).astype(jnp.float32)


def codon_model(key):
    rate_key, freq_key, label_key = jax.random.split(jax.random.fold_in(key, 11), 3)
    raw_rates = jax.random.uniform(rate_key, (CODONS, CODONS), jnp.float32, 0.1, 2.0)
    exchange_rates = (raw_rates + raw_rates.T) / 2.0
    raw_freq = jax.random.uniform(freq_key, (CODONS,), jnp.float32, 0.5, 2.0)
    freq = raw_freq / jnp.sum(raw_freq)
    off_diag = exchange_rates * freq[None, :] * (1.0 - jnp.eye(CODONS, dtype=jnp.float32))
    diag_rates = -jnp.sum(off_diag, axis=1)
    mean_rate = -jnp.sum(freq * diag_rates)
    off_diag = off_diag / mean_rate
    diag_rates = diag_rates / mean_rate
    root_freq_sqrt = jnp.sqrt(freq)
    symmetric = off_diag * root_freq_sqrt[:, None] / root_freq_sqrt[None, :] + jnp.diag(diag_rates)
    symmetric = (symmetric + symmetric.T) / 2.0
    values, vectors = jnp.linalg.eigh(symmetric)
    right = vectors / root_freq_sqrt[:, None]
    left = vectors.T * root_freq_sqrt[None, :]
    label_draw = jax.random.bernoulli(label_key, 0.6, (CODONS, CODONS))
    label_draw = jnp.logical_and(label_draw, label_draw.T).astype(jnp.float32)
    labeled = off_diag * label_draw
    full_right = jnp.eye(STATES, dtype=jnp.float32).at[:CODONS, :CODONS].set(right)
    full_left = jnp.eye(STATES, dtype=jnp.float32).at[:CODONS, :CODONS].set(left)
    full_values = jnp.zeros((STATES,), jnp.float32).at[:CODONS].set(values)
    full_labeled = jnp.zeros((STATES, STATES), jnp.float32).at[:CODONS, :CODONS].set(labeled)
    full_freq = jnp.zeros((STATES,), jnp.float32).at[:CODONS].set(freq)
    return (full_right, full_left, full_values, full_labeled, full_freq)


def draw_eig_vectors(key, part):
    return codon_model(key)[0].astype(jnp.float32)


def draw_eig_inverse(key, part):
    return codon_model(key)[1].astype(jnp.float32)


def draw_eig_values(key, part):
    return codon_model(key)[2].astype(jnp.float32)


def draw_labeled_rates(key, part):
    return codon_model(key)[3].astype(jnp.float32)


def draw_root_freq(key, part):
    return codon_model(key)[4].astype(jnp.float32)


def plant(drawn, own_key, low, top_value):
    longest = drawn.shape.index(max(drawn.shape))
    spots = []
    for shift in (0, 1):
        where = [jax.random.randint(jax.random.fold_in(own_key, axis), (), 0, length) for axis, length in enumerate(drawn.shape)]
        where[longest] = (where[longest] + shift) % drawn.shape[longest]
        spots.append(tuple(where))
    return drawn.at[spots[0]].set(low).at[spots[1]].set(top_value)


def shard_levels(key, extent, cuts, low, largest):
    level, own = 1.0, jax.random.fold_in(key, 6)
    for axis_at, shards_of in cuts:
        draws = jnp.exp(jax.random.uniform(jax.random.fold_in(own, axis_at), (shards_of,), jnp.float32, low / len(cuts), largest / len(cuts)))
        level = level * jnp.repeat(draws, extent[axis_at] // shards_of).reshape([-1 if axis == axis_at else 1 for axis in range(len(extent))])
    return level


def setup_inputs(seed: int = 0) -> dict:
    key_list = jax.random.split(jax.random.key(seed), 12)
    return {
        "tips": draw_tips(jax.random.fold_in(key_list[11], 71), 0),
        "parents": draw_parents(jax.random.fold_in(key_list[11], 71), 0),
        "branch_lengths": jnp.clip(jnp.exp(math.log(0.6) - 3.4011974 * jax.random.uniform(key_list[2], (BRANCHES,), jnp.float32) ** shard_levels(key_list[2], (BRANCHES,), ((0, 16),), -0.2, 0.2)), 0.02, 0.6),
        "top_parents": draw_top_parents(jax.random.fold_in(key_list[11], 71), 0),
        "top_lengths": jnp.clip(jnp.exp(jax.random.uniform(key_list[4], (TOP_BR,), jnp.float32, math.log(0.02), math.log(0.6))), 0.02, 0.6),
        "weights": plant(jax.random.randint(key_list[5], (SITES,), 1, 17), jax.random.fold_in(key_list[5], 1), 1, 16).astype(jnp.int32),
        "eig_vectors": draw_eig_vectors(jax.random.fold_in(key_list[11], 71), 0),
        "eig_inverse": draw_eig_inverse(jax.random.fold_in(key_list[11], 71), 0),
        "eig_values": draw_eig_values(jax.random.fold_in(key_list[11], 71), 0),
        "labeled_rates": draw_labeled_rates(jax.random.fold_in(key_list[11], 71), 0),
        "root_freq": draw_root_freq(jax.random.fold_in(key_list[11], 71), 0),
    }


PRECISE = lax.Precision.HIGHEST

def propagate(eig_vectors, eig_inverse, eig_values, branch, partial_value):
    projected = jnp.dot(eig_inverse, partial_value, precision=PRECISE)
    damping = jnp.exp(eig_values * branch)
    return jnp.dot(eig_vectors, damping[:, None] * projected, precision=PRECISE)

def integrals(eig_values, branch):
    spread = (eig_values[:, None] - eig_values[None, :]) * branch
    near_zero = jnp.abs(spread) < 0.0001
    divisor = jnp.where(near_zero, jnp.ones_like(spread), spread)
    growth = jnp.where(near_zero, 1.0 + spread / 2.0 + spread * spread / 6.0, jnp.expm1(spread) / divisor)
    return branch * jnp.exp(eig_values[None, :] * branch) * growth

def climb_tree(leaf_rows, tree_links, lengths, eig_vectors, eig_inverse, eig_values):
    leaf_count = leaf_rows.shape[0]
    edge_count = tree_links.shape[0]
    inside = jnp.concatenate([leaf_rows, jnp.ones((leaf_count - 1, leaf_rows.shape[1], leaf_rows.shape[2]), jnp.float32)], axis=0)

    def finish(inside, log_scale, position):
        node_row = lax.dynamic_index_in_dim(inside, position, 0, keepdims=False)
        biggest = jnp.max(node_row, axis=0)
        internal = position >= leaf_count
        node_row = jnp.where(internal, node_row / biggest, node_row)
        log_scale = log_scale + jnp.where(internal, jnp.log(biggest), jnp.zeros_like(biggest))
        return (lax.dynamic_update_index_in_dim(inside, node_row, position, 0), log_scale, node_row)

    def visit(position, state_pair):
        inside, log_scale = state_pair
        inside, log_scale, node_row = finish(inside, log_scale, position)
        message = propagate(eig_vectors, eig_inverse, eig_values, lengths[position], node_row)
        parent_node = tree_links[position]
        target = lax.dynamic_index_in_dim(inside, parent_node, 0, keepdims=False) * message
        return (lax.dynamic_update_index_in_dim(inside, target, parent_node, 0), log_scale)
    log_scale = jnp.zeros((leaf_rows.shape[2],), jnp.float32)
    inside, log_scale = lax.fori_loop(0, edge_count, visit, (inside, log_scale))
    inside, log_scale, _ = finish(inside, log_scale, edge_count)
    return (inside, log_scale)

def descend(inside, tree_links, lengths, root_out, weight, eig_vectors, eig_inverse, eig_values, count_basis):
    node_count = inside.shape[0]
    edge_count = node_count - 1
    labels = jnp.arange(node_count, dtype=jnp.int32)
    edges = jnp.arange(edge_count, dtype=jnp.int32)
    member = tree_links[None, :] == labels[:, None]
    child_sum = jnp.sum(jnp.where(member, edges[None, :], 0), axis=1).astype(jnp.int32)
    sibling = (child_sum[tree_links] - edges).astype(jnp.int32)
    outside = jnp.zeros_like(inside).at[node_count - 1].set(root_out)

    def visit(counter, state_pair):
        outside, totals = state_pair
        position = edge_count - 1 - counter
        parent_node = tree_links[position]
        beside = sibling[position]
        branch = lengths[position]
        partner = propagate(eig_vectors, eig_inverse, eig_values, lengths[beside], lax.dynamic_index_in_dim(inside, beside, 0, keepdims=False))
        arriving = lax.dynamic_index_in_dim(outside, parent_node, 0, keepdims=False) * partner
        weighted = jnp.dot(eig_vectors.T, arriving, precision=PRECISE)
        projected = jnp.dot(eig_inverse, lax.dynamic_index_in_dim(inside, position, 0, keepdims=False), precision=PRECISE)
        damping = jnp.exp(eig_values * branch)
        denominator = jnp.sum(weighted * damping[:, None] * projected, axis=0)
        mixed_rows = jnp.dot(count_basis * integrals(eig_values, branch), projected, precision=PRECISE)
        numerator = jnp.sum(weighted * mixed_rows, axis=0)
        pattern_total = jnp.sum(weight * numerator / denominator)
        outward = jnp.dot(eig_inverse.T, damping[:, None] * weighted, precision=PRECISE)
        outward = outward / jnp.max(outward, axis=0)
        outside = lax.dynamic_update_index_in_dim(outside, outward, position, 0)
        return (outside, totals.at[position].set(pattern_total))
    totals = jnp.zeros((edge_count,), jnp.float32)
    return lax.fori_loop(0, edge_count, visit, (outside, totals))

def reference(tips, parents, branch_lengths, top_parents, top_lengths, weights, eig_vectors, eig_inverse, eig_values, labeled_rates, root_freq):
    codon_mask = (jnp.arange(STATES) < CODONS).astype(jnp.float32)
    count_basis = jnp.dot(jnp.dot(eig_inverse, labeled_rates, precision=PRECISE), eig_vectors, precision=PRECISE)
    tip_blocks = tips.reshape(N_LEAF, LEAVES_DEV, STATES, SITES)
    parent_blocks = parents.reshape(N_LEAF, BR_DEV)
    length_blocks = branch_lengths.reshape(N_LEAF, BR_DEV)

    def upward(subtree):
        leaf_rows, tree_links, lengths = subtree
        inside, log_scale = climb_tree(leaf_rows * codon_mask[None, :, None], tree_links, lengths, eig_vectors, eig_inverse, eig_values)
        return (inside[-1], log_scale)
    root_rows, root_logs = lax.map(upward, (tip_blocks, parent_blocks, length_blocks))
    top_inside, top_logs = climb_tree(root_rows, top_parents, top_lengths, eig_vectors, eig_inverse, eig_values)
    weight = weights.astype(jnp.float32)
    likelihood = jnp.sum(root_freq[:, None] * top_inside[-1], axis=0)
    site_loglik = (jnp.log(likelihood) + top_logs + jnp.sum(root_logs, axis=0)) / TAXA
    root_start = jnp.broadcast_to(root_freq[:, None], (STATES, SITES))
    top_outside, top_totals = descend(top_inside, top_parents, top_lengths, root_start, weight, eig_vectors, eig_inverse, eig_values, count_basis)

    def downward(subtree):
        leaf_rows, tree_links, lengths, root_out = subtree
        inside, _ = climb_tree(leaf_rows * codon_mask[None, :, None], tree_links, lengths, eig_vectors, eig_inverse, eig_values)
        _, totals = descend(inside, tree_links, lengths, root_out, weight, eig_vectors, eig_inverse, eig_values, count_basis)
        return totals
    local_totals = lax.map(downward, (tip_blocks, parent_blocks, length_blocks, top_outside[:N_LEAF]))
    weight_total = jnp.sum(weight)
    return (local_totals.reshape(BRANCHES) / weight_total, top_totals / weight_total, site_loglik)
```

```python
import functools

import jax
import jax.numpy as jnp
from jax import lax
from jax.experimental import pallas as pl
from jax.experimental.pallas import tpu as pltpu
from jax.sharding import PartitionSpec as P

CODONS = 61

PRECISE = lax.Precision.HIGHEST
F32 = jnp.float32
VMEM_LIMIT = 48 * 1024 * 1024


def _dot(a, b):
    return jnp.dot(a, b, precision=PRECISE, preferred_element_type=F32)


def integrals(eig_values, branch):
    spread = (eig_values[:, None] - eig_values[None, :]) * branch
    near_zero = jnp.abs(spread) < 0.0001
    divisor = jnp.where(near_zero, jnp.ones_like(spread), spread)
    growth = jnp.where(
        near_zero, 1.0 + spread / 2.0 + spread * spread / 6.0, jnp.expm1(spread) / divisor
    )
    return branch * jnp.exp(eig_values[None, :] * branch) * growth


def branch_matrices(eig_vectors, eig_inverse, eig_values, count_basis, lengths):
    damping = jnp.exp(eig_values[None, :] * lengths[:, None])
    trans = jnp.einsum(
        "sk,ekt->est", eig_vectors, damping[:, :, None] * eig_inverse[None], precision=PRECISE
    )
    basis = count_basis[None] * jax.vmap(lambda t: integrals(eig_values, t))(lengths)
    mixed = jnp.einsum("sk,ekl->esl", eig_vectors, basis, precision=PRECISE)
    mixed = jnp.einsum("esl,lt->est", mixed, eig_inverse, precision=PRECISE)
    return trans, jnp.swapaxes(trans, 1, 2), mixed


def _climb_kernel(par_ref, leaf_ref, p_ref, m_ref, root_ref, msg_ref, num_ref, inner_ref, *,
                  mask):
    leaf_count = leaf_ref.shape[0]
    edge_count, states, columns = msg_ref.shape
    inner_ref[...] = jnp.ones(inner_ref.shape, F32)
    if mask:
        keep = (lax.broadcasted_iota(jnp.int32, (states, columns), 0) < CODONS).astype(F32)
    unroll = edge_count <= 32

    def push(c, x):
        msg = _dot(p_ref[c], x)
        msg_ref[c] = msg
        num_ref[c] = _dot(m_ref[c], x)
        p = par_ref[c] - leaf_count
        inner_ref[p] = inner_ref[p] * msg

    def leaf_step(c, carry):
        x = leaf_ref[c, 0:states, :]
        if mask:
            x = x * keep
        push(c, x)
        return carry

    lax.fori_loop(0, leaf_count, leaf_step, 0, unroll=unroll)

    def inner_step(c, logs):
        x = inner_ref[c - leaf_count]
        big = jnp.max(x, axis=0, keepdims=True)
        push(c, x / big)
        return logs + jnp.log(big)

    logs = lax.fori_loop(
        leaf_count, edge_count, inner_step, jnp.zeros((1, columns), F32), unroll=unroll
    )
    x = inner_ref[leaf_count - 2]
    big = jnp.max(x, axis=0, keepdims=True)
    root_ref[0:states, :] = x / big
    root_ref[states:states + 1, :] = logs + jnp.log(big)


def climb(parents, leaves, trans, mixed, mask):
    leaf_count, _, columns = leaves.shape
    edge_count, states, _ = trans.shape
    vmem = pl.BlockSpec(memory_space=pltpu.VMEM)
    return pl.pallas_call(
        functools.partial(_climb_kernel, mask=mask),
        out_shape=(
            jax.ShapeDtypeStruct((states + 1, columns), F32),
            jax.ShapeDtypeStruct((edge_count, states, columns), F32),
            jax.ShapeDtypeStruct((edge_count, states, columns), F32),
        ),
        in_specs=[pl.BlockSpec(memory_space=pltpu.SMEM), vmem, vmem, vmem],
        out_specs=(vmem, vmem, vmem),
        scratch_shapes=[pltpu.VMEM((leaf_count - 1, states, columns), F32)],
        compiler_params=pltpu.CompilerParams(vmem_limit_bytes=VMEM_LIMIT),
    )(parents, leaves, trans, mixed)


def _descend_kernel(par_ref, pick_ref, out_root_ref, msg_ref, num_ref, pt_ref, w_ref,
                    tot_ref, leaf_out_ref, outside_ref, kids_ref, *, want_leaf):
    edge_count, states, columns = msg_ref.shape
    leaf_count = (edge_count + 2) // 2
    node_count = edge_count + 1
    unroll = edge_count <= 32

    def clear(n, carry):
        kids_ref[n] = 0
        return carry

    lax.fori_loop(0, node_count, clear, 0)

    def add_kid(e, carry):
        p = par_ref[e]
        kids_ref[p] = kids_ref[p] + e
        return carry

    lax.fori_loop(0, edge_count, add_kid, 0)
    outside_ref[leaf_count - 2] = out_root_ref[...]
    w = w_ref[...]

    def arrive(c):
        p = par_ref[c]
        s = kids_ref[p] - c
        arriving = outside_ref[p - leaf_count] * msg_ref[s]
        den = jnp.sum(arriving * msg_ref[c], axis=0, keepdims=True)
        num = jnp.sum(arriving * num_ref[c], axis=0, keepdims=True)
        tot_ref[c] = w * num / den
        return arriving

    def outward(c, arriving):
        out = _dot(pt_ref[c], arriving)
        return out / jnp.max(out, axis=0, keepdims=True)

    def inner_step(i, carry):
        c = edge_count - 1 - i
        outside_ref[c - leaf_count] = outward(c, arrive(c))
        return carry

    lax.fori_loop(0, edge_count - leaf_count, inner_step, 0, unroll=unroll)

    def leaf_step(i, carry):
        arrive(leaf_count - 1 - i)
        return carry

    lax.fori_loop(0, leaf_count, leaf_step, 0, unroll=unroll)
    if want_leaf:
        g = pick_ref[0]
        p = par_ref[g]
        s = kids_ref[p] - g
        leaf_out_ref[...] = outward(g, outside_ref[p - leaf_count] * msg_ref[s])
    else:
        leaf_out_ref[...] = jnp.zeros(leaf_out_ref.shape, F32)


def descend(parents, pick, root_out, msgs, nums, trans_t, weight_row, want_leaf):
    edge_count, states, columns = msgs.shape
    leaf_count = (edge_count + 2) // 2
    vmem = pl.BlockSpec(memory_space=pltpu.VMEM)
    smem = pl.BlockSpec(memory_space=pltpu.SMEM)
    return pl.pallas_call(
        functools.partial(_descend_kernel, want_leaf=want_leaf),
        out_shape=(
            jax.ShapeDtypeStruct((edge_count, 1, columns), F32),
            jax.ShapeDtypeStruct((states, columns), F32),
        ),
        in_specs=[smem, smem, vmem, vmem, vmem, vmem, vmem],
        out_specs=(vmem, vmem),
        scratch_shapes=[
            pltpu.VMEM((leaf_count - 1, states, columns), F32),
            pltpu.SMEM((edge_count + 1,), jnp.int32),
        ],
        compiler_params=pltpu.CompilerParams(vmem_limit_bytes=VMEM_LIMIT),
    )(parents, pick, root_out, msgs, nums, trans_t, weight_row)


def on_device(
    tips,
    parents,
    branch_lengths,
    top_parents,
    top_lengths,
    weights,
    eig_vectors,
    eig_inverse,
    eig_values,
    labeled_rates,
    root_freq,
):
    states = tips.shape[1]
    columns = tips.shape[2]
    local_edges = parents.shape[0]
    groups = lax.axis_size("leaf")
    member_index = lax.axis_index("leaf")
    taxon_count = tips.shape[0] * groups
    count_basis = jnp.dot(
        jnp.dot(eig_inverse, labeled_rates, precision=PRECISE), eig_vectors, precision=PRECISE
    )
    lengths = jnp.concatenate([branch_lengths, top_lengths])
    trans, trans_t, mixed = branch_matrices(
        eig_vectors, eig_inverse, eig_values, count_basis, lengths
    )
    weight = weights.astype(F32)
    weight_row = weight[None, :]

    root_block, msgs, nums = climb(
        parents, tips, trans[:local_edges], mixed[:local_edges], True
    )
    gathered = lax.all_gather(root_block, "leaf", axis=0, tiled=False)
    top_block, top_msgs, top_nums = climb(
        top_parents, gathered, trans[local_edges:], mixed[local_edges:], False
    )
    top_root = top_block[:states]
    top_logs = top_block[states]
    likelihood = jnp.sum(root_freq[:, None] * top_root, axis=0)
    site_loglik = (
        jnp.log(likelihood) + top_logs + jnp.sum(gathered[:, states], axis=0)
    ) / taxon_count
    root_start = jnp.broadcast_to(root_freq[:, None], (states, columns))
    pick = jnp.reshape(member_index, (1,)).astype(jnp.int32)
    top_rows, subtree_out = descend(
        top_parents, pick, root_start, top_msgs, top_nums, trans_t[local_edges:], weight_row,
        True,
    )
    local_rows, _ = descend(
        parents, pick, subtree_out, msgs, nums, trans_t[:local_edges], weight_row, False
    )
    sums = jnp.concatenate(
        [jnp.sum(local_rows[:, 0], axis=1), jnp.sum(top_rows[:, 0], axis=1),
         jnp.sum(weight)[None]]
    )
    sums = lax.psum(sums, "site")
    weight_total = sums[-1]
    local_sum = sums[:local_edges]
    top_sum = sums[local_edges:-1]
    return (local_sum / weight_total, top_sum / weight_total, site_loglik)


def solution(mesh):
    placed = (
        P("leaf", None, "site"),
        P("leaf"),
        P("leaf"),
        P(),
        P(),
        P("site"),
        P(),
        P(),
        P(),
        P(),
        P(),
    )
    return jax.shard_map(
        on_device,
        mesh=mesh,
        in_specs=placed,
        out_specs=(P("leaf"), P(), P("site")),
        check_vma=False,
    )
```

```python
import functools

import jax
import jax.numpy as jnp
from jax import lax
from jax.experimental import pallas as pl
from jax.experimental.pallas import tpu as pltpu
from jax.sharding import PartitionSpec as P

CODONS = 61

PRECISE = lax.Precision.HIGHEST
F32 = jnp.float32
VMEM_LIMIT = 56 * 1024 * 1024
VMEM = pl.BlockSpec(memory_space=pltpu.VMEM)
SMEM = pl.BlockSpec(memory_space=pltpu.SMEM)


def _dot(a, b):
    return jnp.dot(a, b, precision=PRECISE, preferred_element_type=F32)


def integrals(eig_values, branch):
    spread = (eig_values[:, None] - eig_values[None, :]) * branch
    near_zero = jnp.abs(spread) < 0.0001
    divisor = jnp.where(near_zero, jnp.ones_like(spread), spread)
    growth = jnp.where(
        near_zero, 1.0 + spread / 2.0 + spread * spread / 6.0, jnp.expm1(spread) / divisor
    )
    return branch * jnp.exp(eig_values[None, :] * branch) * growth


def _params(edge_count):
    return pltpu.CompilerParams(vmem_limit_bytes=VMEM_LIMIT)


def _unroll(edge_count):
    return edge_count <= 32


def _climb_kernel(par_ref, len_ref, leaf_ref, v_ref, vi_ref, lam_ref,
                  root_ref, msg_ref, x_ref, inner_ref):
    leaf_count = leaf_ref.shape[0]
    edge_count, states, columns = msg_ref.shape
    vecs = v_ref[...]
    inv = vi_ref[...]
    lam = lam_ref[...]
    inner_ref[...] = jnp.ones(inner_ref.shape, F32)
    keep = (lax.broadcasted_iota(jnp.int32, (states, columns), 0) < CODONS).astype(F32)
    unroll = _unroll(edge_count)

    def push(c, x):
        trans = _dot(vecs, jnp.exp(lam * len_ref[c]) * inv)
        msg = _dot(trans, x)
        msg_ref[c] = msg
        x_ref[c] = x
        p = par_ref[c] - leaf_count
        inner_ref[p] = inner_ref[p] * msg

    def leaf_step(c, carry):
        push(c, leaf_ref[c] * keep)
        return carry

    lax.fori_loop(0, leaf_count, leaf_step, 0, unroll=unroll)

    def inner_step(c, logs):
        x = inner_ref[c - leaf_count]
        big = jnp.max(x, axis=0, keepdims=True)
        push(c, x / big)
        return logs + jnp.log(big)

    logs = lax.fori_loop(
        leaf_count, edge_count, inner_step, jnp.zeros((1, columns), F32), unroll=unroll
    )
    x = inner_ref[leaf_count - 2]
    big = jnp.max(x, axis=0, keepdims=True)
    root_ref[0:states, :] = x / big
    root_ref[states:states + 1, :] = logs + jnp.log(big)


def climb(parents, lengths, tips, vecs, inv, lam_col):
    leaf_count, states, columns = tips.shape
    edge_count = parents.shape[0]
    return pl.pallas_call(
        _climb_kernel,
        out_shape=(
            jax.ShapeDtypeStruct((states + 1, columns), F32),
            jax.ShapeDtypeStruct((edge_count, states, columns), F32),
            jax.ShapeDtypeStruct((edge_count, states, columns), F32),
        ),
        in_specs=[SMEM, SMEM, VMEM, VMEM, VMEM, VMEM],
        out_specs=(VMEM, VMEM, VMEM),
        scratch_shapes=[pltpu.VMEM((leaf_count - 1, states, columns), F32)],
        compiler_params=_params(edge_count),
    )(parents, lengths, tips, vecs, inv, lam_col)


def _matrix_kernel(len_ref, top_len_ref, v_ref, vi_ref, lab_ref, lam_ref, lam_row_ref,
                   jl_ref, jt_ref, xs_ref,
                   num_ref, ptl_ref, pt_ref, ptt_ref, mt_ref):
    local_edges = jl_ref.shape[0]
    top_edges = jt_ref.shape[0]
    vecs = v_ref[...]
    inv = vi_ref[...]
    lam = lam_ref[...]
    lam_row = lam_row_ref[...]
    basis = _dot(_dot(inv, lab_ref[...]), vecs)
    vecs_t = vecs.T
    inv_t = inv.T

    def local_step(c, carry):
        t = len_ref[c]
        mixed = _dot(_dot(vecs, basis * jl_ref[c]), inv)
        num_ref[c] = _dot(mixed, xs_ref[c])
        ptl_ref[c] = _dot(inv_t * jnp.exp(lam_row * t), vecs_t)
        return carry

    lax.fori_loop(0, local_edges, local_step, 0, unroll=_unroll(local_edges))

    def top_step(c, carry):
        t = top_len_ref[c]
        pt_ref[c] = _dot(vecs, jnp.exp(lam * t) * inv)
        ptt_ref[c] = _dot(inv_t * jnp.exp(lam_row * t), vecs_t)
        mt_ref[c] = _dot(_dot(vecs, basis * jt_ref[c]), inv)
        return carry

    lax.fori_loop(0, top_edges, top_step, 0, unroll=_unroll(top_edges))


def matrices(lengths, top_lengths, vecs, inv, labeled, lam_col, lam_row, j_local, j_top, xs):
    local_edges, states, columns = xs.shape
    top_edges = top_lengths.shape[0]
    sq = (states, states)
    return pl.pallas_call(
        _matrix_kernel,
        out_shape=(
            jax.ShapeDtypeStruct((local_edges, states, columns), F32),
            jax.ShapeDtypeStruct((local_edges,) + sq, F32),
            jax.ShapeDtypeStruct((top_edges,) + sq, F32),
            jax.ShapeDtypeStruct((top_edges,) + sq, F32),
            jax.ShapeDtypeStruct((top_edges,) + sq, F32),
        ),
        in_specs=[SMEM, SMEM] + [VMEM] * 8,
        out_specs=(VMEM,) * 5,
        compiler_params=_params(top_edges),
    )(lengths, top_lengths, vecs, inv, labeled, lam_col, lam_row, j_local, j_top, xs)


def _lane_put(row, lane, value):
    lanes = lax.broadcasted_iota(jnp.int32, row.shape, 1)
    return jnp.where(lanes == lane, value, row)


def _descend(par_ref, kids_ref, outside_ref, msg_ref, num_ref, pt_ref, w, root_out,
             lane_offset, row, want_leaf=None):
    edge_count = par_ref.shape[0]
    leaf_count = (edge_count + 2) // 2
    node_count = edge_count + 1
    unroll = _unroll(edge_count)

    def clear(n, carry):
        kids_ref[n] = 0
        return carry

    lax.fori_loop(0, node_count, clear, 0)

    def add_kid(e, carry):
        p = par_ref[e]
        kids_ref[p] = kids_ref[p] + e
        return carry

    lax.fori_loop(0, edge_count, add_kid, 0)
    outside_ref[leaf_count - 2] = root_out

    def arriving_of(c):
        p = par_ref[c]
        s = kids_ref[p] - c
        return outside_ref[p - leaf_count] * msg_ref[s]

    def count(c, arriving, row):
        den = jnp.sum(arriving * msg_ref[c], axis=0, keepdims=True)
        num = jnp.sum(arriving * num_ref[c], axis=0, keepdims=True)
        total = jnp.sum(w * num / den, axis=1, keepdims=True)
        return _lane_put(row, lane_offset + c, total)

    def outward(c, arriving):
        out = _dot(pt_ref[c], arriving)
        return out / jnp.max(out, axis=0, keepdims=True)

    def inner_step(i, row):
        c = edge_count - 1 - i
        arriving = arriving_of(c)
        outside_ref[c - leaf_count] = outward(c, arriving)
        return count(c, arriving, row)

    row = lax.fori_loop(0, edge_count - leaf_count, inner_step, row, unroll=unroll)

    def leaf_step(i, row):
        c = leaf_count - 1 - i
        return count(c, arriving_of(c), row)

    row = lax.fori_loop(0, leaf_count, leaf_step, row, unroll=unroll)
    leaf_out = None
    if want_leaf is not None:
        leaf_out = outward(want_leaf, arriving_of(want_leaf))
    return row, leaf_out


def _join_kernel(tpar_ref, tlen_ref, pick_ref, lpar_ref,
                 gat_ref, tp_ref, tpt_ref, tm_ref, rf_ref, w_ref,
                 lmsg_ref, lnum_ref, lpt_ref,
                 row_ref, loglik_ref,
                 tinner_ref, tmsg_ref, tnum_ref, toutside_ref, loutside_ref,
                 tkids_ref, lkids_ref, *, taxon_count):
    top_edges = tpar_ref.shape[0]
    leaf_count = gat_ref.shape[0]
    local_edges = lpar_ref.shape[0]
    states, columns = tmsg_ref.shape[1], tmsg_ref.shape[2]
    unroll = _unroll(top_edges)
    g = pick_ref[0]
    tinner_ref[...] = jnp.ones(tinner_ref.shape, F32)

    def push(c, x):
        msg = _dot(tp_ref[c], x)
        tmsg_ref[c] = msg
        tnum_ref[c] = _dot(tm_ref[c], x)
        p = tpar_ref[c] - leaf_count
        tinner_ref[p] = tinner_ref[p] * msg

    def leaf_step(c, logs):
        block = gat_ref[jnp.bitwise_xor(c, g)]
        push(c, block[0:states, :])
        return logs + block[states:states + 1, :]

    leaf_logs = lax.fori_loop(
        0, leaf_count, leaf_step, jnp.zeros((1, columns), F32), unroll=unroll
    )

    def inner_step(c, logs):
        x = tinner_ref[c - leaf_count]
        big = jnp.max(x, axis=0, keepdims=True)
        push(c, x / big)
        return logs + jnp.log(big)

    logs = lax.fori_loop(
        leaf_count, top_edges, inner_step, jnp.zeros((1, columns), F32), unroll=unroll
    )
    x = tinner_ref[leaf_count - 2]
    big = jnp.max(x, axis=0, keepdims=True)
    logs = logs + jnp.log(big)
    rf = rf_ref[...]
    likelihood = jnp.sum(rf * (x / big), axis=0, keepdims=True)
    loglik_ref[...] = (jnp.log(likelihood) + logs + leaf_logs) / taxon_count

    w = w_ref[...]
    row = jnp.zeros((1, row_ref.shape[1]), F32)
    row, subtree_out = _descend(
        tpar_ref, tkids_ref, toutside_ref, tmsg_ref, tnum_ref, tpt_ref, w,
        jnp.broadcast_to(rf, (states, columns)), local_edges, row, want_leaf=g,
    )
    row, _ = _descend(
        lpar_ref, lkids_ref, loutside_ref, lmsg_ref, lnum_ref, lpt_ref, w,
        subtree_out, 0, row,
    )
    row_ref[...] = _lane_put(row, local_edges + top_edges, jnp.sum(w, axis=1, keepdims=True))


def join(top_parents, top_lengths, pick, parents, gathered, tp, tpt, tm, rf_col, w_row,
         lmsgs, lnums, lpt, taxon_count):
    leaf_count, _, columns = gathered.shape
    top_edges = top_parents.shape[0]
    local_edges, states, _ = lmsgs.shape
    lanes = max(128, -(-(local_edges + top_edges + 1) // 128) * 128)
    return pl.pallas_call(
        functools.partial(_join_kernel, taxon_count=taxon_count),
        out_shape=(
            jax.ShapeDtypeStruct((1, lanes), F32),
            jax.ShapeDtypeStruct((1, columns), F32),
        ),
        in_specs=[SMEM] * 4 + [VMEM] * 9,
        out_specs=(VMEM, VMEM),
        scratch_shapes=[
            pltpu.VMEM((leaf_count - 1, states, columns), F32),
            pltpu.VMEM((top_edges, states, columns), F32),
            pltpu.VMEM((top_edges, states, columns), F32),
            pltpu.VMEM((leaf_count - 1, states, columns), F32),
            pltpu.VMEM(((local_edges + 2) // 2 - 1, states, columns), F32),
            pltpu.SMEM((top_edges + 1,), jnp.int32),
            pltpu.SMEM((local_edges + 1,), jnp.int32),
        ],
        compiler_params=_params(top_edges),
    )(top_parents, top_lengths, pick, parents, gathered, tp, tpt, tm, rf_col, w_row,
      lmsgs, lnums, lpt)


def gather_roots(block, groups):
    buf = block[None]
    step = groups // 2
    while step >= 1:
        other = lax.ppermute(buf, "leaf", [(i, i ^ step) for i in range(groups)])
        buf = jnp.stack([buf, other], axis=1).reshape((-1,) + block.shape)
        step //= 2
    return buf


def on_device(
    tips,
    parents,
    branch_lengths,
    top_parents,
    top_lengths,
    weights,
    eig_vectors,
    eig_inverse,
    eig_values,
    labeled_rates,
    root_freq,
):
    states = tips.shape[1]
    local_edges = parents.shape[0]
    groups = lax.axis_size("leaf")
    member_index = lax.axis_index("leaf")
    taxon_count = tips.shape[0] * groups
    lam_col = eig_values[:, None]
    lam_row = eig_values[None, :]

    root_block, msgs, xs = climb(parents, branch_lengths, tips, eig_vectors, eig_inverse, lam_col)
    if groups & (groups - 1) == 0:
        gathered = gather_roots(root_block, groups)
        pick = jnp.reshape(member_index, (1,)).astype(jnp.int32)
    else:
        gathered = lax.all_gather(root_block, "leaf", axis=0, tiled=False)
        pick = jnp.zeros((1,), jnp.int32)
    j_local = jax.vmap(lambda t: integrals(eig_values, t))(branch_lengths)
    j_top = jax.vmap(lambda t: integrals(eig_values, t))(top_lengths)
    nums, lpt, tp, tpt, tm = matrices(
        branch_lengths, top_lengths, eig_vectors, eig_inverse, labeled_rates, lam_col, lam_row,
        j_local, j_top, xs,
    )
    w_row = weights.astype(F32)[None, :]
    row, loglik = join(
        top_parents, top_lengths, pick, parents, gathered, tp, tpt, tm, root_freq[:, None],
        w_row, msgs, nums, lpt, taxon_count,
    )
    sums = lax.psum(row[0], "site")
    top_edges = top_parents.shape[0]
    weight_total = sums[local_edges + top_edges]
    return (
        sums[:local_edges] / weight_total,
        sums[local_edges:local_edges + top_edges] / weight_total,
        loglik[0],
    )


def solution(mesh):
    placed = (
        P("leaf", None, "site"),
        P("leaf"),
        P("leaf"),
        P(),
        P(),
        P("site"),
        P(),
        P(),
        P(),
        P(),
        P(),
    )
    return jax.shard_map(
        on_device,
        mesh=mesh,
        in_specs=placed,
        out_specs=(P("leaf"), P(), P("site")),
        check_vma=False,
    )
```

```python
import functools

import jax
import jax.numpy as jnp
from jax import lax
from jax.experimental import pallas as pl
from jax.experimental.pallas import tpu as pltpu
from jax.sharding import PartitionSpec as P

CODONS = 61

PRECISE = lax.Precision.HIGHEST
F32 = jnp.float32
VMEM_LIMIT = 56 * 1024 * 1024
VMEM = pl.BlockSpec(memory_space=pltpu.VMEM)
SMEM = pl.BlockSpec(memory_space=pltpu.SMEM)


def _dot(a, b):
    return jnp.dot(a, b, precision=PRECISE, preferred_element_type=F32)


def integrals(eig_values, branch):
    spread = (eig_values[:, None] - eig_values[None, :]) * branch
    near_zero = jnp.abs(spread) < 0.0001
    divisor = jnp.where(near_zero, jnp.ones_like(spread), spread)
    growth = jnp.where(
        near_zero, 1.0 + spread / 2.0 + spread * spread / 6.0, jnp.expm1(spread) / divisor
    )
    return branch * jnp.exp(eig_values[None, :] * branch) * growth


PARAMS = pltpu.CompilerParams(vmem_limit_bytes=VMEM_LIMIT)


def _cols(c, columns):
    return slice(c * columns, (c + 1) * columns)


def _climb_kernel(par_ref, len_ref, leaf_ref, v_ref, vi_ref, lam_ref,
                  root_ref, msg_ref, xw_ref, tr_ref, inner_ref):
    leaf_count = leaf_ref.shape[0]
    edge_count, states, columns = msg_ref.shape
    vecs = v_ref[...]
    inv = vi_ref[...]
    lam = lam_ref[...]
    inner_ref[...] = jnp.ones(inner_ref.shape, F32)
    keep = (lax.broadcasted_iota(jnp.int32, (states, columns), 0) < CODONS).astype(F32)
    logs = jnp.zeros((1, columns), F32)
    for c in range(edge_count):
        if c < leaf_count:
            x = leaf_ref[c] * keep
        else:
            x = inner_ref[c - leaf_count]
            big = jnp.max(x, axis=0, keepdims=True)
            x = x / big
            logs = logs + jnp.log(big)
        trans = _dot(vecs, jnp.exp(lam * len_ref[c]) * inv)
        tr_ref[c] = trans
        msg = _dot(trans, x)
        msg_ref[c] = msg
        xw_ref[:, _cols(c, columns)] = x
        p = par_ref[c] - leaf_count
        inner_ref[p] = inner_ref[p] * msg
    x = inner_ref[leaf_count - 2]
    big = jnp.max(x, axis=0, keepdims=True)
    root_ref[0:states, :] = x / big
    root_ref[states:states + 1, :] = logs + jnp.log(big)


def climb(parents, lengths, tips, vecs, inv, lam_col):
    leaf_count, states, columns = tips.shape
    edge_count = parents.shape[0]
    return pl.pallas_call(
        _climb_kernel,
        out_shape=(
            jax.ShapeDtypeStruct((states + 1, columns), F32),
            jax.ShapeDtypeStruct((edge_count, states, columns), F32),
            jax.ShapeDtypeStruct((states, edge_count * columns), F32),
            jax.ShapeDtypeStruct((edge_count, states, states), F32),
        ),
        in_specs=[SMEM, SMEM, VMEM, VMEM, VMEM, VMEM],
        out_specs=(VMEM,) * 4,
        scratch_shapes=[pltpu.VMEM((leaf_count - 1, states, columns), F32)],
        compiler_params=PARAMS,
    )(parents, lengths, tips, vecs, inv, lam_col)


def _matrix_kernel(top_len_ref, v_ref, vi_ref, lab_ref, lam_ref, jl_ref, xw_ref, trl_ref,
                   mixed_ref, ptl_ref, tp_ref, tpt_ref, basis_ref, vw_ref):
    local_edges, states, columns = mixed_ref.shape
    top_edges = tp_ref.shape[0]
    vecs = v_ref[...]
    inv = vi_ref[...]
    lam = lam_ref[...]
    basis = _dot(_dot(inv, lab_ref[...]), vecs)
    basis_ref[...] = basis
    vw_ref[...] = _dot(inv, xw_ref[...])
    for c in range(local_edges):
        mixed_ref[c] = _dot(basis * jl_ref[c], vw_ref[:, _cols(c, columns)])
        ptl_ref[c] = trl_ref[c].T
    for c in range(top_edges):
        trans = _dot(vecs, jnp.exp(lam * top_len_ref[c]) * inv)
        tp_ref[c] = trans
        tpt_ref[c] = trans.T


def matrices(top_lengths, vecs, inv, labeled, lam_col, j_local, xw, trl):
    local_edges, states, _ = trl.shape
    columns = xw.shape[1] // local_edges
    top_edges = top_lengths.shape[0]
    sq = (states, states)
    return pl.pallas_call(
        _matrix_kernel,
        out_shape=(
            jax.ShapeDtypeStruct((local_edges, states, columns), F32),
            jax.ShapeDtypeStruct((local_edges,) + sq, F32),
            jax.ShapeDtypeStruct((top_edges,) + sq, F32),
            jax.ShapeDtypeStruct((top_edges,) + sq, F32),
            jax.ShapeDtypeStruct(sq, F32),
        ),
        in_specs=[SMEM] + [VMEM] * 7,
        out_specs=(VMEM,) * 5,
        scratch_shapes=[pltpu.VMEM((states, local_edges * columns), F32)],
        compiler_params=PARAMS,
    )(top_lengths, vecs, inv, labeled, lam_col, j_local, xw, trl)


def _lane_put(row, lane, value):
    lanes = lax.broadcasted_iota(jnp.int32, row.shape, 1)
    return jnp.where(lanes == lane, value, row)


def _descend(par_ref, kids_ref, outside_ref, arr_ref, msg_ref, pt_ref, root_out, pick=None):
    edge_count = par_ref.shape[0]
    leaf_count = (edge_count + 2) // 2
    columns = msg_ref.shape[2]
    for n in range(edge_count + 1):
        kids_ref[n] = 0
    for e in range(edge_count):
        p = par_ref[e]
        kids_ref[p] = kids_ref[p] + e
    outside_ref[leaf_count - 2] = root_out

    def arriving_of(c):
        p = par_ref[c]
        s = kids_ref[p] - c
        return outside_ref[p - leaf_count] * msg_ref[s]

    def outward(c, arriving):
        out = _dot(pt_ref[c], arriving)
        return out / jnp.max(out, axis=0, keepdims=True)

    for c in range(edge_count - 1, -1, -1):
        arriving = arriving_of(c)
        arr_ref[:, _cols(c, columns)] = arriving
        if c >= leaf_count:
            outside_ref[c - leaf_count] = outward(c, arriving)
    if pick is not None:
        return outward(pick, arriving_of(pick))
    return None


def _counts(row, lane_offset, w, vt, arr_ref, msg_ref, mixed_of):
    edge_count, _, columns = msg_ref.shape
    weighted = _dot(vt, arr_ref[...])
    for c in range(edge_count):
        cols = _cols(c, columns)
        num = jnp.sum(weighted[:, cols] * mixed_of(c), axis=0, keepdims=True)
        den = jnp.sum(arr_ref[:, cols] * msg_ref[c], axis=0, keepdims=True)
        total = jnp.sum(w * num / den, axis=1, keepdims=True)
        row = _lane_put(row, lane_offset + c, total)
    return row


def _join_kernel(tpar_ref, pick_ref, lpar_ref,
                 gat_ref, tp_ref, tpt_ref, basis_ref, jt_ref, v_ref, vi_ref, rf_ref, w_ref,
                 lmsg_ref, lmixed_ref, lpt_ref,
                 row_ref, loglik_ref,
                 tinner_ref, tmsg_ref, txw_ref, tvw_ref, toutside_ref, tarr_ref,
                 loutside_ref, larr_ref, tkids_ref, lkids_ref, *, taxon_count):
    top_edges = tpar_ref.shape[0]
    leaf_count = gat_ref.shape[0]
    local_edges = lpar_ref.shape[0]
    states, columns = tmsg_ref.shape[1], tmsg_ref.shape[2]
    g = pick_ref[0]
    tinner_ref[...] = jnp.ones(tinner_ref.shape, F32)
    logs = jnp.zeros((1, columns), F32)
    leaf_logs = jnp.zeros((1, columns), F32)
    for c in range(top_edges):
        if c < leaf_count:
            block = gat_ref[jnp.bitwise_xor(c, g)]
            x = block[0:states, :]
            leaf_logs = leaf_logs + block[states:states + 1, :]
        else:
            x = tinner_ref[c - leaf_count]
            big = jnp.max(x, axis=0, keepdims=True)
            x = x / big
            logs = logs + jnp.log(big)
        msg = _dot(tp_ref[c], x)
        tmsg_ref[c] = msg
        txw_ref[:, _cols(c, columns)] = x
        p = tpar_ref[c] - leaf_count
        tinner_ref[p] = tinner_ref[p] * msg
    x = tinner_ref[leaf_count - 2]
    big = jnp.max(x, axis=0, keepdims=True)
    logs = logs + jnp.log(big)
    rf = rf_ref[...]
    likelihood = jnp.sum(rf * (x / big), axis=0, keepdims=True)
    loglik_ref[...] = (jnp.log(likelihood) + logs + leaf_logs) / taxon_count

    inv = vi_ref[...]
    vt = v_ref[...].T
    basis = basis_ref[...]
    tvw_ref[...] = _dot(inv, txw_ref[...])
    subtree_out = _descend(
        tpar_ref, tkids_ref, toutside_ref, tarr_ref, tmsg_ref, tpt_ref,
        jnp.broadcast_to(rf, (states, columns)), pick=g,
    )
    _descend(lpar_ref, lkids_ref, loutside_ref, larr_ref, lmsg_ref, lpt_ref, subtree_out)
    w = w_ref[...]
    row = jnp.zeros((1, row_ref.shape[1]), F32)
    row = _counts(
        row, local_edges, w, vt, tarr_ref, tmsg_ref,
        lambda c: _dot(basis * jt_ref[c], tvw_ref[:, _cols(c, columns)]),
    )
    row = _counts(row, 0, w, vt, larr_ref, lmsg_ref, lambda c: lmixed_ref[c])
    row_ref[...] = _lane_put(row, local_edges + top_edges, jnp.sum(w, axis=1, keepdims=True))


def join(top_parents, pick, parents, gathered, tp, tpt, basis, j_top, vecs, inv, rf_col, w_row,
         lmsgs, lmixed, lpt, taxon_count):
    leaf_count, _, columns = gathered.shape
    top_edges = top_parents.shape[0]
    local_edges, states, _ = lmsgs.shape
    local_leaves = (local_edges + 2) // 2
    lanes = max(128, -(-(local_edges + top_edges + 1) // 128) * 128)
    return pl.pallas_call(
        functools.partial(_join_kernel, taxon_count=taxon_count),
        out_shape=(
            jax.ShapeDtypeStruct((1, lanes), F32),
            jax.ShapeDtypeStruct((1, columns), F32),
        ),
        in_specs=[SMEM] * 3 + [VMEM] * 12,
        out_specs=(VMEM, VMEM),
        scratch_shapes=[
            pltpu.VMEM((leaf_count - 1, states, columns), F32),
            pltpu.VMEM((top_edges, states, columns), F32),
            pltpu.VMEM((states, top_edges * columns), F32),
            pltpu.VMEM((states, top_edges * columns), F32),
            pltpu.VMEM((leaf_count - 1, states, columns), F32),
            pltpu.VMEM((states, top_edges * columns), F32),
            pltpu.VMEM((local_leaves - 1, states, columns), F32),
            pltpu.VMEM((states, local_edges * columns), F32),
            pltpu.SMEM((top_edges + 1,), jnp.int32),
            pltpu.SMEM((local_edges + 1,), jnp.int32),
        ],
        compiler_params=PARAMS,
    )(top_parents, pick, parents, gathered, tp, tpt, basis, j_top, vecs, inv, rf_col, w_row,
      lmsgs, lmixed, lpt)


def gather_roots(block, groups):
    buf = block[None]
    step = groups // 2
    while step >= 1:
        other = lax.ppermute(buf, "leaf", [(i, i ^ step) for i in range(groups)])
        buf = jnp.stack([buf, other], axis=1).reshape((-1,) + block.shape)
        step //= 2
    return buf


def on_device(
    tips,
    parents,
    branch_lengths,
    top_parents,
    top_lengths,
    weights,
    eig_vectors,
    eig_inverse,
    eig_values,
    labeled_rates,
    root_freq,
):
    local_edges = parents.shape[0]
    top_edges = top_parents.shape[0]
    groups = lax.axis_size("leaf")
    member_index = lax.axis_index("leaf")
    taxon_count = tips.shape[0] * groups
    lam_col = eig_values[:, None]

    root_block, msgs, xw, trl = climb(
        parents, branch_lengths, tips, eig_vectors, eig_inverse, lam_col
    )
    if groups & (groups - 1) == 0:
        gathered = gather_roots(root_block, groups)
        pick = jnp.reshape(member_index, (1,)).astype(jnp.int32)
    else:
        gathered = lax.all_gather(root_block, "leaf", axis=0, tiled=False)
        pick = jnp.zeros((1,), jnp.int32)
    j_local = jax.vmap(lambda t: integrals(eig_values, t))(branch_lengths)
    j_top = jax.vmap(lambda t: integrals(eig_values, t))(top_lengths)
    lmixed, lpt, tp, tpt, basis = matrices(
        top_lengths, eig_vectors, eig_inverse, labeled_rates, lam_col, j_local, xw, trl
    )
    w_row = weights.astype(F32)[None, :]
    row, loglik = join(
        top_parents, pick, parents, gathered, tp, tpt, basis, j_top, eig_vectors, eig_inverse,
        root_freq[:, None], w_row, msgs, lmixed, lpt, taxon_count,
    )
    sums = lax.psum(row[0], "site")
    weight_total = sums[local_edges + top_edges]
    return (
        sums[:local_edges] / weight_total,
        sums[local_edges:local_edges + top_edges] / weight_total,
        loglik[0],
    )


def solution(mesh):
    placed = (
        P("leaf", None, "site"),
        P("leaf"),
        P("leaf"),
        P(),
        P(),
        P("site"),
        P(),
        P(),
        P(),
        P(),
        P(),
    )
    return jax.shard_map(
        on_device,
        mesh=mesh,
        in_specs=placed,
        out_specs=(P("leaf"), P(), P("site")),
        check_vma=False,
    )
```

```python
import functools

import jax
import jax.numpy as jnp
from jax import lax
from jax.experimental import pallas as pl
from jax.experimental.pallas import tpu as pltpu
from jax.sharding import PartitionSpec as P

CODONS = 61

PRECISE = lax.Precision.HIGHEST
FAST = lax.Precision.HIGH
F32 = jnp.float32
VMEM_LIMIT = 56 * 1024 * 1024
VMEM = pl.BlockSpec(memory_space=pltpu.VMEM)
SMEM = pl.BlockSpec(memory_space=pltpu.SMEM)


def _dot(a, b):
    return jnp.dot(a, b, precision=FAST, preferred_element_type=F32)


def integrals(eig_values, branch):
    spread = (eig_values[:, None] - eig_values[None, :]) * branch
    near_zero = jnp.abs(spread) < 0.0001
    divisor = jnp.where(near_zero, jnp.ones_like(spread), spread)
    growth = jnp.where(
        near_zero, 1.0 + spread / 2.0 + spread * spread / 6.0, jnp.expm1(spread) / divisor
    )
    return branch * jnp.exp(eig_values[None, :] * branch) * growth


PARAMS = pltpu.CompilerParams(vmem_limit_bytes=VMEM_LIMIT)


def _cols(c, columns):
    return slice(c * columns, (c + 1) * columns)


def _climb_kernel(par_ref, len_ref, leaf_ref, v_ref, vi_ref, lam_ref,
                  root_ref, msg_ref, xw_ref, tr_ref, inner_ref):
    leaf_count = leaf_ref.shape[0]
    edge_count, states, columns = msg_ref.shape
    vecs = v_ref[...]
    inv = vi_ref[...]
    lam = lam_ref[...]
    inner_ref[...] = jnp.ones(inner_ref.shape, F32)
    keep = (lax.broadcasted_iota(jnp.int32, (states, columns), 0) < CODONS).astype(F32)
    logs = jnp.zeros((1, columns), F32)
    for c in range(edge_count):
        if c < leaf_count:
            x = leaf_ref[c] * keep
        else:
            x = inner_ref[c - leaf_count]
            big = jnp.max(x, axis=0, keepdims=True)
            x = x / big
            logs = logs + jnp.log(big)
        trans = _dot(vecs, jnp.exp(lam * len_ref[c]) * inv)
        tr_ref[c] = trans
        msg = _dot(trans, x)
        msg_ref[c] = msg
        xw_ref[:, _cols(c, columns)] = x
        p = par_ref[c] - leaf_count
        inner_ref[p] = inner_ref[p] * msg
    x = inner_ref[leaf_count - 2]
    big = jnp.max(x, axis=0, keepdims=True)
    root_ref[0:states, :] = x / big
    root_ref[states:states + 1, :] = logs + jnp.log(big)


def climb(parents, lengths, tips, vecs, inv, lam_col):
    leaf_count, states, columns = tips.shape
    edge_count = parents.shape[0]
    return pl.pallas_call(
        _climb_kernel,
        out_shape=(
            jax.ShapeDtypeStruct((states + 1, columns), F32),
            jax.ShapeDtypeStruct((edge_count, states, columns), F32),
            jax.ShapeDtypeStruct((states, edge_count * columns), F32),
            jax.ShapeDtypeStruct((edge_count, states, states), F32),
        ),
        in_specs=[SMEM, SMEM, VMEM, VMEM, VMEM, VMEM],
        out_specs=(VMEM,) * 4,
        scratch_shapes=[pltpu.VMEM((leaf_count - 1, states, columns), F32)],
        compiler_params=PARAMS,
    )(parents, lengths, tips, vecs, inv, lam_col)


def _matrix_kernel(top_len_ref, v_ref, vi_ref, lab_ref, lam_ref, jl_ref, xw_ref, trl_ref,
                   mixed_ref, ptl_ref, tp_ref, tpt_ref, basis_ref, vw_ref):
    local_edges, states, columns = mixed_ref.shape
    top_edges = tp_ref.shape[0]
    vecs = v_ref[...]
    inv = vi_ref[...]
    lam = lam_ref[...]
    basis = _dot(_dot(inv, lab_ref[...]), vecs)
    basis_ref[...] = basis
    vw_ref[...] = _dot(inv, xw_ref[...])
    for c in range(local_edges):
        mixed_ref[c] = _dot(basis * jl_ref[c], vw_ref[:, _cols(c, columns)])
        ptl_ref[c] = trl_ref[c].T
    for c in range(top_edges):
        trans = _dot(vecs, jnp.exp(lam * top_len_ref[c]) * inv)
        tp_ref[c] = trans
        tpt_ref[c] = trans.T


def matrices(top_lengths, vecs, inv, labeled, lam_col, j_local, xw, trl):
    local_edges, states, _ = trl.shape
    columns = xw.shape[1] // local_edges
    top_edges = top_lengths.shape[0]
    sq = (states, states)
    return pl.pallas_call(
        _matrix_kernel,
        out_shape=(
            jax.ShapeDtypeStruct((local_edges, states, columns), F32),
            jax.ShapeDtypeStruct((local_edges,) + sq, F32),
            jax.ShapeDtypeStruct((top_edges,) + sq, F32),
            jax.ShapeDtypeStruct((top_edges,) + sq, F32),
            jax.ShapeDtypeStruct(sq, F32),
        ),
        in_specs=[SMEM] + [VMEM] * 7,
        out_specs=(VMEM,) * 5,
        scratch_shapes=[pltpu.VMEM((states, local_edges * columns), F32)],
        compiler_params=PARAMS,
    )(top_lengths, vecs, inv, labeled, lam_col, j_local, xw, trl)


def _lane_put(row, lane, value):
    lanes = lax.broadcasted_iota(jnp.int32, row.shape, 1)
    return jnp.where(lanes == lane, value, row)


def _descend(par_ref, kids_ref, outside_ref, arr_ref, msg_ref, pt_ref, root_out, pick=None):
    edge_count = par_ref.shape[0]
    leaf_count = (edge_count + 2) // 2
    columns = msg_ref.shape[2]
    for n in range(edge_count + 1):
        kids_ref[n] = 0
    for e in range(edge_count):
        p = par_ref[e]
        kids_ref[p] = kids_ref[p] + e
    outside_ref[leaf_count - 2] = root_out

    def arriving_of(c):
        p = par_ref[c]
        s = kids_ref[p] - c
        return outside_ref[p - leaf_count] * msg_ref[s]

    def outward(c, arriving):
        out = _dot(pt_ref[c], arriving)
        return out / jnp.max(out, axis=0, keepdims=True)

    for c in range(edge_count - 1, -1, -1):
        arriving = arriving_of(c)
        arr_ref[:, _cols(c, columns)] = arriving
        if c >= leaf_count:
            outside_ref[c - leaf_count] = outward(c, arriving)
    if pick is not None:
        return outward(pick, arriving_of(pick))
    return None


def _counts(row, lane_offset, w, vt, arr_ref, msg_ref, mixed_of):
    edge_count, _, columns = msg_ref.shape
    weighted = _dot(vt, arr_ref[...])
    for c in range(edge_count):
        cols = _cols(c, columns)
        num = jnp.sum(weighted[:, cols] * mixed_of(c), axis=0, keepdims=True)
        den = jnp.sum(arr_ref[:, cols] * msg_ref[c], axis=0, keepdims=True)
        total = jnp.sum(w * num / den, axis=1, keepdims=True)
        row = _lane_put(row, lane_offset + c, total)
    return row


def _join_kernel(tpar_ref, pick_ref, lpar_ref,
                 gat_ref, tp_ref, tpt_ref, basis_ref, jt_ref, v_ref, vi_ref, rf_ref, w_ref,
                 lmsg_ref, lmixed_ref, lpt_ref,
                 row_ref, loglik_ref,
                 tinner_ref, tmsg_ref, txw_ref, tvw_ref, toutside_ref, tarr_ref,
                 loutside_ref, larr_ref, tkids_ref, lkids_ref, *, taxon_count):
    top_edges = tpar_ref.shape[0]
    leaf_count = gat_ref.shape[0]
    local_edges = lpar_ref.shape[0]
    states, columns = tmsg_ref.shape[1], tmsg_ref.shape[2]
    g = pick_ref[0]
    tinner_ref[...] = jnp.ones(tinner_ref.shape, F32)
    logs = jnp.zeros((1, columns), F32)
    leaf_logs = jnp.zeros((1, columns), F32)
    for c in range(top_edges):
        if c < leaf_count:
            block = gat_ref[jnp.bitwise_xor(c, g)]
            x = block[0:states, :]
            leaf_logs = leaf_logs + block[states:states + 1, :]
        else:
            x = tinner_ref[c - leaf_count]
            big = jnp.max(x, axis=0, keepdims=True)
            x = x / big
            logs = logs + jnp.log(big)
        msg = _dot(tp_ref[c], x)
        tmsg_ref[c] = msg
        txw_ref[:, _cols(c, columns)] = x
        p = tpar_ref[c] - leaf_count
        tinner_ref[p] = tinner_ref[p] * msg
    x = tinner_ref[leaf_count - 2]
    big = jnp.max(x, axis=0, keepdims=True)
    logs = logs + jnp.log(big)
    rf = rf_ref[...]
    likelihood = jnp.sum(rf * (x / big), axis=0, keepdims=True)
    loglik_ref[...] = (jnp.log(likelihood) + logs + leaf_logs) / taxon_count

    inv = vi_ref[...]
    vt = v_ref[...].T
    basis = basis_ref[...]
    tvw_ref[...] = _dot(inv, txw_ref[...])
    subtree_out = _descend(
        tpar_ref, tkids_ref, toutside_ref, tarr_ref, tmsg_ref, tpt_ref,
        jnp.broadcast_to(rf, (states, columns)), pick=g,
    )
    _descend(lpar_ref, lkids_ref, loutside_ref, larr_ref, lmsg_ref, lpt_ref, subtree_out)
    w = w_ref[...]
    row = jnp.zeros((1, row_ref.shape[1]), F32)
    row = _counts(
        row, local_edges, w, vt, tarr_ref, tmsg_ref,
        lambda c: _dot(basis * jt_ref[c], tvw_ref[:, _cols(c, columns)]),
    )
    row = _counts(row, 0, w, vt, larr_ref, lmsg_ref, lambda c: lmixed_ref[c])
    row_ref[...] = _lane_put(row, local_edges + top_edges, jnp.sum(w, axis=1, keepdims=True))


def join(top_parents, pick, parents, gathered, tp, tpt, basis, j_top, vecs, inv, rf_col, w_row,
         lmsgs, lmixed, lpt, taxon_count):
    leaf_count, _, columns = gathered.shape
    top_edges = top_parents.shape[0]
    local_edges, states, _ = lmsgs.shape
    local_leaves = (local_edges + 2) // 2
    lanes = max(128, -(-(local_edges + top_edges + 1) // 128) * 128)
    return pl.pallas_call(
        functools.partial(_join_kernel, taxon_count=taxon_count),
        out_shape=(
            jax.ShapeDtypeStruct((1, lanes), F32),
            jax.ShapeDtypeStruct((1, columns), F32),
        ),
        in_specs=[SMEM] * 3 + [VMEM] * 12,
        out_specs=(VMEM, VMEM),
        scratch_shapes=[
            pltpu.VMEM((leaf_count - 1, states, columns), F32),
            pltpu.VMEM((top_edges, states, columns), F32),
            pltpu.VMEM((states, top_edges * columns), F32),
            pltpu.VMEM((states, top_edges * columns), F32),
            pltpu.VMEM((leaf_count - 1, states, columns), F32),
            pltpu.VMEM((states, top_edges * columns), F32),
            pltpu.VMEM((local_leaves - 1, states, columns), F32),
            pltpu.VMEM((states, local_edges * columns), F32),
            pltpu.SMEM((top_edges + 1,), jnp.int32),
            pltpu.SMEM((local_edges + 1,), jnp.int32),
        ],
        compiler_params=PARAMS,
    )(top_parents, pick, parents, gathered, tp, tpt, basis, j_top, vecs, inv, rf_col, w_row,
      lmsgs, lmixed, lpt)


def gather_roots(block, groups):
    buf = block[None]
    step = groups // 2
    while step >= 1:
        other = lax.ppermute(buf, "leaf", [(i, i ^ step) for i in range(groups)])
        buf = jnp.stack([buf, other], axis=1).reshape((-1,) + block.shape)
        step //= 2
    return buf


def on_device(
    tips,
    parents,
    branch_lengths,
    top_parents,
    top_lengths,
    weights,
    eig_vectors,
    eig_inverse,
    eig_values,
    labeled_rates,
    root_freq,
):
    local_edges = parents.shape[0]
    top_edges = top_parents.shape[0]
    groups = lax.axis_size("leaf")
    member_index = lax.axis_index("leaf")
    taxon_count = tips.shape[0] * groups
    lam_col = eig_values[:, None]

    root_block, msgs, xw, trl = climb(
        parents, branch_lengths, tips, eig_vectors, eig_inverse, lam_col
    )
    if groups & (groups - 1) == 0:
        gathered = gather_roots(root_block, groups)
        pick = jnp.reshape(member_index, (1,)).astype(jnp.int32)
    else:
        gathered = lax.all_gather(root_block, "leaf", axis=0, tiled=False)
        pick = jnp.zeros((1,), jnp.int32)
    j_local = jax.vmap(lambda t: integrals(eig_values, t))(branch_lengths)
    j_top = jax.vmap(lambda t: integrals(eig_values, t))(top_lengths)
    lmixed, lpt, tp, tpt, basis = matrices(
        top_lengths, eig_vectors, eig_inverse, labeled_rates, lam_col, j_local, xw, trl
    )
    w_row = weights.astype(F32)[None, :]
    row, loglik = join(
        top_parents, pick, parents, gathered, tp, tpt, basis, j_top, eig_vectors, eig_inverse,
        root_freq[:, None], w_row, msgs, lmixed, lpt, taxon_count,
    )
    sums = lax.psum(row[0], "site")
    weight_total = sums[local_edges + top_edges]
    return (
        sums[:local_edges] / weight_total,
        sums[local_edges:local_edges + top_edges] / weight_total,
        loglik[0],
    )


def solution(mesh):
    placed = (
        P("leaf", None, "site"),
        P("leaf"),
        P("leaf"),
        P(),
        P(),
        P("site"),
        P(),
        P(),
        P(),
        P(),
        P(),
    )
    return jax.shard_map(
        on_device,
        mesh=mesh,
        in_specs=placed,
        out_specs=(P("leaf"), P(), P("site")),
        check_vma=False,
    )
```

```python
import functools

import jax
import jax.numpy as jnp
from jax import lax
from jax.experimental import pallas as pl
from jax.experimental.pallas import tpu as pltpu
from jax.sharding import PartitionSpec as P

CODONS = 61

PRECISE = lax.Precision.HIGHEST
FAST = lax.Precision.HIGH
F32 = jnp.float32
VMEM_LIMIT = 56 * 1024 * 1024
VMEM = pl.BlockSpec(memory_space=pltpu.VMEM)
SMEM = pl.BlockSpec(memory_space=pltpu.SMEM)


def _dot(a, b):
    return jnp.dot(a, b, precision=FAST, preferred_element_type=F32)


def integrals(eig_values, branch):
    spread = (eig_values[:, None] - eig_values[None, :]) * branch
    near_zero = jnp.abs(spread) < 0.0001
    divisor = jnp.where(near_zero, jnp.ones_like(spread), spread)
    growth = jnp.where(
        near_zero, 1.0 + spread / 2.0 + spread * spread / 6.0, jnp.expm1(spread) / divisor
    )
    return branch * jnp.exp(eig_values[None, :] * branch) * growth


PARAMS = pltpu.CompilerParams(vmem_limit_bytes=VMEM_LIMIT)


def _cols(c, columns):
    return slice(c * columns, (c + 1) * columns)


def _climb_kernel(par_ref, len_ref, leaf_ref, v_ref, vi_ref, lam_ref,
                  root_ref, msg_ref, xw_ref, tr_ref, inner_ref):
    leaf_count = leaf_ref.shape[0]
    edge_count, states, columns = msg_ref.shape
    vecs = v_ref[...]
    inv = vi_ref[...]
    lam = lam_ref[...]
    inner_ref[...] = jnp.ones(inner_ref.shape, F32)
    keep = (lax.broadcasted_iota(jnp.int32, (states, columns), 0) < CODONS).astype(F32)
    logs = jnp.zeros((1, columns), F32)
    for c in range(edge_count):
        if c < leaf_count:
            x = leaf_ref[c] * keep
        else:
            x = inner_ref[c - leaf_count]
            big = jnp.max(x, axis=0, keepdims=True)
            x = x / big
            logs = logs + jnp.log(big)
        trans = _dot(vecs * jnp.exp(lam * len_ref[c]), inv)
        tr_ref[c] = trans
        msg = _dot(trans, x)
        msg_ref[c] = msg
        xw_ref[:, _cols(c, columns)] = x
        p = par_ref[c] - leaf_count
        inner_ref[p] = inner_ref[p] * msg
    x = inner_ref[leaf_count - 2]
    big = jnp.max(x, axis=0, keepdims=True)
    root_ref[0:states, :] = x / big
    root_ref[states:states + 1, :] = logs + jnp.log(big)


def climb(parents, lengths, tips, vecs, inv, lam_row):
    leaf_count, states, columns = tips.shape
    edge_count = parents.shape[0]
    return pl.pallas_call(
        _climb_kernel,
        out_shape=(
            jax.ShapeDtypeStruct((states + 1, columns), F32),
            jax.ShapeDtypeStruct((edge_count, states, columns), F32),
            jax.ShapeDtypeStruct((states, edge_count * columns), F32),
            jax.ShapeDtypeStruct((edge_count, states, states), F32),
        ),
        in_specs=[SMEM, SMEM, VMEM, VMEM, VMEM, VMEM],
        out_specs=(VMEM,) * 4,
        scratch_shapes=[pltpu.VMEM((leaf_count - 1, states, columns), F32)],
        compiler_params=PARAMS,
    )(parents, lengths, tips, vecs, inv, lam_row)


def _matrix_kernel(top_len_ref, v_ref, vi_ref, lab_ref, lam_ref, jl_ref, xw_ref, trl_ref,
                   mixed_ref, ptl_ref, tp_ref, tpt_ref, basis_ref, vw_ref):
    local_edges, states, columns = mixed_ref.shape
    top_edges = tp_ref.shape[0]
    vecs = v_ref[...]
    inv = vi_ref[...]
    lam = lam_ref[...]
    basis = _dot(_dot(inv, lab_ref[...]), vecs)
    basis_ref[...] = basis
    vw_ref[...] = _dot(inv, xw_ref[...])
    for c in range(local_edges):
        mixed_ref[c] = _dot(basis * jl_ref[c], vw_ref[:, _cols(c, columns)])
        ptl_ref[c] = trl_ref[c].T
    for c in range(top_edges):
        trans = _dot(vecs * jnp.exp(lam * top_len_ref[c]), inv)
        tp_ref[c] = trans
        tpt_ref[c] = trans.T


def matrices(top_lengths, vecs, inv, labeled, lam_row, j_local, xw, trl):
    local_edges, states, _ = trl.shape
    columns = xw.shape[1] // local_edges
    top_edges = top_lengths.shape[0]
    sq = (states, states)
    return pl.pallas_call(
        _matrix_kernel,
        out_shape=(
            jax.ShapeDtypeStruct((local_edges, states, columns), F32),
            jax.ShapeDtypeStruct((local_edges,) + sq, F32),
            jax.ShapeDtypeStruct((top_edges,) + sq, F32),
            jax.ShapeDtypeStruct((top_edges,) + sq, F32),
            jax.ShapeDtypeStruct(sq, F32),
        ),
        in_specs=[SMEM] + [VMEM] * 7,
        out_specs=(VMEM,) * 5,
        scratch_shapes=[pltpu.VMEM((states, local_edges * columns), F32)],
        compiler_params=PARAMS,
    )(top_lengths, vecs, inv, labeled, lam_row, j_local, xw, trl)


def _lane_put(row, lane, value):
    lanes = lax.broadcasted_iota(jnp.int32, row.shape, 1)
    return jnp.where(lanes == lane, value, row)


def _descend(par_ref, kids_ref, outside_ref, arr_ref, msg_ref, pt_ref, root_out, pick=None):
    edge_count = par_ref.shape[0]
    leaf_count = (edge_count + 2) // 2
    columns = msg_ref.shape[2]
    for n in range(edge_count + 1):
        kids_ref[n] = 0
    for e in range(edge_count):
        p = par_ref[e]
        kids_ref[p] = kids_ref[p] + e
    outside_ref[leaf_count - 2] = root_out

    def arriving_of(c):
        p = par_ref[c]
        s = kids_ref[p] - c
        return outside_ref[p - leaf_count] * msg_ref[s]

    def outward(c, arriving):
        out = _dot(pt_ref[c], arriving)
        return out / jnp.max(out, axis=0, keepdims=True)

    for c in range(edge_count - 1, -1, -1):
        arriving = arriving_of(c)
        arr_ref[:, _cols(c, columns)] = arriving
        if c >= leaf_count:
            outside_ref[c - leaf_count] = outward(c, arriving)
    if pick is not None:
        return outward(pick, arriving_of(pick))
    return None


def _counts(row, lane_offset, w, vt, arr_ref, msg_ref, mixed_of):
    edge_count, _, columns = msg_ref.shape
    weighted = _dot(vt, arr_ref[...])
    for c in range(edge_count):
        cols = _cols(c, columns)
        num = jnp.sum(weighted[:, cols] * mixed_of(c), axis=0, keepdims=True)
        den = jnp.sum(arr_ref[:, cols] * msg_ref[c], axis=0, keepdims=True)
        total = jnp.sum(w * num / den, axis=1, keepdims=True)
        row = _lane_put(row, lane_offset + c, total)
    return row


def _join_kernel(tpar_ref, pick_ref, lpar_ref,
                 gat0_ref, gat1_ref, tp_ref, tpt_ref, basis_ref, jt_ref, v_ref, vi_ref, rf_ref,
                 w_ref, wo_ref, lmsg_ref, lmixed_ref, lpt_ref,
                 local_ref, top_ref, loglik_ref,
                 tinner_ref, tmsg_ref, txw_ref, tvw_ref, toutside_ref, tarr_ref,
                 loutside_ref, larr_ref, tkids_ref, lkids_ref, *, taxon_count, paired):
    top_edges = tpar_ref.shape[0]
    leaf_count = (top_edges + 2) // 2
    local_edges = lpar_ref.shape[0]
    states, columns = tmsg_ref.shape[1], tmsg_ref.shape[2]
    g = pick_ref[0]
    tinner_ref[...] = jnp.ones(tinner_ref.shape, F32)
    logs = jnp.zeros((1, columns), F32)
    leaf_logs = jnp.zeros((1, columns), F32)
    for c in range(top_edges):
        if c < leaf_count:
            if paired:
                spot = jnp.bitwise_xor(c, g)
                half = spot // 2
                block = jnp.where(spot % 2 == 0, gat0_ref[half], gat1_ref[half])
            else:
                block = gat0_ref[c]
            x = block[0:states, :]
            leaf_logs = leaf_logs + block[states:states + 1, :]
        else:
            x = tinner_ref[c - leaf_count]
            big = jnp.max(x, axis=0, keepdims=True)
            x = x / big
            logs = logs + jnp.log(big)
        msg = _dot(tp_ref[c], x)
        tmsg_ref[c] = msg
        txw_ref[:, _cols(c, columns)] = x
        p = tpar_ref[c] - leaf_count
        tinner_ref[p] = tinner_ref[p] * msg
    x = tinner_ref[leaf_count - 2]
    big = jnp.max(x, axis=0, keepdims=True)
    logs = logs + jnp.log(big)
    rf = rf_ref[...]
    likelihood = jnp.dot(rf, x / big, precision=PRECISE, preferred_element_type=F32)
    loglik_ref[...] = (jnp.log(likelihood) + logs + leaf_logs) / taxon_count

    eye = (lax.broadcasted_iota(jnp.int32, (states, states), 0)
           == lax.broadcasted_iota(jnp.int32, (states, states), 1))
    rf_col = jnp.sum(jnp.where(eye, rf, 0.0), axis=1, keepdims=True)
    inv = vi_ref[...]
    vt = v_ref[...].T
    basis = basis_ref[...]
    tvw_ref[...] = _dot(inv, txw_ref[...])
    subtree_out = _descend(
        tpar_ref, tkids_ref, toutside_ref, tarr_ref, tmsg_ref, tpt_ref,
        jnp.broadcast_to(rf_col, (states, columns)), pick=g,
    )
    _descend(lpar_ref, lkids_ref, loutside_ref, larr_ref, lmsg_ref, lpt_ref, subtree_out)
    w = w_ref[...]
    weight_total = jnp.sum(w, axis=1, keepdims=True) + jnp.sum(wo_ref[...], axis=1, keepdims=True)
    lanes = max(local_edges, top_edges)
    row = jnp.zeros((1, lanes), F32)
    row = _counts(
        row, 0, w, vt, tarr_ref, tmsg_ref,
        lambda c: _dot(basis * jt_ref[c], tvw_ref[:, _cols(c, columns)]),
    )
    top_ref[...] = row[:, 0:top_edges] / weight_total
    row = jnp.zeros((1, lanes), F32)
    row = _counts(row, 0, w, vt, larr_ref, lmsg_ref, lambda c: lmixed_ref[c])
    local_ref[...] = row[:, 0:local_edges] / weight_total


def join(top_parents, pick, parents, halves, tp, tpt, basis, j_top, vecs, inv, rf_row, w_row,
         w_other, lmsgs, lmixed, lpt, taxon_count, paired):
    gat0, gat1 = halves
    columns = gat0.shape[2]
    top_edges = top_parents.shape[0]
    leaf_count = (top_edges + 2) // 2
    local_edges, states, _ = lmsgs.shape
    local_leaves = (local_edges + 2) // 2
    return pl.pallas_call(
        functools.partial(_join_kernel, taxon_count=taxon_count, paired=paired),
        out_shape=(
            jax.ShapeDtypeStruct((1, local_edges), F32),
            jax.ShapeDtypeStruct((1, top_edges), F32),
            jax.ShapeDtypeStruct((1, columns), F32),
        ),
        in_specs=[SMEM] * 3 + [VMEM] * 14,
        out_specs=(VMEM, VMEM, VMEM),
        scratch_shapes=[
            pltpu.VMEM((leaf_count - 1, states, columns), F32),
            pltpu.VMEM((top_edges, states, columns), F32),
            pltpu.VMEM((states, top_edges * columns), F32),
            pltpu.VMEM((states, top_edges * columns), F32),
            pltpu.VMEM((leaf_count - 1, states, columns), F32),
            pltpu.VMEM((states, top_edges * columns), F32),
            pltpu.VMEM((local_leaves - 1, states, columns), F32),
            pltpu.VMEM((states, local_edges * columns), F32),
            pltpu.SMEM((top_edges + 1,), jnp.int32),
            pltpu.SMEM((local_edges + 1,), jnp.int32),
        ],
        compiler_params=PARAMS,
    )(top_parents, pick, parents, gat0, gat1, tp, tpt, basis, j_top, vecs, inv, rf_row, w_row,
      w_other, lmsgs, lmixed, lpt)


def gather_roots(block, groups):
    buf = block[None]
    step = groups // 2
    while step >= 1:
        other = lax.ppermute(buf, "leaf", [(i, i ^ step) for i in range(groups)])
        if step == 1:
            return buf, other
        buf = jnp.stack([buf, other], axis=1).reshape((-1,) + block.shape)
        step //= 2
    return buf, buf


def on_device(
    tips,
    parents,
    branch_lengths,
    top_parents,
    top_lengths,
    weights,
    eig_vectors,
    eig_inverse,
    eig_values,
    labeled_rates,
    root_freq,
):
    groups = lax.axis_size("leaf")
    sites = lax.axis_size("site")
    member_index = lax.axis_index("leaf")
    taxon_count = tips.shape[0] * groups
    lam_row = eig_values[None, :]
    w_row = weights.astype(F32)[None, :]
    if sites == 2:
        w_other = lax.ppermute(w_row, "site", [(0, 1), (1, 0)])
    else:
        w_other = lax.psum(jnp.sum(w_row), "site") - jnp.sum(w_row)
        w_other = jnp.reshape(w_other, (1, 1))

    root_block, msgs, xw, trl = climb(
        parents, branch_lengths, tips, eig_vectors, eig_inverse, lam_row
    )
    paired = groups & (groups - 1) == 0
    if paired:
        halves = gather_roots(root_block, groups)
        pick = jnp.reshape(member_index, (1,)).astype(jnp.int32)
    else:
        gathered = lax.all_gather(root_block, "leaf", axis=0, tiled=False)
        halves = (gathered, gathered)
        pick = jnp.zeros((1,), jnp.int32)
    j_local = jax.vmap(lambda t: integrals(eig_values, t))(branch_lengths)
    j_top = jax.vmap(lambda t: integrals(eig_values, t))(top_lengths)
    lmixed, lpt, tp, tpt, basis = matrices(
        top_lengths, eig_vectors, eig_inverse, labeled_rates, lam_row, j_local, xw, trl
    )
    local_row, top_row, loglik = join(
        top_parents, pick, parents, halves, tp, tpt, basis, j_top, eig_vectors, eig_inverse,
        root_freq[None, :], w_row, w_other, msgs, lmixed, lpt, taxon_count, paired,
    )
    local_sum, top_sum = lax.psum((local_row[0], top_row[0]), "site")
    return (local_sum, top_sum, loglik[0])


def solution(mesh):
    placed = (
        P("leaf", None, "site"),
        P("leaf"),
        P("leaf"),
        P(),
        P(),
        P("site"),
        P(),
        P(),
        P(),
        P(),
        P(),
    )
    return jax.shard_map(
        on_device,
        mesh=mesh,
        in_specs=placed,
        out_specs=(P("leaf"), P(), P("site")),
        check_vma=False,
    )
```

```python
import functools

import jax
import jax.numpy as jnp
from jax import lax
from jax.experimental import pallas as pl
from jax.experimental.pallas import tpu as pltpu
from jax.sharding import PartitionSpec as P

CODONS = 61

PRECISE = lax.Precision.HIGHEST
FAST = lax.Precision.HIGH
F32 = jnp.float32
VMEM_LIMIT = 56 * 1024 * 1024
VMEM = pl.BlockSpec(memory_space=pltpu.VMEM)
SMEM = pl.BlockSpec(memory_space=pltpu.SMEM)


def _dot(a, b):
    return jnp.dot(a, b, precision=FAST, preferred_element_type=F32)


def integrals(eig_values, branch):
    spread = (eig_values[:, None] - eig_values[None, :]) * branch
    near_zero = jnp.abs(spread) < 0.0001
    divisor = jnp.where(near_zero, jnp.ones_like(spread), spread)
    growth = jnp.where(
        near_zero, 1.0 + spread / 2.0 + spread * spread / 6.0, jnp.expm1(spread) / divisor
    )
    return branch * jnp.exp(eig_values[None, :] * branch) * growth


PARAMS = pltpu.CompilerParams(vmem_limit_bytes=VMEM_LIMIT)


def _cols(c, columns):
    return slice(c * columns, (c + 1) * columns)


def _climb_kernel(par_ref, len_ref, leaf_ref, v_ref, vi_ref, lam_ref,
                  root_ref, msg_ref, xw_ref, tr_ref, inner_ref):
    leaf_count = leaf_ref.shape[0]
    edge_count, states, columns = msg_ref.shape
    vecs = v_ref[...]
    inv = vi_ref[...]
    lam = lam_ref[...]
    inner_ref[...] = jnp.ones(inner_ref.shape, F32)
    keep = (lax.broadcasted_iota(jnp.int32, (states, columns), 0) < CODONS).astype(F32)
    logs = jnp.zeros((1, columns), F32)
    for c in range(edge_count):
        if c < leaf_count:
            x = leaf_ref[c] * keep
        else:
            x = inner_ref[c - leaf_count]
            big = jnp.max(x, axis=0, keepdims=True)
            x = x / big
            logs = logs + jnp.log(big)
        trans = _dot(vecs * jnp.exp(lam * len_ref[c]), inv)
        tr_ref[c] = trans
        msg = _dot(trans, x)
        msg_ref[c] = msg
        xw_ref[:, _cols(c, columns)] = x
        p = par_ref[c] - leaf_count
        inner_ref[p] = inner_ref[p] * msg
    x = inner_ref[leaf_count - 2]
    big = jnp.max(x, axis=0, keepdims=True)
    root_ref[0:states, :] = x / big
    root_ref[states:states + 1, :] = logs + jnp.log(big)


def climb(parents, lengths, tips, vecs, inv, lam_row):
    leaf_count, states, columns = tips.shape
    edge_count = parents.shape[0]
    return pl.pallas_call(
        _climb_kernel,
        out_shape=(
            jax.ShapeDtypeStruct((states + 1, columns), F32),
            jax.ShapeDtypeStruct((edge_count, states, columns), F32),
            jax.ShapeDtypeStruct((states, edge_count * columns), F32),
            jax.ShapeDtypeStruct((edge_count, states, states), F32),
        ),
        in_specs=[SMEM, SMEM, VMEM, VMEM, VMEM, VMEM],
        out_specs=(VMEM,) * 4,
        scratch_shapes=[pltpu.VMEM((leaf_count - 1, states, columns), F32)],
        compiler_params=PARAMS,
    )(parents, lengths, tips, vecs, inv, lam_row)


def _local_matrix_kernel(v_ref, vi_ref, lab_ref, jl_ref, xw_ref, trl_ref, w_ref, wo_ref,
                         mixed_ref, ptl_ref, basis_ref, token_ref, wt_ref, vw_ref):
    local_edges, states, columns = mixed_ref.shape
    token_ref[...] = jnp.zeros(token_ref.shape, F32)
    wt_ref[...] = (jnp.sum(w_ref[...], axis=1, keepdims=True)
                   + jnp.sum(wo_ref[...], axis=1, keepdims=True))
    vecs = v_ref[...]
    inv = vi_ref[...]
    basis = _dot(_dot(inv, lab_ref[...]), vecs)
    basis_ref[...] = basis
    vw_ref[...] = _dot(inv, xw_ref[...])
    for c in range(local_edges):
        mixed_ref[c] = _dot(basis * jl_ref[c], vw_ref[:, _cols(c, columns)])
        ptl_ref[c] = trl_ref[c].T


def local_matrices(vecs, inv, labeled, j_local, xw, trl, w_row, w_other):
    local_edges, states, _ = trl.shape
    columns = xw.shape[1] // local_edges
    sq = (states, states)
    return pl.pallas_call(
        _local_matrix_kernel,
        out_shape=(
            jax.ShapeDtypeStruct((local_edges, states, columns), F32),
            jax.ShapeDtypeStruct((local_edges,) + sq, F32),
            jax.ShapeDtypeStruct(sq, F32),
            jax.ShapeDtypeStruct((1, 1), F32),
            jax.ShapeDtypeStruct((1, 1), F32),
        ),
        in_specs=[VMEM] * 8,
        out_specs=(VMEM,) * 5,
        scratch_shapes=[pltpu.VMEM((states, local_edges * columns), F32)],
        compiler_params=PARAMS,
    )(vecs, inv, labeled, j_local, xw, trl, w_row, w_other)


def _top_matrix_kernel(top_len_ref, v_ref, vi_ref, lam_ref, tp_ref, tpt_ref, token_ref):
    top_edges = tp_ref.shape[0]
    token_ref[...] = jnp.zeros(token_ref.shape, F32)
    vecs = v_ref[...]
    inv = vi_ref[...]
    lam = lam_ref[...]
    for c in range(top_edges):
        trans = _dot(vecs * jnp.exp(lam * top_len_ref[c]), inv)
        tp_ref[c] = trans
        tpt_ref[c] = trans.T


def top_matrices(top_lengths, vecs, inv, lam_row):
    top_edges = top_lengths.shape[0]
    states = vecs.shape[0]
    sq = (states, states)
    return pl.pallas_call(
        _top_matrix_kernel,
        out_shape=(
            jax.ShapeDtypeStruct((top_edges,) + sq, F32),
            jax.ShapeDtypeStruct((top_edges,) + sq, F32),
            jax.ShapeDtypeStruct((1, 1), F32),
        ),
        in_specs=[SMEM] + [VMEM] * 3,
        out_specs=(VMEM,) * 3,
        compiler_params=PARAMS,
    )(top_lengths, vecs, inv, lam_row)


def _lane_put(row, lane, value):
    lanes = lax.broadcasted_iota(jnp.int32, row.shape, 1)
    return jnp.where(lanes == lane, value, row)


def _descend(par_ref, kids_ref, outside_ref, arr_ref, msg_ref, pt_ref, root_out, pick=None):
    edge_count = par_ref.shape[0]
    leaf_count = (edge_count + 2) // 2
    columns = msg_ref.shape[2]
    for n in range(edge_count + 1):
        kids_ref[n] = 0
    for e in range(edge_count):
        p = par_ref[e]
        kids_ref[p] = kids_ref[p] + e
    outside_ref[leaf_count - 2] = root_out

    def arriving_of(c):
        p = par_ref[c]
        s = kids_ref[p] - c
        return outside_ref[p - leaf_count] * msg_ref[s]

    def outward(c, arriving):
        out = _dot(pt_ref[c], arriving)
        return out / jnp.max(out, axis=0, keepdims=True)

    for c in range(edge_count - 1, -1, -1):
        arriving = arriving_of(c)
        arr_ref[:, _cols(c, columns)] = arriving
        if c >= leaf_count:
            outside_ref[c - leaf_count] = outward(c, arriving)
    if pick is not None:
        return outward(pick, arriving_of(pick))
    return None


def _counts(row, lane_offset, w, vt, arr_ref, msg_ref, mixed_of):
    edge_count, _, columns = msg_ref.shape
    weighted = _dot(vt, arr_ref[...])
    for c in range(edge_count):
        cols = _cols(c, columns)
        num = jnp.sum(weighted[:, cols] * mixed_of(c), axis=0, keepdims=True)
        den = jnp.sum(arr_ref[:, cols] * msg_ref[c], axis=0, keepdims=True)
        total = jnp.sum(w * num / den, axis=1, keepdims=True)
        row = _lane_put(row, lane_offset + c, total)
    return row


def _join_kernel(tpar_ref, pick_ref, lpar_ref,
                 gat0_ref, gat1_ref, tp_ref, tpt_ref, basis_ref, jt_ref, v_ref, vi_ref, rf_ref,
                 w_ref, wo_ref, lmsg_ref, lmixed_ref, lpt_ref,
                 local_ref, top_ref, loglik_ref,
                 tinner_ref, tmsg_ref, txw_ref, tvw_ref, toutside_ref, tarr_ref,
                 loutside_ref, larr_ref, tkids_ref, lkids_ref, *, taxon_count, paired):
    top_edges = tpar_ref.shape[0]
    leaf_count = (top_edges + 2) // 2
    local_edges = lpar_ref.shape[0]
    states, columns = tmsg_ref.shape[1], tmsg_ref.shape[2]
    g = pick_ref[0]
    tinner_ref[...] = jnp.ones(tinner_ref.shape, F32)
    logs = jnp.zeros((1, columns), F32)
    leaf_logs = jnp.zeros((1, columns), F32)
    for c in range(top_edges):
        if c < leaf_count:
            if paired:
                spot = jnp.bitwise_xor(c, g)
                half = spot // 2
                block = jnp.where(spot % 2 == 0, gat0_ref[half], gat1_ref[half])
            else:
                block = gat0_ref[c]
            x = block[0:states, :]
            leaf_logs = leaf_logs + block[states:states + 1, :]
        else:
            x = tinner_ref[c - leaf_count]
            big = jnp.max(x, axis=0, keepdims=True)
            x = x / big
            logs = logs + jnp.log(big)
        msg = _dot(tp_ref[c], x)
        tmsg_ref[c] = msg
        txw_ref[:, _cols(c, columns)] = x
        p = tpar_ref[c] - leaf_count
        tinner_ref[p] = tinner_ref[p] * msg
    x = tinner_ref[leaf_count - 2]
    big = jnp.max(x, axis=0, keepdims=True)
    logs = logs + jnp.log(big)
    rf = rf_ref[...]
    likelihood = jnp.dot(rf, x / big, precision=PRECISE, preferred_element_type=F32)
    loglik_ref[...] = (jnp.log(likelihood) + logs + leaf_logs) / taxon_count

    eye = (lax.broadcasted_iota(jnp.int32, (states, states), 0)
           == lax.broadcasted_iota(jnp.int32, (states, states), 1))
    rf_col = jnp.sum(jnp.where(eye, rf, 0.0), axis=1, keepdims=True)
    inv = vi_ref[...]
    vt = v_ref[...].T
    basis = basis_ref[...]
    tvw_ref[...] = _dot(inv, txw_ref[...])
    subtree_out = _descend(
        tpar_ref, tkids_ref, toutside_ref, tarr_ref, tmsg_ref, tpt_ref,
        jnp.broadcast_to(rf_col, (states, columns)), pick=g,
    )
    _descend(lpar_ref, lkids_ref, loutside_ref, larr_ref, lmsg_ref, lpt_ref, subtree_out)
    w = w_ref[...]
    weight_total = wo_ref[...]
    lanes = max(local_edges, top_edges)
    row = jnp.zeros((1, lanes), F32)
    row = _counts(
        row, 0, w, vt, tarr_ref, tmsg_ref,
        lambda c: _dot(basis * jt_ref[c], tvw_ref[:, _cols(c, columns)]),
    )
    top_ref[...] = row[:, 0:top_edges] / weight_total
    row = jnp.zeros((1, lanes), F32)
    row = _counts(row, 0, w, vt, larr_ref, lmsg_ref, lambda c: lmixed_ref[c])
    local_ref[...] = row[:, 0:local_edges] / weight_total


def join(top_parents, pick, parents, halves, tp, tpt, basis, j_top, vecs, inv, rf_row, w_row,
         w_other, lmsgs, lmixed, lpt, taxon_count, paired):
    gat0, gat1 = halves
    columns = gat0.shape[2]
    top_edges = top_parents.shape[0]
    leaf_count = (top_edges + 2) // 2
    local_edges, states, _ = lmsgs.shape
    local_leaves = (local_edges + 2) // 2
    return pl.pallas_call(
        functools.partial(_join_kernel, taxon_count=taxon_count, paired=paired),
        out_shape=(
            jax.ShapeDtypeStruct((1, local_edges), F32),
            jax.ShapeDtypeStruct((1, top_edges), F32),
            jax.ShapeDtypeStruct((1, columns), F32),
        ),
        in_specs=[SMEM] * 3 + [VMEM] * 14,
        out_specs=(VMEM, VMEM, VMEM),
        scratch_shapes=[
            pltpu.VMEM((leaf_count - 1, states, columns), F32),
            pltpu.VMEM((top_edges, states, columns), F32),
            pltpu.VMEM((states, top_edges * columns), F32),
            pltpu.VMEM((states, top_edges * columns), F32),
            pltpu.VMEM((leaf_count - 1, states, columns), F32),
            pltpu.VMEM((states, top_edges * columns), F32),
            pltpu.VMEM((local_leaves - 1, states, columns), F32),
            pltpu.VMEM((states, local_edges * columns), F32),
            pltpu.SMEM((top_edges + 1,), jnp.int32),
            pltpu.SMEM((local_edges + 1,), jnp.int32),
        ],
        compiler_params=PARAMS,
    )(top_parents, pick, parents, gat0, gat1, tp, tpt, basis, j_top, vecs, inv, rf_row, w_row,
      w_other, lmsgs, lmixed, lpt)


def gather_roots(block, groups, tokens):
    buf = block[None]
    step = groups // 2
    while step >= 1:
        other = lax.ppermute(buf, "leaf", [(i, i ^ step) for i in range(groups)])
        if step == 1:
            return buf, other
        buf = jnp.stack([buf, other], axis=1).reshape((-1,) + block.shape)
        step //= 2
        if step in tokens:
            buf = buf + tokens[step]
    return buf, buf


def on_device(
    tips,
    parents,
    branch_lengths,
    top_parents,
    top_lengths,
    weights,
    eig_vectors,
    eig_inverse,
    eig_values,
    labeled_rates,
    root_freq,
):
    groups = lax.axis_size("leaf")
    sites = lax.axis_size("site")
    member_index = lax.axis_index("leaf")
    taxon_count = tips.shape[0] * groups
    lam_row = eig_values[None, :]
    w_row = weights.astype(F32)[None, :]
    if sites == 2:
        w_other = lax.ppermute(w_row, "site", [(0, 1), (1, 0)])
    else:
        w_other = lax.psum(jnp.sum(w_row), "site") - jnp.sum(w_row)
        w_other = jnp.reshape(w_other, (1, 1))

    root_block, msgs, xw, trl = climb(
        parents, branch_lengths, tips, eig_vectors, eig_inverse, lam_row
    )
    paired = groups & (groups - 1) == 0
    j_local = jax.vmap(lambda t: integrals(eig_values, t))(branch_lengths)
    j_top = jax.vmap(lambda t: integrals(eig_values, t))(top_lengths)
    tp, tpt, top_token = top_matrices(top_lengths, eig_vectors, eig_inverse, lam_row)
    lmixed, lpt, basis, local_token, weight_total = local_matrices(
        eig_vectors, eig_inverse, labeled_rates, j_local, xw, trl, w_row, w_other
    )
    if paired:
        tokens = {
            groups // 4: j_top[0, 0, 0] * 0.0,
            groups // 8: top_token[0, 0],
            1: local_token[0, 0],
        }
        halves = gather_roots(root_block, groups, tokens)
        pick = jnp.reshape(member_index, (1,)).astype(jnp.int32)
    else:
        gathered = lax.all_gather(root_block, "leaf", axis=0, tiled=False)
        halves = (gathered, gathered)
        pick = jnp.zeros((1,), jnp.int32)
    local_row, top_row, loglik = join(
        top_parents, pick, parents, halves, tp, tpt, basis, j_top, eig_vectors, eig_inverse,
        root_freq[None, :], w_row, weight_total, msgs, lmixed, lpt, taxon_count, paired,
    )
    local_sum, top_sum = lax.psum((local_row[0], top_row[0]), "site")
    return (local_sum, top_sum, loglik[0])


def solution(mesh):
    placed = (
        P("leaf", None, "site"),
        P("leaf"),
        P("leaf"),
        P(),
        P(),
        P("site"),
        P(),
        P(),
        P(),
        P(),
        P(),
    )
    return jax.shard_map(
        on_device,
        mesh=mesh,
        in_specs=placed,
        out_specs=(P("leaf"), P(), P("site")),
        check_vma=False,
    )
```

```python
import functools

import jax
import jax.numpy as jnp
from jax import lax
from jax.experimental import pallas as pl
from jax.experimental.pallas import tpu as pltpu
from jax.sharding import PartitionSpec as P

CODONS = 61

PRECISE = lax.Precision.HIGHEST
FAST = lax.Precision.HIGH
F32 = jnp.float32
VMEM_LIMIT = 56 * 1024 * 1024
VMEM = pl.BlockSpec(memory_space=pltpu.VMEM)
SMEM = pl.BlockSpec(memory_space=pltpu.SMEM)


def _dot(a, b):
    return jnp.dot(a, b, precision=FAST, preferred_element_type=F32)


def integrals(eig_values, branch):
    spread = (eig_values[:, None] - eig_values[None, :]) * branch
    near_zero = jnp.abs(spread) < 0.0001
    divisor = jnp.where(near_zero, jnp.ones_like(spread), spread)
    growth = jnp.where(
        near_zero, 1.0 + spread / 2.0 + spread * spread / 6.0, jnp.expm1(spread) / divisor
    )
    return branch * jnp.exp(eig_values[None, :] * branch) * growth


PARAMS = pltpu.CompilerParams(vmem_limit_bytes=VMEM_LIMIT)


def _cols(c, columns):
    return slice(c * columns, (c + 1) * columns)


def _climb_kernel(par_ref, len_ref, leaf_ref, v_ref, vi_ref, lam_ref,
                  root_ref, msg_ref, xw_ref, tr_ref, inner_ref):
    leaf_count = leaf_ref.shape[0]
    edge_count, states, columns = msg_ref.shape
    vecs = v_ref[...]
    inv = vi_ref[...]
    lam = lam_ref[...]
    inner_ref[...] = jnp.ones(inner_ref.shape, F32)
    keep = (lax.broadcasted_iota(jnp.int32, (states, columns), 0) < CODONS).astype(F32)
    logs = jnp.zeros((1, columns), F32)
    for c in range(edge_count):
        if c < leaf_count:
            x = leaf_ref[c] * keep
        else:
            x = inner_ref[c - leaf_count]
            big = jnp.max(x, axis=0, keepdims=True)
            x = x / big
            logs = logs + jnp.log(big)
        trans = _dot(vecs * jnp.exp(lam * len_ref[c]), inv)
        tr_ref[c] = trans
        msg = _dot(trans, x)
        msg_ref[c] = msg
        xw_ref[:, _cols(c, columns)] = x
        p = par_ref[c] - leaf_count
        inner_ref[p] = inner_ref[p] * msg
    x = inner_ref[leaf_count - 2]
    big = jnp.max(x, axis=0, keepdims=True)
    root_ref[0:states, :] = x / big
    root_ref[states:states + 1, :] = logs + jnp.log(big)


def climb(parents, lengths, tips, vecs, inv, lam_row):
    leaf_count, states, columns = tips.shape
    edge_count = parents.shape[0]
    return pl.pallas_call(
        _climb_kernel,
        out_shape=(
            jax.ShapeDtypeStruct((states + 1, columns), F32),
            jax.ShapeDtypeStruct((edge_count, states, columns), F32),
            jax.ShapeDtypeStruct((states, edge_count * columns), F32),
            jax.ShapeDtypeStruct((edge_count, states, states), F32),
        ),
        in_specs=[SMEM, SMEM, VMEM, VMEM, VMEM, VMEM],
        out_specs=(VMEM,) * 4,
        scratch_shapes=[pltpu.VMEM((leaf_count - 1, states, columns), F32)],
        compiler_params=PARAMS,
    )(parents, lengths, tips, vecs, inv, lam_row)


def _local_matrix_kernel(v_ref, vi_ref, lab_ref, jl_ref, xw_ref, trl_ref, w_ref, wo_ref,
                         mixed_ref, ptl_ref, basis_ref, token_ref, wt_ref, vw_ref):
    local_edges, states, columns = mixed_ref.shape
    token_ref[...] = jnp.zeros(token_ref.shape, F32)
    wt_ref[...] = (jnp.sum(w_ref[...], axis=1, keepdims=True)
                   + jnp.sum(wo_ref[...], axis=1, keepdims=True))
    vecs = v_ref[...]
    inv = vi_ref[...]
    basis = _dot(_dot(inv, lab_ref[...]), vecs)
    basis_ref[...] = basis
    vw_ref[...] = _dot(inv, xw_ref[...])
    for c in range(local_edges):
        mixed_ref[c] = _dot(basis * jl_ref[c], vw_ref[:, _cols(c, columns)])
        ptl_ref[c] = trl_ref[c].T


def local_matrices(vecs, inv, labeled, j_local, xw, trl, w_row, w_other):
    local_edges, states, _ = trl.shape
    columns = xw.shape[1] // local_edges
    sq = (states, states)
    return pl.pallas_call(
        _local_matrix_kernel,
        out_shape=(
            jax.ShapeDtypeStruct((local_edges, states, columns), F32),
            jax.ShapeDtypeStruct((local_edges,) + sq, F32),
            jax.ShapeDtypeStruct(sq, F32),
            jax.ShapeDtypeStruct((1, 1), F32),
            jax.ShapeDtypeStruct((1, 1), F32),
        ),
        in_specs=[VMEM] * 8,
        out_specs=(VMEM,) * 5,
        scratch_shapes=[pltpu.VMEM((states, local_edges * columns), F32)],
        compiler_params=PARAMS,
    )(vecs, inv, labeled, j_local, xw, trl, w_row, w_other)


def _top_matrix_kernel(top_len_ref, v_ref, vi_ref, lam_ref, tp_ref, tpt_ref, token_ref):
    top_edges = tp_ref.shape[0]
    token_ref[...] = jnp.zeros(token_ref.shape, F32)
    vecs = v_ref[...]
    inv = vi_ref[...]
    lam = lam_ref[...]
    for c in range(top_edges):
        trans = _dot(vecs * jnp.exp(lam * top_len_ref[c]), inv)
        tp_ref[c] = trans
        tpt_ref[c] = trans.T


def top_matrices(top_lengths, vecs, inv, lam_row):
    top_edges = top_lengths.shape[0]
    states = vecs.shape[0]
    sq = (states, states)
    return pl.pallas_call(
        _top_matrix_kernel,
        out_shape=(
            jax.ShapeDtypeStruct((top_edges,) + sq, F32),
            jax.ShapeDtypeStruct((top_edges,) + sq, F32),
            jax.ShapeDtypeStruct((1, 1), F32),
        ),
        in_specs=[SMEM] + [VMEM] * 3,
        out_specs=(VMEM,) * 3,
        compiler_params=PARAMS,
    )(top_lengths, vecs, inv, lam_row)


def _lane_put(row, lane, value):
    lanes = lax.broadcasted_iota(jnp.int32, row.shape, 1)
    return jnp.where(lanes == lane, value, row)


def _descend(par_ref, kids_ref, outside_ref, msg_ref, pt_ref, root_out, count, row, pick=None):
    edge_count = par_ref.shape[0]
    leaf_count = (edge_count + 2) // 2
    for n in range(edge_count + 1):
        kids_ref[n] = 0
    for e in range(edge_count):
        p = par_ref[e]
        kids_ref[p] = kids_ref[p] + e
    outside_ref[leaf_count - 2] = root_out

    def arriving_of(c):
        p = par_ref[c]
        s = kids_ref[p] - c
        return outside_ref[p - leaf_count] * msg_ref[s]

    def outward(c, arriving):
        out = _dot(pt_ref[c], arriving)
        return out / jnp.max(out, axis=0, keepdims=True)

    for c in range(edge_count - 1, -1, -1):
        arriving = arriving_of(c)
        if c >= leaf_count:
            outside_ref[c - leaf_count] = outward(c, arriving)
        row = count(c, arriving, row)
    if pick is not None:
        return row, outward(pick, arriving_of(pick))
    return row, None


def _count_fn(w, vt, weight_total, msg_ref, mixed_ref):
    def count(c, arriving, row):
        weighted = _dot(vt, arriving)
        num = jnp.sum(weighted * mixed_ref[c], axis=0, keepdims=True)
        den = jnp.sum(arriving * msg_ref[c], axis=0, keepdims=True)
        total = jnp.sum(w * num / den, axis=1, keepdims=True)
        return _lane_put(row, c, total / weight_total)
    return count


def _join_kernel(tpar_ref, pick_ref, lpar_ref,
                 gat0_ref, gat1_ref, tp_ref, tpt_ref, basis_ref, jt_ref, v_ref, vi_ref, rf_ref,
                 w_ref, wo_ref, lmsg_ref, lmixed_ref, lpt_ref,
                 local_ref, top_ref, loglik_ref,
                 tinner_ref, tmsg_ref, tmixed_ref, toutside_ref,
                 loutside_ref, tkids_ref, lkids_ref, *, taxon_count, paired):
    top_edges = tpar_ref.shape[0]
    leaf_count = (top_edges + 2) // 2
    local_edges = lpar_ref.shape[0]
    states, columns = tmsg_ref.shape[1], tmsg_ref.shape[2]
    g = pick_ref[0]
    inv = vi_ref[...]
    basis = basis_ref[...]
    tinner_ref[...] = jnp.ones(tinner_ref.shape, F32)
    logs = jnp.zeros((1, columns), F32)
    leaf_logs = jnp.zeros((1, columns), F32)
    for c in range(top_edges):
        if c < leaf_count:
            if paired:
                spot = jnp.bitwise_xor(c, g)
                half = spot // 2
                block = jnp.where(spot % 2 == 0, gat0_ref[half], gat1_ref[half])
            else:
                block = gat0_ref[c]
            x = block[0:states, :]
            leaf_logs = leaf_logs + block[states:states + 1, :]
        else:
            x = tinner_ref[c - leaf_count]
            big = jnp.max(x, axis=0, keepdims=True)
            x = x / big
            logs = logs + jnp.log(big)
        msg = _dot(tp_ref[c], x)
        tmsg_ref[c] = msg
        p = tpar_ref[c] - leaf_count
        tinner_ref[p] = tinner_ref[p] * msg
        tmixed_ref[c] = _dot(basis * jt_ref[c], _dot(inv, x))
    x = tinner_ref[leaf_count - 2]
    big = jnp.max(x, axis=0, keepdims=True)
    logs = logs + jnp.log(big)
    rf = rf_ref[...]
    likelihood = jnp.dot(rf, x / big, precision=PRECISE, preferred_element_type=F32)
    loglik_ref[...] = (jnp.log(likelihood) + logs + leaf_logs) / taxon_count

    eye = (lax.broadcasted_iota(jnp.int32, (states, states), 0)
           == lax.broadcasted_iota(jnp.int32, (states, states), 1))
    rf_col = jnp.sum(jnp.where(eye, rf, 0.0), axis=1, keepdims=True)
    vt = v_ref[...].T
    w = w_ref[...]
    weight_total = wo_ref[...]
    lanes = max(local_edges, top_edges)
    row, subtree_out = _descend(
        tpar_ref, tkids_ref, toutside_ref, tmsg_ref, tpt_ref,
        jnp.broadcast_to(rf_col, (states, columns)),
        _count_fn(w, vt, weight_total, tmsg_ref, tmixed_ref), jnp.zeros((1, lanes), F32), pick=g,
    )
    top_ref[...] = row[:, 0:top_edges]
    row, _ = _descend(
        lpar_ref, lkids_ref, loutside_ref, lmsg_ref, lpt_ref, subtree_out,
        _count_fn(w, vt, weight_total, lmsg_ref, lmixed_ref), jnp.zeros((1, lanes), F32),
    )
    local_ref[...] = row[:, 0:local_edges]


def join(top_parents, pick, parents, halves, tp, tpt, basis, j_top, vecs, inv, rf_row, w_row,
         w_other, lmsgs, lmixed, lpt, taxon_count, paired):
    gat0, gat1 = halves
    columns = gat0.shape[2]
    top_edges = top_parents.shape[0]
    leaf_count = (top_edges + 2) // 2
    local_edges, states, _ = lmsgs.shape
    local_leaves = (local_edges + 2) // 2
    return pl.pallas_call(
        functools.partial(_join_kernel, taxon_count=taxon_count, paired=paired),
        out_shape=(
            jax.ShapeDtypeStruct((1, local_edges), F32),
            jax.ShapeDtypeStruct((1, top_edges), F32),
            jax.ShapeDtypeStruct((1, columns), F32),
        ),
        in_specs=[SMEM] * 3 + [VMEM] * 14,
        out_specs=(VMEM, VMEM, VMEM),
        scratch_shapes=[
            pltpu.VMEM((leaf_count - 1, states, columns), F32),
            pltpu.VMEM((top_edges, states, columns), F32),
            pltpu.VMEM((top_edges, states, columns), F32),
            pltpu.VMEM((leaf_count - 1, states, columns), F32),
            pltpu.VMEM((local_leaves - 1, states, columns), F32),
            pltpu.SMEM((top_edges + 1,), jnp.int32),
            pltpu.SMEM((local_edges + 1,), jnp.int32),
        ],
        compiler_params=PARAMS,
    )(top_parents, pick, parents, gat0, gat1, tp, tpt, basis, j_top, vecs, inv, rf_row, w_row,
      w_other, lmsgs, lmixed, lpt)


def gather_roots(block, groups, tokens):
    buf = block[None]
    step = groups // 2
    while step >= 1:
        other = lax.ppermute(buf, "leaf", [(i, i ^ step) for i in range(groups)])
        if step == 1:
            return buf, other
        buf = jnp.stack([buf, other], axis=1).reshape((-1,) + block.shape)
        step //= 2
        if step in tokens:
            buf = buf + tokens[step]
    return buf, buf


def on_device(
    tips,
    parents,
    branch_lengths,
    top_parents,
    top_lengths,
    weights,
    eig_vectors,
    eig_inverse,
    eig_values,
    labeled_rates,
    root_freq,
):
    groups = lax.axis_size("leaf")
    sites = lax.axis_size("site")
    member_index = lax.axis_index("leaf")
    taxon_count = tips.shape[0] * groups
    lam_row = eig_values[None, :]
    w_row = weights.astype(F32)[None, :]
    if sites == 2:
        w_other = lax.ppermute(w_row, "site", [(0, 1), (1, 0)])
    else:
        w_other = lax.psum(jnp.sum(w_row), "site") - jnp.sum(w_row)
        w_other = jnp.reshape(w_other, (1, 1))

    root_block, msgs, xw, trl = climb(
        parents, branch_lengths, tips, eig_vectors, eig_inverse, lam_row
    )
    paired = groups & (groups - 1) == 0
    j_local = jax.vmap(lambda t: integrals(eig_values, t))(branch_lengths)
    j_top = jax.vmap(lambda t: integrals(eig_values, t))(top_lengths)
    tp, tpt, top_token = top_matrices(top_lengths, eig_vectors, eig_inverse, lam_row)
    lmixed, lpt, basis, local_token, weight_total = local_matrices(
        eig_vectors, eig_inverse, labeled_rates, j_local, xw, trl, w_row, w_other
    )
    if paired:
        tokens = {
            groups // 4: j_top[0, 0, 0] * 0.0,
            groups // 8: top_token[0, 0],
            1: local_token[0, 0],
        }
        halves = gather_roots(root_block, groups, tokens)
        pick = jnp.reshape(member_index, (1,)).astype(jnp.int32)
    else:
        gathered = lax.all_gather(root_block, "leaf", axis=0, tiled=False)
        halves = (gathered, gathered)
        pick = jnp.zeros((1,), jnp.int32)
    local_row, top_row, loglik = join(
        top_parents, pick, parents, halves, tp, tpt, basis, j_top, eig_vectors, eig_inverse,
        root_freq[None, :], w_row, weight_total, msgs, lmixed, lpt, taxon_count, paired,
    )
    local_sum, top_sum = lax.psum((local_row[0], top_row[0]), "site")
    return (local_sum, top_sum, loglik[0])


def solution(mesh):
    placed = (
        P("leaf", None, "site"),
        P("leaf"),
        P("leaf"),
        P(),
        P(),
        P("site"),
        P(),
        P(),
        P(),
        P(),
        P(),
    )
    return jax.shard_map(
        on_device,
        mesh=mesh,
        in_specs=placed,
        out_specs=(P("leaf"), P(), P("site")),
        check_vma=False,
    )
```

```python
import functools

import jax
import jax.numpy as jnp
from jax import lax
from jax.experimental import pallas as pl
from jax.experimental.pallas import tpu as pltpu
from jax.sharding import PartitionSpec as P

CODONS = 61

PRECISE = lax.Precision.HIGHEST
FAST = lax.Precision.HIGH
F32 = jnp.float32
VMEM_LIMIT = 56 * 1024 * 1024
VMEM = pl.BlockSpec(memory_space=pltpu.VMEM)
SMEM = pl.BlockSpec(memory_space=pltpu.SMEM)


def _dot(a, b):
    return jnp.dot(a, b, precision=FAST, preferred_element_type=F32)


def integrals(eig_values, branch):
    spread = (eig_values[:, None] - eig_values[None, :]) * branch
    near_zero = jnp.abs(spread) < 0.0001
    divisor = jnp.where(near_zero, jnp.ones_like(spread), spread)
    growth = jnp.where(
        near_zero, 1.0 + spread / 2.0 + spread * spread / 6.0, jnp.expm1(spread) / divisor
    )
    return branch * jnp.exp(eig_values[None, :] * branch) * growth


PARAMS = pltpu.CompilerParams(vmem_limit_bytes=VMEM_LIMIT)


def _cols(c, columns):
    return slice(c * columns, (c + 1) * columns)


def _climb_kernel(par_ref, len_ref, leaf_ref, v_ref, vi_ref, lam_ref,
                  root_ref, msg_ref, xw_ref, tr_ref, inner_ref):
    leaf_count = leaf_ref.shape[0]
    edge_count, states, columns = msg_ref.shape
    vecs = v_ref[...]
    inv = vi_ref[...]
    lam = lam_ref[...]
    inner_ref[...] = jnp.ones(inner_ref.shape, F32)
    keep = (lax.broadcasted_iota(jnp.int32, (states, columns), 0) < CODONS).astype(F32)
    logs = jnp.zeros((1, columns), F32)
    for c in range(edge_count):
        if c < leaf_count:
            x = leaf_ref[c] * keep
        else:
            x = inner_ref[c - leaf_count]
            big = jnp.max(x, axis=0, keepdims=True)
            x = x / big
            logs = logs + jnp.log(big)
        trans = _dot(vecs * jnp.exp(lam * len_ref[c]), inv)
        tr_ref[c] = trans
        msg = _dot(trans, x)
        msg_ref[c] = msg
        xw_ref[:, _cols(c, columns)] = x
        p = par_ref[c] - leaf_count
        inner_ref[p] = inner_ref[p] * msg
    x = inner_ref[leaf_count - 2]
    big = jnp.max(x, axis=0, keepdims=True)
    root_ref[0:states, :] = x / big
    root_ref[states:states + 1, :] = logs + jnp.log(big)


def climb(parents, lengths, tips, vecs, inv, lam_row):
    leaf_count, states, columns = tips.shape
    edge_count = parents.shape[0]
    return pl.pallas_call(
        _climb_kernel,
        out_shape=(
            jax.ShapeDtypeStruct((states + 1, columns), F32),
            jax.ShapeDtypeStruct((edge_count, states, columns), F32),
            jax.ShapeDtypeStruct((states, edge_count * columns), F32),
            jax.ShapeDtypeStruct((edge_count, states, states), F32),
        ),
        in_specs=[SMEM, SMEM, VMEM, VMEM, VMEM, VMEM],
        out_specs=(VMEM,) * 4,
        scratch_shapes=[pltpu.VMEM((leaf_count - 1, states, columns), F32)],
        compiler_params=PARAMS,
    )(parents, lengths, tips, vecs, inv, lam_row)


def _local_matrix_kernel(v_ref, vi_ref, lab_ref, jl_ref, xw_ref, trl_ref,
                         mixed_ref, ptl_ref, basis_ref, token_ref, vw_ref):
    local_edges, states, columns = mixed_ref.shape
    token_ref[...] = jnp.zeros(token_ref.shape, F32)
    vecs = v_ref[...]
    inv = vi_ref[...]
    basis = _dot(_dot(inv, lab_ref[...]), vecs)
    basis_ref[...] = basis
    vw_ref[...] = _dot(inv, xw_ref[...])
    for c in range(local_edges):
        mixed_ref[c] = _dot(basis * jl_ref[c], vw_ref[:, _cols(c, columns)])
        ptl_ref[c] = trl_ref[c].T


def local_matrices(vecs, inv, labeled, j_local, xw, trl):
    local_edges, states, _ = trl.shape
    columns = xw.shape[1] // local_edges
    sq = (states, states)
    return pl.pallas_call(
        _local_matrix_kernel,
        out_shape=(
            jax.ShapeDtypeStruct((local_edges, states, columns), F32),
            jax.ShapeDtypeStruct((local_edges,) + sq, F32),
            jax.ShapeDtypeStruct(sq, F32),
            jax.ShapeDtypeStruct((1, 1), F32),
        ),
        in_specs=[VMEM] * 6,
        out_specs=(VMEM,) * 4,
        scratch_shapes=[pltpu.VMEM((states, local_edges * columns), F32)],
        compiler_params=PARAMS,
    )(vecs, inv, labeled, j_local, xw, trl)


def _top_matrix_kernel(top_len_ref, v_ref, vi_ref, lam_ref, tp_ref, tpt_ref, token_ref):
    top_edges = tp_ref.shape[0]
    token_ref[...] = jnp.zeros(token_ref.shape, F32)
    vecs = v_ref[...]
    inv = vi_ref[...]
    lam = lam_ref[...]
    for c in range(top_edges):
        trans = _dot(vecs * jnp.exp(lam * top_len_ref[c]), inv)
        tp_ref[c] = trans
        tpt_ref[c] = trans.T


def top_matrices(top_lengths, vecs, inv, lam_row):
    top_edges = top_lengths.shape[0]
    states = vecs.shape[0]
    sq = (states, states)
    return pl.pallas_call(
        _top_matrix_kernel,
        out_shape=(
            jax.ShapeDtypeStruct((top_edges,) + sq, F32),
            jax.ShapeDtypeStruct((top_edges,) + sq, F32),
            jax.ShapeDtypeStruct((1, 1), F32),
        ),
        in_specs=[SMEM] + [VMEM] * 3,
        out_specs=(VMEM,) * 3,
        compiler_params=PARAMS,
    )(top_lengths, vecs, inv, lam_row)


def _lane_put(row, lane, value):
    lanes = lax.broadcasted_iota(jnp.int32, row.shape, 1)
    return jnp.where(lanes == lane, value, row)


def _descend(par_ref, kids_ref, outside_ref, arr_ref, msg_ref, pt_ref, root_out, pick=None):
    edge_count = par_ref.shape[0]
    leaf_count = (edge_count + 2) // 2
    columns = msg_ref.shape[2]
    for n in range(edge_count + 1):
        kids_ref[n] = 0
    for e in range(edge_count):
        p = par_ref[e]
        kids_ref[p] = kids_ref[p] + e
    outside_ref[leaf_count - 2] = root_out

    def arriving_of(c):
        p = par_ref[c]
        s = kids_ref[p] - c
        return outside_ref[p - leaf_count] * msg_ref[s]

    def outward(c, arriving):
        out = _dot(pt_ref[c], arriving)
        return out / jnp.max(out, axis=0, keepdims=True)

    for c in range(edge_count - 1, -1, -1):
        arriving = arriving_of(c)
        arr_ref[:, _cols(c, columns)] = arriving
        if c >= leaf_count:
            outside_ref[c - leaf_count] = outward(c, arriving)
    if pick is not None:
        return outward(pick, arriving_of(pick))
    return None


def _counts(row, lane_offset, w, vt, arr_ref, msg_ref, mixed_of):
    edge_count, _, columns = msg_ref.shape
    weighted = _dot(vt, arr_ref[...])
    for c in range(edge_count):
        cols = _cols(c, columns)
        num = jnp.sum(weighted[:, cols] * mixed_of(c), axis=0, keepdims=True)
        den = jnp.sum(arr_ref[:, cols] * msg_ref[c], axis=0, keepdims=True)
        total = jnp.sum(w * num / den, axis=1, keepdims=True)
        row = _lane_put(row, lane_offset + c, total)
    return row


def _join_kernel(tpar_ref, pick_ref, lpar_ref,
                 gat0_ref, gat1_ref, tp_ref, tpt_ref, basis_ref, jt_ref, v_ref, vi_ref, rf_ref,
                 w_ref, wo_ref, lmsg_ref, lmixed_ref, lpt_ref,
                 local_ref, top_ref, loglik_ref,
                 tinner_ref, tmsg_ref, txw_ref, tvw_ref, toutside_ref, tarr_ref,
                 loutside_ref, larr_ref, tkids_ref, lkids_ref, *, taxon_count, paired):
    top_edges = tpar_ref.shape[0]
    leaf_count = (top_edges + 2) // 2
    local_edges = lpar_ref.shape[0]
    states, columns = tmsg_ref.shape[1], tmsg_ref.shape[2]
    g = pick_ref[0]
    tinner_ref[...] = jnp.ones(tinner_ref.shape, F32)
    logs = jnp.zeros((1, columns), F32)
    leaf_logs = jnp.zeros((1, columns), F32)
    for c in range(top_edges):
        if c < leaf_count:
            if paired:
                spot = jnp.bitwise_xor(c, g)
                half = spot // 2
                block = jnp.where(spot % 2 == 0, gat0_ref[half], gat1_ref[half])
            else:
                block = gat0_ref[c]
            x = block[0:states, :]
            leaf_logs = leaf_logs + block[states:states + 1, :]
        else:
            x = tinner_ref[c - leaf_count]
            big = jnp.max(x, axis=0, keepdims=True)
            x = x / big
            logs = logs + jnp.log(big)
        msg = _dot(tp_ref[c], x)
        tmsg_ref[c] = msg
        txw_ref[:, _cols(c, columns)] = x
        p = tpar_ref[c] - leaf_count
        tinner_ref[p] = tinner_ref[p] * msg
    x = tinner_ref[leaf_count - 2]
    big = jnp.max(x, axis=0, keepdims=True)
    logs = logs + jnp.log(big)
    rf = rf_ref[...]
    likelihood = jnp.dot(rf, x / big, precision=PRECISE, preferred_element_type=F32)
    loglik_ref[...] = (jnp.log(likelihood) + logs + leaf_logs) / taxon_count

    eye = (lax.broadcasted_iota(jnp.int32, (states, states), 0)
           == lax.broadcasted_iota(jnp.int32, (states, states), 1))
    rf_col = jnp.sum(jnp.where(eye, rf, 0.0), axis=1, keepdims=True)
    inv = vi_ref[...]
    vt = v_ref[...].T
    basis = basis_ref[...]
    tvw_ref[...] = _dot(inv, txw_ref[...])
    subtree_out = _descend(
        tpar_ref, tkids_ref, toutside_ref, tarr_ref, tmsg_ref, tpt_ref,
        jnp.broadcast_to(rf_col, (states, columns)), pick=g,
    )
    _descend(lpar_ref, lkids_ref, loutside_ref, larr_ref, lmsg_ref, lpt_ref, subtree_out)
    w = w_ref[...]
    weight_total = jnp.sum(w, axis=1, keepdims=True) + jnp.sum(wo_ref[...], axis=1, keepdims=True)
    lanes = max(local_edges, top_edges)
    row = jnp.zeros((1, lanes), F32)
    row = _counts(
        row, 0, w, vt, tarr_ref, tmsg_ref,
        lambda c: _dot(basis * jt_ref[c], tvw_ref[:, _cols(c, columns)]),
    )
    top_ref[...] = row[:, 0:top_edges] / weight_total
    row = jnp.zeros((1, lanes), F32)
    row = _counts(row, 0, w, vt, larr_ref, lmsg_ref, lambda c: lmixed_ref[c])
    local_ref[...] = row[:, 0:local_edges] / weight_total


def join(top_parents, pick, parents, halves, tp, tpt, basis, j_top, vecs, inv, rf_row, w_row,
         w_other, lmsgs, lmixed, lpt, taxon_count, paired):
    gat0, gat1 = halves
    columns = gat0.shape[2]
    top_edges = top_parents.shape[0]
    leaf_count = (top_edges + 2) // 2
    local_edges, states, _ = lmsgs.shape
    local_leaves = (local_edges + 2) // 2
    return pl.pallas_call(
        functools.partial(_join_kernel, taxon_count=taxon_count, paired=paired),
        out_shape=(
            jax.ShapeDtypeStruct((1, local_edges), F32),
            jax.ShapeDtypeStruct((1, top_edges), F32),
            jax.ShapeDtypeStruct((1, columns), F32),
        ),
        in_specs=[SMEM] * 3 + [VMEM] * 14,
        out_specs=(VMEM, VMEM, VMEM),
        scratch_shapes=[
            pltpu.VMEM((leaf_count - 1, states, columns), F32),
            pltpu.VMEM((top_edges, states, columns), F32),
            pltpu.VMEM((states, top_edges * columns), F32),
            pltpu.VMEM((states, top_edges * columns), F32),
            pltpu.VMEM((leaf_count - 1, states, columns), F32),
            pltpu.VMEM((states, top_edges * columns), F32),
            pltpu.VMEM((local_leaves - 1, states, columns), F32),
            pltpu.VMEM((states, local_edges * columns), F32),
            pltpu.SMEM((top_edges + 1,), jnp.int32),
            pltpu.SMEM((local_edges + 1,), jnp.int32),
        ],
        compiler_params=PARAMS,
    )(top_parents, pick, parents, gat0, gat1, tp, tpt, basis, j_top, vecs, inv, rf_row, w_row,
      w_other, lmsgs, lmixed, lpt)


def gather_roots(block, groups, tokens):
    buf = block[None]
    step = groups // 2
    while step >= 1:
        other = lax.ppermute(buf, "leaf", [(i, i ^ step) for i in range(groups)])
        if step == 1:
            return buf, other
        buf = jnp.stack([buf, other], axis=1).reshape((-1,) + block.shape)
        step //= 2
        if step in tokens:
            buf = buf + tokens[step]
    return buf, buf


def on_device(
    tips,
    parents,
    branch_lengths,
    top_parents,
    top_lengths,
    weights,
    eig_vectors,
    eig_inverse,
    eig_values,
    labeled_rates,
    root_freq,
):
    groups = lax.axis_size("leaf")
    sites = lax.axis_size("site")
    member_index = lax.axis_index("leaf")
    taxon_count = tips.shape[0] * groups
    lam_row = eig_values[None, :]
    w_row = weights.astype(F32)[None, :]
    if sites == 2:
        w_other = lax.ppermute(w_row, "site", [(0, 1), (1, 0)])
    else:
        w_other = lax.psum(jnp.sum(w_row), "site") - jnp.sum(w_row)
        w_other = jnp.reshape(w_other, (1, 1))

    root_block, msgs, xw, trl = climb(
        parents, branch_lengths, tips, eig_vectors, eig_inverse, lam_row
    )
    paired = groups & (groups - 1) == 0
    j_local = jax.vmap(lambda t: integrals(eig_values, t))(branch_lengths)
    j_top = jax.vmap(lambda t: integrals(eig_values, t))(top_lengths)
    tp, tpt, top_token = top_matrices(top_lengths, eig_vectors, eig_inverse, lam_row)
    lmixed, lpt, basis, local_token = local_matrices(
        eig_vectors, eig_inverse, labeled_rates, j_local, xw, trl
    )
    if paired:
        tokens = {
            groups // 4: j_top[0, 0, 0] * 0.0,
            groups // 8: top_token[0, 0],
            1: local_token[0, 0],
        }
        halves = gather_roots(root_block, groups, tokens)
        pick = jnp.reshape(member_index, (1,)).astype(jnp.int32)
    else:
        gathered = lax.all_gather(root_block, "leaf", axis=0, tiled=False)
        halves = (gathered, gathered)
        pick = jnp.zeros((1,), jnp.int32)
    local_row, top_row, loglik = join(
        top_parents, pick, parents, halves, tp, tpt, basis, j_top, eig_vectors, eig_inverse,
        root_freq[None, :], w_row, w_other, msgs, lmixed, lpt, taxon_count, paired,
    )
    local_sum, top_sum = lax.psum((local_row[0], top_row[0]), "site")
    return (local_sum, top_sum, loglik[0])


def solution(mesh):
    placed = (
        P("leaf", None, "site"),
        P("leaf"),
        P("leaf"),
        P(),
        P(),
        P("site"),
        P(),
        P(),
        P(),
        P(),
        P(),
    )
    return jax.shard_map(
        on_device,
        mesh=mesh,
        in_specs=placed,
        out_specs=(P("leaf"), P(), P("site")),
        check_vma=False,
    )
```

```python
import functools

import jax
import jax.numpy as jnp
from jax import lax
from jax.experimental import pallas as pl
from jax.experimental.pallas import tpu as pltpu
from jax.sharding import PartitionSpec as P

CODONS = 61

PRECISE = lax.Precision.HIGHEST
FAST = lax.Precision.HIGH
F32 = jnp.float32
VMEM_LIMIT = 56 * 1024 * 1024
VMEM = pl.BlockSpec(memory_space=pltpu.VMEM)
SMEM = pl.BlockSpec(memory_space=pltpu.SMEM)


def _dot(a, b):
    return jnp.dot(a, b, precision=FAST, preferred_element_type=F32)


def integrals(eig_values, branch):
    spread = (eig_values[:, None] - eig_values[None, :]) * branch
    near_zero = jnp.abs(spread) < 0.0001
    divisor = jnp.where(near_zero, jnp.ones_like(spread), spread)
    growth = jnp.where(
        near_zero, 1.0 + spread / 2.0 + spread * spread / 6.0, jnp.expm1(spread) / divisor
    )
    return branch * jnp.exp(eig_values[None, :] * branch) * growth


PARAMS = pltpu.CompilerParams(vmem_limit_bytes=VMEM_LIMIT)


def _cols(c, columns):
    return slice(c * columns, (c + 1) * columns)


def _climb_kernel(par_ref, len_ref, leaf_ref, v_ref, vi_ref, lam_ref,
                  root_ref, msg_ref, xw_ref, tr_ref, inner_ref):
    leaf_count = leaf_ref.shape[0]
    edge_count, states, columns = msg_ref.shape
    vecs = v_ref[...]
    inv = vi_ref[...]
    lam = lam_ref[...]
    inner_ref[...] = jnp.ones(inner_ref.shape, F32)
    keep = (lax.broadcasted_iota(jnp.int32, (states, columns), 0) < CODONS).astype(F32)
    logs = jnp.zeros((1, columns), F32)
    for c in range(edge_count):
        if c < leaf_count:
            x = leaf_ref[c] * keep
        else:
            x = inner_ref[c - leaf_count]
            big = jnp.max(x, axis=0, keepdims=True)
            x = x / big
            logs = logs + jnp.log(big)
        trans = _dot(vecs * jnp.exp(lam * len_ref[c]), inv)
        tr_ref[c] = trans
        msg = _dot(trans, x)
        msg_ref[c] = msg
        xw_ref[:, _cols(c, columns)] = x
        p = par_ref[c] - leaf_count
        inner_ref[p] = inner_ref[p] * msg
    x = inner_ref[leaf_count - 2]
    big = jnp.max(x, axis=0, keepdims=True)
    root_ref[0:states, :] = x / big
    root_ref[states:states + 1, :] = logs + jnp.log(big)


def climb(parents, lengths, tips, vecs, inv, lam_row):
    leaf_count, states, columns = tips.shape
    edge_count = parents.shape[0]
    return pl.pallas_call(
        _climb_kernel,
        out_shape=(
            jax.ShapeDtypeStruct((states + 1, columns), F32),
            jax.ShapeDtypeStruct((edge_count, states, columns), F32),
            jax.ShapeDtypeStruct((states, edge_count * columns), F32),
            jax.ShapeDtypeStruct((edge_count, states, states), F32),
        ),
        in_specs=[SMEM, SMEM, VMEM, VMEM, VMEM, VMEM],
        out_specs=(VMEM,) * 4,
        scratch_shapes=[pltpu.VMEM((leaf_count - 1, states, columns), F32)],
        compiler_params=PARAMS,
    )(parents, lengths, tips, vecs, inv, lam_row)


def _local_matrix_kernel(v_ref, vi_ref, lab_ref, jl_ref, xw_ref, trl_ref,
                         mixed_ref, ptl_ref, basis_ref, token_ref, vw_ref):
    local_edges, states, columns = mixed_ref.shape
    token_ref[...] = jnp.zeros(token_ref.shape, F32)
    vecs = v_ref[...]
    inv = vi_ref[...]
    basis = _dot(_dot(inv, lab_ref[...]), vecs)
    basis_ref[...] = basis
    vw_ref[...] = _dot(inv, xw_ref[...])
    for c in range(local_edges):
        mixed_ref[c] = _dot(basis * jl_ref[c], vw_ref[:, _cols(c, columns)])
        ptl_ref[c] = trl_ref[c].T


def local_matrices(vecs, inv, labeled, j_local, xw, trl):
    local_edges, states, _ = trl.shape
    columns = xw.shape[1] // local_edges
    sq = (states, states)
    return pl.pallas_call(
        _local_matrix_kernel,
        out_shape=(
            jax.ShapeDtypeStruct((local_edges, states, columns), F32),
            jax.ShapeDtypeStruct((local_edges,) + sq, F32),
            jax.ShapeDtypeStruct(sq, F32),
            jax.ShapeDtypeStruct((1, 1), F32),
        ),
        in_specs=[VMEM] * 6,
        out_specs=(VMEM,) * 4,
        scratch_shapes=[pltpu.VMEM((states, local_edges * columns), F32)],
        compiler_params=PARAMS,
    )(vecs, inv, labeled, j_local, xw, trl)


def _top_matrix_kernel(top_len_ref, v_ref, vi_ref, lam_ref, tp_ref, tpt_ref, token_ref):
    top_edges = tp_ref.shape[0]
    token_ref[...] = jnp.zeros(token_ref.shape, F32)
    vecs = v_ref[...]
    inv = vi_ref[...]
    lam = lam_ref[...]
    for c in range(top_edges):
        trans = _dot(vecs * jnp.exp(lam * top_len_ref[c]), inv)
        tp_ref[c] = trans
        tpt_ref[c] = trans.T


def top_matrices(top_lengths, vecs, inv, lam_row):
    top_edges = top_lengths.shape[0]
    states = vecs.shape[0]
    sq = (states, states)
    return pl.pallas_call(
        _top_matrix_kernel,
        out_shape=(
            jax.ShapeDtypeStruct((top_edges,) + sq, F32),
            jax.ShapeDtypeStruct((top_edges,) + sq, F32),
            jax.ShapeDtypeStruct((1, 1), F32),
        ),
        in_specs=[SMEM] + [VMEM] * 3,
        out_specs=(VMEM,) * 3,
        compiler_params=PARAMS,
    )(top_lengths, vecs, inv, lam_row)


def _lane_put(row, lane, value):
    lanes = lax.broadcasted_iota(jnp.int32, row.shape, 1)
    return jnp.where(lanes == lane, value, row)


def _descend(par_ref, kids_ref, outside_ref, arr_ref, msg_ref, pt_ref, root_out, pick=None):
    edge_count = par_ref.shape[0]
    leaf_count = (edge_count + 2) // 2
    columns = msg_ref.shape[2]
    for n in range(edge_count + 1):
        kids_ref[n] = 0
    for e in range(edge_count):
        p = par_ref[e]
        kids_ref[p] = kids_ref[p] + e
    outside_ref[leaf_count - 2] = root_out

    def arriving_of(c):
        p = par_ref[c]
        s = kids_ref[p] - c
        return outside_ref[p - leaf_count] * msg_ref[s]

    def outward(c, arriving):
        out = _dot(pt_ref[c], arriving)
        return out / jnp.max(out, axis=0, keepdims=True)

    for c in range(edge_count - 1, -1, -1):
        arriving = arriving_of(c)
        arr_ref[:, _cols(c, columns)] = arriving
        if c >= leaf_count:
            outside_ref[c - leaf_count] = outward(c, arriving)
    if pick is not None:
        return outward(pick, arriving_of(pick))
    return None


def _counts(row, lane_offset, w, vt, arr_ref, msg_ref, mixed_of):
    edge_count, _, columns = msg_ref.shape
    weighted = _dot(vt, arr_ref[...])
    for c in range(edge_count):
        cols = _cols(c, columns)
        num = jnp.sum(weighted[:, cols] * mixed_of(c), axis=0, keepdims=True)
        den = jnp.sum(arr_ref[:, cols] * msg_ref[c], axis=0, keepdims=True)
        total = jnp.sum(w * num / den, axis=1, keepdims=True)
        row = _lane_put(row, lane_offset + c, total)
    return row


def _join_kernel(tpar_ref, pick_ref, lpar_ref,
                 gat0_ref, gat1_ref, tp_ref, tpt_ref, basis_ref, jt_ref, v_ref, vi_ref, rf_ref,
                 w_ref, wo_ref, lmsg_ref, lmixed_ref, lpt_ref,
                 local_ref, top_ref, loglik_ref,
                 tinner_ref, tmsg_ref, txw_ref, tvw_ref, toutside_ref, tarr_ref,
                 loutside_ref, larr_ref, tkids_ref, lkids_ref, *, taxon_count, paired):
    top_edges = tpar_ref.shape[0]
    leaf_count = (top_edges + 2) // 2
    local_edges = lpar_ref.shape[0]
    states, columns = tmsg_ref.shape[1], tmsg_ref.shape[2]
    g = pick_ref[0]
    tinner_ref[...] = jnp.ones(tinner_ref.shape, F32)
    logs = jnp.zeros((1, columns), F32)
    leaf_logs = jnp.zeros((1, columns), F32)
    for c in range(top_edges):
        if c < leaf_count:
            if paired:
                spot = jnp.bitwise_xor(c, g)
                half = spot // 2
                block = jnp.where(spot % 2 == 0, gat0_ref[half], gat1_ref[half])
            else:
                block = gat0_ref[c]
            x = block[0:states, :]
            leaf_logs = leaf_logs + block[states:states + 1, :]
        else:
            x = tinner_ref[c - leaf_count]
            big = jnp.max(x, axis=0, keepdims=True)
            x = x / big
            logs = logs + jnp.log(big)
        msg = _dot(tp_ref[c], x)
        tmsg_ref[c] = msg
        txw_ref[:, _cols(c, columns)] = x
        p = tpar_ref[c] - leaf_count
        tinner_ref[p] = tinner_ref[p] * msg
    x = tinner_ref[leaf_count - 2]
    big = jnp.max(x, axis=0, keepdims=True)
    logs = logs + jnp.log(big)
    rf = rf_ref[...]
    likelihood = jnp.dot(rf, x / big, precision=PRECISE, preferred_element_type=F32)
    loglik_ref[...] = (jnp.log(likelihood) + logs + leaf_logs) / taxon_count

    eye = (lax.broadcasted_iota(jnp.int32, (states, states), 0)
           == lax.broadcasted_iota(jnp.int32, (states, states), 1))
    rf_col = jnp.sum(jnp.where(eye, rf, 0.0), axis=1, keepdims=True)
    inv = vi_ref[...]
    vt = v_ref[...].T
    basis = basis_ref[...]
    tvw_ref[...] = _dot(inv, txw_ref[...])
    subtree_out = _descend(
        tpar_ref, tkids_ref, toutside_ref, tarr_ref, tmsg_ref, tpt_ref,
        jnp.broadcast_to(rf_col, (states, columns)), pick=g,
    )
    _descend(lpar_ref, lkids_ref, loutside_ref, larr_ref, lmsg_ref, lpt_ref, subtree_out)
    w = w_ref[...]
    weight_total = jnp.sum(w, axis=1, keepdims=True) + jnp.sum(wo_ref[...], axis=1, keepdims=True)
    lanes = max(local_edges, top_edges)
    row = jnp.zeros((1, lanes), F32)
    row = _counts(
        row, 0, w, vt, tarr_ref, tmsg_ref,
        lambda c: _dot(basis * jt_ref[c], tvw_ref[:, _cols(c, columns)]),
    )
    top_ref[...] = row[:, 0:top_edges] / weight_total
    row = jnp.zeros((1, lanes), F32)
    row = _counts(row, 0, w, vt, larr_ref, lmsg_ref, lambda c: lmixed_ref[c])
    local_ref[...] = row[:, 0:local_edges] / weight_total


def join(top_parents, pick, parents, halves, tp, tpt, basis, j_top, vecs, inv, rf_row, w_row,
         w_other, lmsgs, lmixed, lpt, taxon_count, paired):
    gat0, gat1 = halves
    columns = gat0.shape[2]
    top_edges = top_parents.shape[0]
    leaf_count = (top_edges + 2) // 2
    local_edges, states, _ = lmsgs.shape
    local_leaves = (local_edges + 2) // 2
    return pl.pallas_call(
        functools.partial(_join_kernel, taxon_count=taxon_count, paired=paired),
        out_shape=(
            jax.ShapeDtypeStruct((1, local_edges), F32),
            jax.ShapeDtypeStruct((1, top_edges), F32),
            jax.ShapeDtypeStruct((1, columns), F32),
        ),
        in_specs=[SMEM] * 3 + [VMEM] * 14,
        out_specs=(VMEM, VMEM, VMEM),
        scratch_shapes=[
            pltpu.VMEM((leaf_count - 1, states, columns), F32),
            pltpu.VMEM((top_edges, states, columns), F32),
            pltpu.VMEM((states, top_edges * columns), F32),
            pltpu.VMEM((states, top_edges * columns), F32),
            pltpu.VMEM((leaf_count - 1, states, columns), F32),
            pltpu.VMEM((states, top_edges * columns), F32),
            pltpu.VMEM((local_leaves - 1, states, columns), F32),
            pltpu.VMEM((states, local_edges * columns), F32),
            pltpu.SMEM((top_edges + 1,), jnp.int32),
            pltpu.SMEM((local_edges + 1,), jnp.int32),
        ],
        compiler_params=PARAMS,
    )(top_parents, pick, parents, gat0, gat1, tp, tpt, basis, j_top, vecs, inv, rf_row, w_row,
      w_other, lmsgs, lmixed, lpt)


def gather_roots(block, groups, tokens):
    buf = block[None]
    step = groups // 2
    while step >= 1:
        other = lax.ppermute(buf, "leaf", [(i, i ^ step) for i in range(groups)])
        if step == 1:
            return buf, other
        buf = jnp.stack([buf, other], axis=1).reshape((-1,) + block.shape)
        step //= 2
        if step in tokens:
            spot = (0, block.shape[0] - 1, 0)
            buf = buf.at[spot].add(tokens[step])
    return buf, buf


def on_device(
    tips,
    parents,
    branch_lengths,
    top_parents,
    top_lengths,
    weights,
    eig_vectors,
    eig_inverse,
    eig_values,
    labeled_rates,
    root_freq,
):
    groups = lax.axis_size("leaf")
    sites = lax.axis_size("site")
    member_index = lax.axis_index("leaf")
    taxon_count = tips.shape[0] * groups
    lam_row = eig_values[None, :]
    w_row = weights.astype(F32)[None, :]
    if sites == 2:
        w_other = lax.ppermute(w_row, "site", [(0, 1), (1, 0)])
    else:
        w_other = lax.psum(jnp.sum(w_row), "site") - jnp.sum(w_row)
        w_other = jnp.reshape(w_other, (1, 1))

    root_block, msgs, xw, trl = climb(
        parents, branch_lengths, tips, eig_vectors, eig_inverse, lam_row
    )
    paired = groups & (groups - 1) == 0
    j_local = jax.vmap(lambda t: integrals(eig_values, t))(branch_lengths)
    j_top = jax.vmap(lambda t: integrals(eig_values, t))(top_lengths)
    tp, tpt, top_token = top_matrices(top_lengths, eig_vectors, eig_inverse, lam_row)
    lmixed, lpt, basis, local_token = local_matrices(
        eig_vectors, eig_inverse, labeled_rates, j_local, xw, trl
    )
    if paired:
        tokens = {
            groups // 4: j_top[0, 0, 0] * 0.0,
            groups // 8: top_token[0, 0],
            1: local_token[0, 0],
        }
        halves = gather_roots(root_block, groups, tokens)
        pick = jnp.reshape(member_index, (1,)).astype(jnp.int32)
    else:
        gathered = lax.all_gather(root_block, "leaf", axis=0, tiled=False)
        halves = (gathered, gathered)
        pick = jnp.zeros((1,), jnp.int32)
    local_row, top_row, loglik = join(
        top_parents, pick, parents, halves, tp, tpt, basis, j_top, eig_vectors, eig_inverse,
        root_freq[None, :], w_row, w_other, msgs, lmixed, lpt, taxon_count, paired,
    )
    local_sum, top_sum = lax.psum((local_row[0], top_row[0]), "site")
    return (local_sum, top_sum, loglik[0])


def solution(mesh):
    placed = (
        P("leaf", None, "site"),
        P("leaf"),
        P("leaf"),
        P(),
        P(),
        P("site"),
        P(),
        P(),
        P(),
        P(),
        P(),
    )
    return jax.shard_map(
        on_device,
        mesh=mesh,
        in_specs=placed,
        out_specs=(P("leaf"), P(), P("site")),
        check_vma=False,
    )
```

```python
import functools

import jax
import jax.numpy as jnp
from jax import lax
from jax.experimental import pallas as pl
from jax.experimental.pallas import tpu as pltpu
from jax.sharding import PartitionSpec as P

CODONS = 61

PRECISE = lax.Precision.HIGHEST
FAST = lax.Precision.HIGH
F32 = jnp.float32
VMEM_LIMIT = 56 * 1024 * 1024
VMEM = pl.BlockSpec(memory_space=pltpu.VMEM)
SMEM = pl.BlockSpec(memory_space=pltpu.SMEM)


def _dot(a, b):
    return jnp.dot(a, b, precision=FAST, preferred_element_type=F32)


def integrals(eig_values, branch):
    spread = (eig_values[:, None] - eig_values[None, :]) * branch
    near_zero = jnp.abs(spread) < 0.0001
    divisor = jnp.where(near_zero, jnp.ones_like(spread), spread)
    growth = jnp.where(
        near_zero, 1.0 + spread / 2.0 + spread * spread / 6.0, jnp.expm1(spread) / divisor
    )
    return branch * jnp.exp(eig_values[None, :] * branch) * growth


PARAMS = pltpu.CompilerParams(vmem_limit_bytes=VMEM_LIMIT)


def _cols(c, columns):
    return slice(c * columns, (c + 1) * columns)


def _climb_kernel(par_ref, len_ref, leaf_ref, v_ref, vi_ref, lam_ref,
                  root_ref, msg_ref, xw_ref, tr_ref, inner_ref):
    leaf_count = leaf_ref.shape[0]
    edge_count, states, columns = msg_ref.shape
    vecs = v_ref[...]
    inv = vi_ref[...]
    lam = lam_ref[...]
    inner_ref[...] = jnp.ones(inner_ref.shape, F32)
    keep = (lax.broadcasted_iota(jnp.int32, (states, columns), 0) < CODONS).astype(F32)
    logs = jnp.zeros((1, columns), F32)
    for c in range(edge_count):
        if c < leaf_count:
            x = leaf_ref[c] * keep
        else:
            x = inner_ref[c - leaf_count]
            big = jnp.max(x, axis=0, keepdims=True)
            x = x / big
            logs = logs + jnp.log(big)
        trans = _dot(vecs * jnp.exp(lam * len_ref[c]), inv)
        tr_ref[c] = trans
        msg = _dot(trans, x)
        msg_ref[c] = msg
        xw_ref[:, _cols(c, columns)] = x
        p = par_ref[c] - leaf_count
        inner_ref[p] = inner_ref[p] * msg
    x = inner_ref[leaf_count - 2]
    big = jnp.max(x, axis=0, keepdims=True)
    root_ref[0:states, :] = x / big
    root_ref[states:states + 1, :] = logs + jnp.log(big)


def climb(parents, lengths, tips, vecs, inv, lam_row):
    leaf_count, states, columns = tips.shape
    edge_count = parents.shape[0]
    return pl.pallas_call(
        _climb_kernel,
        out_shape=(
            jax.ShapeDtypeStruct((states + 1, columns), F32),
            jax.ShapeDtypeStruct((edge_count, states, columns), F32),
            jax.ShapeDtypeStruct((states, edge_count * columns), F32),
            jax.ShapeDtypeStruct((edge_count, states, states), F32),
        ),
        in_specs=[SMEM, SMEM, VMEM, VMEM, VMEM, VMEM],
        out_specs=(VMEM,) * 4,
        scratch_shapes=[pltpu.VMEM((leaf_count - 1, states, columns), F32)],
        compiler_params=PARAMS,
    )(parents, lengths, tips, vecs, inv, lam_row)


def _matrix_kernel(top_len_ref, v_ref, vi_ref, lab_ref, lam_ref, jl_ref, xw_ref,
                   mixed_ref, tp_ref, basis_ref, vw_ref):
    local_edges, states, columns = mixed_ref.shape
    top_edges = tp_ref.shape[0]
    vecs = v_ref[...]
    inv = vi_ref[...]
    lam = lam_ref[...]
    basis = _dot(_dot(inv, lab_ref[...]), vecs)
    basis_ref[...] = basis
    vw_ref[...] = _dot(inv, xw_ref[...])
    for c in range(local_edges):
        mixed_ref[c] = _dot(basis * jl_ref[c], vw_ref[:, _cols(c, columns)])
    for c in range(top_edges):
        tp_ref[c] = _dot(vecs * jnp.exp(lam * top_len_ref[c]), inv)


def matrices(top_lengths, vecs, inv, labeled, lam_row, j_local, xw):
    local_edges, states, _ = j_local.shape
    columns = xw.shape[1] // local_edges
    top_edges = top_lengths.shape[0]
    sq = (states, states)
    return pl.pallas_call(
        _matrix_kernel,
        out_shape=(
            jax.ShapeDtypeStruct((local_edges, states, columns), F32),
            jax.ShapeDtypeStruct((top_edges,) + sq, F32),
            jax.ShapeDtypeStruct(sq, F32),
        ),
        in_specs=[SMEM] + [VMEM] * 6,
        out_specs=(VMEM,) * 3,
        scratch_shapes=[pltpu.VMEM((states, local_edges * columns), F32)],
        compiler_params=PARAMS,
    )(top_lengths, vecs, inv, labeled, lam_row, j_local, xw)


def _lane_put(row, lane, value):
    lanes = lax.broadcasted_iota(jnp.int32, row.shape, 1)
    return jnp.where(lanes == lane, value, row)


def _descend(par_ref, kids_ref, outside_ref, arr_ref, msg_ref, pt_ref, root_out, pick=None):
    edge_count = par_ref.shape[0]
    leaf_count = (edge_count + 2) // 2
    columns = msg_ref.shape[2]
    for n in range(edge_count + 1):
        kids_ref[n] = 0
    for e in range(edge_count):
        p = par_ref[e]
        kids_ref[p] = kids_ref[p] + e
    outside_ref[leaf_count - 2] = root_out

    def arriving_of(c):
        p = par_ref[c]
        s = kids_ref[p] - c
        return outside_ref[p - leaf_count] * msg_ref[s]

    def outward(c, arriving):
        out = lax.dot_general(pt_ref[c], arriving, (((0,), (0,)), ((), ())),
                              precision=FAST, preferred_element_type=F32)
        return out / jnp.max(out, axis=0, keepdims=True)

    for c in range(edge_count - 1, -1, -1):
        arriving = arriving_of(c)
        arr_ref[:, _cols(c, columns)] = arriving
        if c >= leaf_count:
            outside_ref[c - leaf_count] = outward(c, arriving)
    if pick is not None:
        return outward(pick, arriving_of(pick))
    return None


def _counts(row, lane_offset, w, vt, arr_ref, msg_ref, mixed_of):
    edge_count, _, columns = msg_ref.shape
    weighted = _dot(vt, arr_ref[...])
    for c in range(edge_count):
        cols = _cols(c, columns)
        num = jnp.sum(weighted[:, cols] * mixed_of(c), axis=0, keepdims=True)
        den = jnp.sum(arr_ref[:, cols] * msg_ref[c], axis=0, keepdims=True)
        total = jnp.sum(w * num / den, axis=1, keepdims=True)
        row = _lane_put(row, lane_offset + c, total)
    return row


def _join_kernel(tpar_ref, pick_ref, lpar_ref,
                 gat0_ref, gat1_ref, tp_ref, tpt_ref, basis_ref, jt_ref, v_ref, vi_ref, rf_ref,
                 w_ref, wo_ref, lmsg_ref, lmixed_ref, lpt_ref,
                 local_ref, top_ref, loglik_ref,
                 tinner_ref, tmsg_ref, txw_ref, tvw_ref, toutside_ref, tarr_ref,
                 loutside_ref, larr_ref, tkids_ref, lkids_ref, *, taxon_count, paired):
    top_edges = tpar_ref.shape[0]
    leaf_count = (top_edges + 2) // 2
    local_edges = lpar_ref.shape[0]
    states, columns = tmsg_ref.shape[1], tmsg_ref.shape[2]
    g = pick_ref[0]
    tinner_ref[...] = jnp.ones(tinner_ref.shape, F32)
    logs = jnp.zeros((1, columns), F32)
    leaf_logs = jnp.zeros((1, columns), F32)
    for c in range(top_edges):
        if c < leaf_count:
            if paired:
                spot = jnp.bitwise_xor(c, g)
                half = spot // 2
                block = jnp.where(spot % 2 == 0, gat0_ref[half], gat1_ref[half])
            else:
                block = gat0_ref[c]
            x = block[0:states, :]
            leaf_logs = leaf_logs + block[states:states + 1, :]
        else:
            x = tinner_ref[c - leaf_count]
            big = jnp.max(x, axis=0, keepdims=True)
            x = x / big
            logs = logs + jnp.log(big)
        msg = _dot(tp_ref[c], x)
        tmsg_ref[c] = msg
        txw_ref[:, _cols(c, columns)] = x
        p = tpar_ref[c] - leaf_count
        tinner_ref[p] = tinner_ref[p] * msg
    x = tinner_ref[leaf_count - 2]
    big = jnp.max(x, axis=0, keepdims=True)
    logs = logs + jnp.log(big)
    rf = rf_ref[...]
    likelihood = jnp.dot(rf, x / big, precision=PRECISE, preferred_element_type=F32)
    loglik_ref[...] = (jnp.log(likelihood) + logs + leaf_logs) / taxon_count

    eye = (lax.broadcasted_iota(jnp.int32, (states, states), 0)
           == lax.broadcasted_iota(jnp.int32, (states, states), 1))
    rf_col = jnp.sum(jnp.where(eye, rf, 0.0), axis=1, keepdims=True)
    inv = vi_ref[...]
    vt = v_ref[...].T
    basis = basis_ref[...]
    tvw_ref[...] = _dot(inv, txw_ref[...])
    subtree_out = _descend(
        tpar_ref, tkids_ref, toutside_ref, tarr_ref, tmsg_ref, tpt_ref,
        jnp.broadcast_to(rf_col, (states, columns)), pick=g,
    )
    _descend(lpar_ref, lkids_ref, loutside_ref, larr_ref, lmsg_ref, lpt_ref, subtree_out)
    w = w_ref[...]
    weight_total = jnp.sum(w, axis=1, keepdims=True) + jnp.sum(wo_ref[...], axis=1, keepdims=True)
    lanes = max(local_edges, top_edges)
    row = jnp.zeros((1, lanes), F32)
    row = _counts(
        row, 0, w, vt, tarr_ref, tmsg_ref,
        lambda c: _dot(basis * jt_ref[c], tvw_ref[:, _cols(c, columns)]),
    )
    top_ref[...] = row[:, 0:top_edges] / weight_total
    row = jnp.zeros((1, lanes), F32)
    row = _counts(row, 0, w, vt, larr_ref, lmsg_ref, lambda c: lmixed_ref[c])
    local_ref[...] = row[:, 0:local_edges] / weight_total


def join(top_parents, pick, parents, halves, tp, tpt, basis, j_top, vecs, inv, rf_row, w_row,
         w_other, lmsgs, lmixed, lpt, taxon_count, paired):
    gat0, gat1 = halves
    columns = gat0.shape[2]
    top_edges = top_parents.shape[0]
    leaf_count = (top_edges + 2) // 2
    local_edges, states, _ = lmsgs.shape
    local_leaves = (local_edges + 2) // 2
    return pl.pallas_call(
        functools.partial(_join_kernel, taxon_count=taxon_count, paired=paired),
        out_shape=(
            jax.ShapeDtypeStruct((1, local_edges), F32),
            jax.ShapeDtypeStruct((1, top_edges), F32),
            jax.ShapeDtypeStruct((1, columns), F32),
        ),
        in_specs=[SMEM] * 3 + [VMEM] * 14,
        out_specs=(VMEM, VMEM, VMEM),
        scratch_shapes=[
            pltpu.VMEM((leaf_count - 1, states, columns), F32),
            pltpu.VMEM((top_edges, states, columns), F32),
            pltpu.VMEM((states, top_edges * columns), F32),
            pltpu.VMEM((states, top_edges * columns), F32),
            pltpu.VMEM((leaf_count - 1, states, columns), F32),
            pltpu.VMEM((states, top_edges * columns), F32),
            pltpu.VMEM((local_leaves - 1, states, columns), F32),
            pltpu.VMEM((states, local_edges * columns), F32),
            pltpu.SMEM((top_edges + 1,), jnp.int32),
            pltpu.SMEM((local_edges + 1,), jnp.int32),
        ],
        compiler_params=PARAMS,
    )(top_parents, pick, parents, gat0, gat1, tp, tpt, basis, j_top, vecs, inv, rf_row, w_row,
      w_other, lmsgs, lmixed, lpt)


def gather_roots(block, groups):
    buf = block[None]
    step = groups // 2
    while step >= 1:
        other = lax.ppermute(buf, "leaf", [(i, i ^ step) for i in range(groups)])
        if step == 1:
            return buf, other
        buf = jnp.stack([buf, other], axis=1).reshape((-1,) + block.shape)
        step //= 2
    return buf, buf


def on_device(
    tips,
    parents,
    branch_lengths,
    top_parents,
    top_lengths,
    weights,
    eig_vectors,
    eig_inverse,
    eig_values,
    labeled_rates,
    root_freq,
):
    groups = lax.axis_size("leaf")
    sites = lax.axis_size("site")
    member_index = lax.axis_index("leaf")
    taxon_count = tips.shape[0] * groups
    lam_row = eig_values[None, :]
    w_row = weights.astype(F32)[None, :]
    if sites == 2:
        w_other = lax.ppermute(w_row, "site", [(0, 1), (1, 0)])
    else:
        w_other = lax.psum(jnp.sum(w_row), "site") - jnp.sum(w_row)
        w_other = jnp.reshape(w_other, (1, 1))

    root_block, msgs, xw, trl = climb(
        parents, branch_lengths, tips, eig_vectors, eig_inverse, lam_row
    )
    paired = groups & (groups - 1) == 0
    if paired:
        halves = gather_roots(root_block, groups)
        pick = jnp.reshape(member_index, (1,)).astype(jnp.int32)
    else:
        gathered = lax.all_gather(root_block, "leaf", axis=0, tiled=False)
        halves = (gathered, gathered)
        pick = jnp.zeros((1,), jnp.int32)
    j_local = jax.vmap(lambda t: integrals(eig_values, t))(branch_lengths)
    j_top = jax.vmap(lambda t: integrals(eig_values, t))(top_lengths)
    lmixed, tp, basis = matrices(
        top_lengths, eig_vectors, eig_inverse, labeled_rates, lam_row, j_local, xw
    )
    lpt, tpt = trl, tp
    local_row, top_row, loglik = join(
        top_parents, pick, parents, halves, tp, tpt, basis, j_top, eig_vectors, eig_inverse,
        root_freq[None, :], w_row, w_other, msgs, lmixed, lpt, taxon_count, paired,
    )
    local_sum, top_sum = lax.psum((local_row[0], top_row[0]), "site")
    return (local_sum, top_sum, loglik[0])


def solution(mesh):
    placed = (
        P("leaf", None, "site"),
        P("leaf"),
        P("leaf"),
        P(),
        P(),
        P("site"),
        P(),
        P(),
        P(),
        P(),
        P(),
    )
    return jax.shard_map(
        on_device,
        mesh=mesh,
        in_specs=placed,
        out_specs=(P("leaf"), P(), P("site")),
        check_vma=False,
    )
```

```python
import functools

import jax
import jax.numpy as jnp
from jax import lax
from jax.experimental import pallas as pl
from jax.experimental.pallas import tpu as pltpu
from jax.sharding import PartitionSpec as P

CODONS = 61

PRECISE = lax.Precision.HIGHEST
FAST = lax.Precision.HIGH
F32 = jnp.float32
VMEM_LIMIT = 56 * 1024 * 1024
VMEM = pl.BlockSpec(memory_space=pltpu.VMEM)
SMEM = pl.BlockSpec(memory_space=pltpu.SMEM)


def _dot(a, b):
    return jnp.dot(a, b, precision=FAST, preferred_element_type=F32)


def integrals(eig_values, branch):
    spread = (eig_values[:, None] - eig_values[None, :]) * branch
    near_zero = jnp.abs(spread) < 0.0001
    divisor = jnp.where(near_zero, jnp.ones_like(spread), spread)
    growth = jnp.where(
        near_zero, 1.0 + spread / 2.0 + spread * spread / 6.0, jnp.expm1(spread) / divisor
    )
    return branch * jnp.exp(eig_values[None, :] * branch) * growth


PARAMS = pltpu.CompilerParams(vmem_limit_bytes=VMEM_LIMIT)


def _cols(c, columns):
    return slice(c * columns, (c + 1) * columns)


def _climb_kernel(par_ref, len_ref, leaf_ref, v_ref, vi_ref, lam_ref,
                  root_ref, msg_ref, xw_ref, tr_ref, inner_ref):
    leaf_count = leaf_ref.shape[0]
    edge_count, states, columns = msg_ref.shape
    vecs = v_ref[...]
    inv = vi_ref[...]
    lam = lam_ref[...]
    inner_ref[...] = jnp.ones(inner_ref.shape, F32)
    keep = (lax.broadcasted_iota(jnp.int32, (states, columns), 0) < CODONS).astype(F32)
    logs = jnp.zeros((1, columns), F32)
    for c in range(edge_count):
        if c < leaf_count:
            x = leaf_ref[c] * keep
        else:
            x = inner_ref[c - leaf_count]
            big = jnp.max(x, axis=0, keepdims=True)
            x = x / big
            logs = logs + jnp.log(big)
        trans = _dot(vecs * jnp.exp(lam * len_ref[c]), inv)
        tr_ref[c] = trans
        msg = _dot(trans, x)
        msg_ref[c] = msg
        xw_ref[:, _cols(c, columns)] = x
        p = par_ref[c] - leaf_count
        inner_ref[p] = inner_ref[p] * msg
    x = inner_ref[leaf_count - 2]
    big = jnp.max(x, axis=0, keepdims=True)
    root_ref[0:states, :] = x / big
    root_ref[states:states + 1, :] = logs + jnp.log(big)


def climb(parents, lengths, tips, vecs, inv, lam_row):
    leaf_count, states, columns = tips.shape
    edge_count = parents.shape[0]
    return pl.pallas_call(
        _climb_kernel,
        out_shape=(
            jax.ShapeDtypeStruct((states + 1, columns), F32),
            jax.ShapeDtypeStruct((edge_count, states, columns), F32),
            jax.ShapeDtypeStruct((states, edge_count * columns), F32),
            jax.ShapeDtypeStruct((edge_count, states, states), F32),
        ),
        in_specs=[SMEM, SMEM, VMEM, VMEM, VMEM, VMEM],
        out_specs=(VMEM,) * 4,
        scratch_shapes=[pltpu.VMEM((leaf_count - 1, states, columns), F32)],
        compiler_params=PARAMS,
    )(parents, lengths, tips, vecs, inv, lam_row)


def _matrix_kernel(top_len_ref, v_ref, vi_ref, lab_ref, lam_ref, jl_ref, xw_ref, carry_ref,
                   mixed_ref, tp_ref, basis_ref, carried_ref, vw_ref):
    carried_ref[...] = carry_ref[...]
    local_edges, states, columns = mixed_ref.shape
    top_edges = tp_ref.shape[0]
    vecs = v_ref[...]
    inv = vi_ref[...]
    lam = lam_ref[...]
    basis = _dot(_dot(inv, lab_ref[...]), vecs)
    basis_ref[...] = basis
    vw_ref[...] = _dot(inv, xw_ref[...])
    for c in range(local_edges):
        mixed_ref[c] = _dot(basis * jl_ref[c], vw_ref[:, _cols(c, columns)])
    for c in range(top_edges):
        tp_ref[c] = _dot(vecs * jnp.exp(lam * top_len_ref[c]), inv)


def matrices(top_lengths, vecs, inv, labeled, lam_row, j_local, xw, carry):
    local_edges, states, _ = j_local.shape
    columns = xw.shape[1] // local_edges
    top_edges = top_lengths.shape[0]
    sq = (states, states)
    return pl.pallas_call(
        _matrix_kernel,
        out_shape=(
            jax.ShapeDtypeStruct((local_edges, states, columns), F32),
            jax.ShapeDtypeStruct((top_edges,) + sq, F32),
            jax.ShapeDtypeStruct(sq, F32),
            jax.ShapeDtypeStruct(carry.shape, F32),
        ),
        in_specs=[SMEM] + [VMEM] * 7,
        out_specs=(VMEM,) * 4,
        scratch_shapes=[pltpu.VMEM((states, local_edges * columns), F32)],
        compiler_params=PARAMS,
    )(top_lengths, vecs, inv, labeled, lam_row, j_local, xw, carry)


def _lane_put(row, lane, value):
    lanes = lax.broadcasted_iota(jnp.int32, row.shape, 1)
    return jnp.where(lanes == lane, value, row)


def _descend(par_ref, kids_ref, outside_ref, arr_ref, msg_ref, pt_ref, root_out, pick=None):
    edge_count = par_ref.shape[0]
    leaf_count = (edge_count + 2) // 2
    columns = msg_ref.shape[2]
    for n in range(edge_count + 1):
        kids_ref[n] = 0
    for e in range(edge_count):
        p = par_ref[e]
        kids_ref[p] = kids_ref[p] + e
    outside_ref[leaf_count - 2] = root_out

    def arriving_of(c):
        p = par_ref[c]
        s = kids_ref[p] - c
        return outside_ref[p - leaf_count] * msg_ref[s]

    def outward(c, arriving):
        out = lax.dot_general(pt_ref[c], arriving, (((0,), (0,)), ((), ())),
                              precision=FAST, preferred_element_type=F32)
        return out / jnp.max(out, axis=0, keepdims=True)

    for c in range(edge_count - 1, -1, -1):
        arriving = arriving_of(c)
        arr_ref[:, _cols(c, columns)] = arriving
        if c >= leaf_count:
            outside_ref[c - leaf_count] = outward(c, arriving)
    if pick is not None:
        return outward(pick, arriving_of(pick))
    return None


def _counts(row, lane_offset, w, vt, arr_ref, msg_ref, mixed_of):
    edge_count, _, columns = msg_ref.shape
    weighted = _dot(vt, arr_ref[...])
    for c in range(edge_count):
        cols = _cols(c, columns)
        num = jnp.sum(weighted[:, cols] * mixed_of(c), axis=0, keepdims=True)
        den = jnp.sum(arr_ref[:, cols] * msg_ref[c], axis=0, keepdims=True)
        total = jnp.sum(w * num / den, axis=1, keepdims=True)
        row = _lane_put(row, lane_offset + c, total)
    return row


def _join_kernel(tpar_ref, pick_ref, lpar_ref,
                 gat0_ref, gat1_ref, tp_ref, tpt_ref, basis_ref, jt_ref, v_ref, vi_ref, rf_ref,
                 w_ref, wo_ref, lmsg_ref, lmixed_ref, lpt_ref,
                 local_ref, top_ref, loglik_ref,
                 tinner_ref, tmsg_ref, txw_ref, tvw_ref, toutside_ref, tarr_ref,
                 loutside_ref, larr_ref, tkids_ref, lkids_ref, *, taxon_count, paired):
    top_edges = tpar_ref.shape[0]
    leaf_count = (top_edges + 2) // 2
    local_edges = lpar_ref.shape[0]
    states, columns = tmsg_ref.shape[1], tmsg_ref.shape[2]
    g = pick_ref[0]
    tinner_ref[...] = jnp.ones(tinner_ref.shape, F32)
    logs = jnp.zeros((1, columns), F32)
    leaf_logs = jnp.zeros((1, columns), F32)
    for c in range(top_edges):
        if c < leaf_count:
            if paired:
                spot = jnp.bitwise_xor(c, g)
                half = spot // 2
                block = jnp.where(spot % 2 == 0, gat0_ref[half], gat1_ref[half])
            else:
                block = gat0_ref[c]
            x = block[0:states, :]
            leaf_logs = leaf_logs + block[states:states + 1, :]
        else:
            x = tinner_ref[c - leaf_count]
            big = jnp.max(x, axis=0, keepdims=True)
            x = x / big
            logs = logs + jnp.log(big)
        msg = _dot(tp_ref[c], x)
        tmsg_ref[c] = msg
        txw_ref[:, _cols(c, columns)] = x
        p = tpar_ref[c] - leaf_count
        tinner_ref[p] = tinner_ref[p] * msg
    x = tinner_ref[leaf_count - 2]
    big = jnp.max(x, axis=0, keepdims=True)
    logs = logs + jnp.log(big)
    rf = rf_ref[...]
    likelihood = jnp.dot(rf, x / big, precision=PRECISE, preferred_element_type=F32)
    loglik_ref[...] = (jnp.log(likelihood) + logs + leaf_logs) / taxon_count

    eye = (lax.broadcasted_iota(jnp.int32, (states, states), 0)
           == lax.broadcasted_iota(jnp.int32, (states, states), 1))
    rf_col = jnp.sum(jnp.where(eye, rf, 0.0), axis=1, keepdims=True)
    inv = vi_ref[...]
    vt = v_ref[...].T
    basis = basis_ref[...]
    tvw_ref[...] = _dot(inv, txw_ref[...])
    subtree_out = _descend(
        tpar_ref, tkids_ref, toutside_ref, tarr_ref, tmsg_ref, tpt_ref,
        jnp.broadcast_to(rf_col, (states, columns)), pick=g,
    )
    _descend(lpar_ref, lkids_ref, loutside_ref, larr_ref, lmsg_ref, lpt_ref, subtree_out)
    w = w_ref[...]
    weight_total = jnp.sum(w, axis=1, keepdims=True) + jnp.sum(wo_ref[...], axis=1, keepdims=True)
    lanes = max(local_edges, top_edges)
    row = jnp.zeros((1, lanes), F32)
    row = _counts(
        row, 0, w, vt, tarr_ref, tmsg_ref,
        lambda c: _dot(basis * jt_ref[c], tvw_ref[:, _cols(c, columns)]),
    )
    top_ref[...] = row[:, 0:top_edges] / weight_total
    row = jnp.zeros((1, lanes), F32)
    row = _counts(row, 0, w, vt, larr_ref, lmsg_ref, lambda c: lmixed_ref[c])
    local_ref[...] = row[:, 0:local_edges] / weight_total


def join(top_parents, pick, parents, halves, tp, tpt, basis, j_top, vecs, inv, rf_row, w_row,
         w_other, lmsgs, lmixed, lpt, taxon_count, paired):
    gat0, gat1 = halves
    columns = gat0.shape[2]
    top_edges = top_parents.shape[0]
    leaf_count = (top_edges + 2) // 2
    local_edges, states, _ = lmsgs.shape
    local_leaves = (local_edges + 2) // 2
    return pl.pallas_call(
        functools.partial(_join_kernel, taxon_count=taxon_count, paired=paired),
        out_shape=(
            jax.ShapeDtypeStruct((1, local_edges), F32),
            jax.ShapeDtypeStruct((1, top_edges), F32),
            jax.ShapeDtypeStruct((1, columns), F32),
        ),
        in_specs=[SMEM] * 3 + [VMEM] * 14,
        out_specs=(VMEM, VMEM, VMEM),
        scratch_shapes=[
            pltpu.VMEM((leaf_count - 1, states, columns), F32),
            pltpu.VMEM((top_edges, states, columns), F32),
            pltpu.VMEM((states, top_edges * columns), F32),
            pltpu.VMEM((states, top_edges * columns), F32),
            pltpu.VMEM((leaf_count - 1, states, columns), F32),
            pltpu.VMEM((states, top_edges * columns), F32),
            pltpu.VMEM((local_leaves - 1, states, columns), F32),
            pltpu.VMEM((states, local_edges * columns), F32),
            pltpu.SMEM((top_edges + 1,), jnp.int32),
            pltpu.SMEM((local_edges + 1,), jnp.int32),
        ],
        compiler_params=PARAMS,
    )(top_parents, pick, parents, gat0, gat1, tp, tpt, basis, j_top, vecs, inv, rf_row, w_row,
      w_other, lmsgs, lmixed, lpt)


def gather_roots(block, groups, hook):
    buf = block[None]
    step = groups // 2
    while step >= 1:
        other = lax.ppermute(buf, "leaf", [(i, i ^ step) for i in range(groups)])
        if step == 1:
            return buf, other
        if step == max(groups // 4, 1):
            buf = hook(buf)
        buf = jnp.stack([buf, other], axis=1).reshape((-1,) + block.shape)
        step //= 2
    return buf, buf


def on_device(
    tips,
    parents,
    branch_lengths,
    top_parents,
    top_lengths,
    weights,
    eig_vectors,
    eig_inverse,
    eig_values,
    labeled_rates,
    root_freq,
):
    groups = lax.axis_size("leaf")
    sites = lax.axis_size("site")
    member_index = lax.axis_index("leaf")
    taxon_count = tips.shape[0] * groups
    lam_row = eig_values[None, :]
    w_row = weights.astype(F32)[None, :]
    if sites == 2:
        w_other = lax.ppermute(w_row, "site", [(0, 1), (1, 0)])
    else:
        w_other = lax.psum(jnp.sum(w_row), "site") - jnp.sum(w_row)
        w_other = jnp.reshape(w_other, (1, 1))

    root_block, msgs, xw, trl = climb(
        parents, branch_lengths, tips, eig_vectors, eig_inverse, lam_row
    )
    paired = groups & (groups - 1) == 0
    j_local = jax.vmap(lambda t: integrals(eig_values, t))(branch_lengths)
    j_top = jax.vmap(lambda t: integrals(eig_values, t))(top_lengths)
    made = {}

    def hook(buf):
        made["m"] = matrices(
            top_lengths, eig_vectors, eig_inverse, labeled_rates, lam_row, j_local, xw, buf
        )
        return made["m"][3]

    if paired:
        halves = gather_roots(root_block, groups, hook)
        pick = jnp.reshape(member_index, (1,)).astype(jnp.int32)
    else:
        gathered = lax.all_gather(root_block, "leaf", axis=0, tiled=False)
        hook(root_block[None])
        halves = (gathered, gathered)
        pick = jnp.zeros((1,), jnp.int32)
    if "m" not in made:
        hook(root_block[None])
    lmixed, tp, basis, _ = made["m"]
    lpt, tpt = trl, tp
    local_row, top_row, loglik = join(
        top_parents, pick, parents, halves, tp, tpt, basis, j_top, eig_vectors, eig_inverse,
        root_freq[None, :], w_row, w_other, msgs, lmixed, lpt, taxon_count, paired,
    )
    local_sum, top_sum = lax.psum((local_row[0], top_row[0]), "site")
    return (local_sum, top_sum, loglik[0])


def solution(mesh):
    placed = (
        P("leaf", None, "site"),
        P("leaf"),
        P("leaf"),
        P(),
        P(),
        P("site"),
        P(),
        P(),
        P(),
        P(),
        P(),
    )
    return jax.shard_map(
        on_device,
        mesh=mesh,
        in_specs=placed,
        out_specs=(P("leaf"), P(), P("site")),
        check_vma=False,
    )
```

```python
import functools

import jax
import jax.numpy as jnp
from jax import lax
from jax.experimental import pallas as pl
from jax.experimental.pallas import tpu as pltpu
from jax.sharding import PartitionSpec as P

CODONS = 61

PRECISE = lax.Precision.HIGHEST
FAST = lax.Precision.HIGH
F32 = jnp.float32
VMEM_LIMIT = 56 * 1024 * 1024
VMEM = pl.BlockSpec(memory_space=pltpu.VMEM)
SMEM = pl.BlockSpec(memory_space=pltpu.SMEM)


def _dot(a, b):
    return jnp.dot(a, b, precision=FAST, preferred_element_type=F32)


def integrals(eig_values, branch):
    spread = (eig_values[:, None] - eig_values[None, :]) * branch
    near_zero = jnp.abs(spread) < 0.0001
    divisor = jnp.where(near_zero, jnp.ones_like(spread), spread)
    growth = jnp.where(
        near_zero, 1.0 + spread / 2.0 + spread * spread / 6.0, jnp.expm1(spread) / divisor
    )
    return branch * jnp.exp(eig_values[None, :] * branch) * growth


PARAMS = pltpu.CompilerParams(vmem_limit_bytes=VMEM_LIMIT)


def _cols(c, columns):
    return slice(c * columns, (c + 1) * columns)


def _climb_kernel(par_ref, len_ref, leaf_ref, v_ref, vi_ref, lam_ref,
                  root_ref, msg_ref, xw_ref, tr_ref, inner_ref):
    leaf_count = leaf_ref.shape[0]
    edge_count, states, columns = msg_ref.shape
    vecs = v_ref[...]
    inv = vi_ref[...]
    lam = lam_ref[...]
    inner_ref[...] = jnp.ones(inner_ref.shape, F32)
    keep = (lax.broadcasted_iota(jnp.int32, (states, columns), 0) < CODONS).astype(F32)
    logs = jnp.zeros((1, columns), F32)
    for c in range(edge_count):
        if c < leaf_count:
            x = leaf_ref[c] * keep
        else:
            x = inner_ref[c - leaf_count]
            big = jnp.max(x, axis=0, keepdims=True)
            x = x / big
            logs = logs + jnp.log(big)
        trans = _dot(vecs * jnp.exp(lam * len_ref[c]), inv)
        tr_ref[c] = trans
        msg = _dot(trans, x)
        msg_ref[c] = msg
        xw_ref[:, _cols(c, columns)] = x
        p = par_ref[c] - leaf_count
        inner_ref[p] = inner_ref[p] * msg
    x = inner_ref[leaf_count - 2]
    big = jnp.max(x, axis=0, keepdims=True)
    root_ref[0:states, :] = x / big
    root_ref[states:states + 1, :] = logs + jnp.log(big)


def climb(parents, lengths, tips, vecs, inv, lam_row):
    leaf_count, states, columns = tips.shape
    edge_count = parents.shape[0]
    return pl.pallas_call(
        _climb_kernel,
        out_shape=(
            jax.ShapeDtypeStruct((states + 1, columns), F32),
            jax.ShapeDtypeStruct((edge_count, states, columns), F32),
            jax.ShapeDtypeStruct((states, edge_count * columns), F32),
            jax.ShapeDtypeStruct((edge_count, states, states), F32),
        ),
        in_specs=[SMEM, SMEM, VMEM, VMEM, VMEM, VMEM],
        out_specs=(VMEM,) * 4,
        scratch_shapes=[pltpu.VMEM((leaf_count - 1, states, columns), F32)],
        compiler_params=PARAMS,
    )(parents, lengths, tips, vecs, inv, lam_row)


def _matrix_kernel(top_len_ref, v_ref, vi_ref, lab_ref, lam_ref, jl_ref, xw_ref, carry_ref,
                   mixed_ref, tp_ref, basis_ref, carried_ref, vw_ref):
    carried_ref[...] = carry_ref[...]
    local_edges, states, columns = mixed_ref.shape
    top_edges = tp_ref.shape[0]
    vecs = v_ref[...]
    inv = vi_ref[...]
    lam = lam_ref[...]
    basis = _dot(_dot(inv, lab_ref[...]), vecs)
    basis_ref[...] = basis
    vw_ref[...] = _dot(inv, xw_ref[...])
    for c in range(local_edges):
        mixed_ref[c] = _dot(basis * jl_ref[c], vw_ref[:, _cols(c, columns)])
    for c in range(top_edges):
        tp_ref[c] = _dot(vecs * jnp.exp(lam * top_len_ref[c]), inv)


def matrices(top_lengths, vecs, inv, labeled, lam_row, j_local, xw, carry):
    local_edges, states, _ = j_local.shape
    columns = xw.shape[1] // local_edges
    top_edges = top_lengths.shape[0]
    sq = (states, states)
    return pl.pallas_call(
        _matrix_kernel,
        out_shape=(
            jax.ShapeDtypeStruct((local_edges, states, columns), F32),
            jax.ShapeDtypeStruct((top_edges,) + sq, F32),
            jax.ShapeDtypeStruct(sq, F32),
            jax.ShapeDtypeStruct(carry.shape, F32),
        ),
        in_specs=[SMEM] + [VMEM] * 7,
        out_specs=(VMEM,) * 4,
        scratch_shapes=[pltpu.VMEM((states, local_edges * columns), F32)],
        compiler_params=PARAMS,
    )(top_lengths, vecs, inv, labeled, lam_row, j_local, xw, carry)


def _lane_put(row, lane, value):
    lanes = lax.broadcasted_iota(jnp.int32, row.shape, 1)
    return jnp.where(lanes == lane, value, row)


def _descend(par_ref, kids_ref, outside_ref, arr_ref, msg_ref, pt_ref, root_out, pick=None):
    edge_count = par_ref.shape[0]
    leaf_count = (edge_count + 2) // 2
    columns = msg_ref.shape[2]
    for n in range(edge_count + 1):
        kids_ref[n] = 0
    for e in range(edge_count):
        p = par_ref[e]
        kids_ref[p] = kids_ref[p] + e
    outside_ref[leaf_count - 2] = root_out

    def arriving_of(c):
        p = par_ref[c]
        s = kids_ref[p] - c
        return outside_ref[p - leaf_count] * msg_ref[s]

    def outward(c, arriving):
        out = lax.dot_general(pt_ref[c], arriving, (((0,), (0,)), ((), ())),
                              precision=FAST, preferred_element_type=F32)
        return out / jnp.max(out, axis=0, keepdims=True)

    for c in range(edge_count - 1, -1, -1):
        arriving = arriving_of(c)
        arr_ref[:, _cols(c, columns)] = arriving
        if c >= leaf_count:
            outside_ref[c - leaf_count] = outward(c, arriving)
    if pick is not None:
        return outward(pick, arriving_of(pick))
    return None


def _counts(row, lane_offset, w, vt, arr_ref, msg_ref, mixed_of):
    edge_count, _, columns = msg_ref.shape
    weighted = _dot(vt, arr_ref[...])
    for c in range(edge_count):
        cols = _cols(c, columns)
        num = jnp.sum(weighted[:, cols] * mixed_of(c), axis=0, keepdims=True)
        den = jnp.sum(arr_ref[:, cols] * msg_ref[c], axis=0, keepdims=True)
        total = jnp.sum(w * num / den, axis=1, keepdims=True)
        row = _lane_put(row, lane_offset + c, total)
    return row


def _join_kernel(tpar_ref, pick_ref, lpar_ref,
                 gat0_ref, gat1_ref, tp_ref, tpt_ref, basis_ref, jt_ref, v_ref, vi_ref, rf_ref,
                 w_ref, wo_ref, lmsg_ref, lmixed_ref, lpt_ref,
                 local_ref, top_ref, loglik_ref,
                 tinner_ref, tmsg_ref, txw_ref, tvw_ref, toutside_ref, tarr_ref,
                 loutside_ref, larr_ref, tkids_ref, lkids_ref, *, taxon_count, paired):
    top_edges = tpar_ref.shape[0]
    leaf_count = (top_edges + 2) // 2
    local_edges = lpar_ref.shape[0]
    states, columns = tmsg_ref.shape[1], tmsg_ref.shape[2]
    g = pick_ref[0]
    tinner_ref[...] = jnp.ones(tinner_ref.shape, F32)
    logs = jnp.zeros((1, columns), F32)
    leaf_logs = jnp.zeros((1, columns), F32)
    for c in range(top_edges):
        if c < leaf_count:
            if paired:
                spot = jnp.bitwise_xor(c, g)
                half = spot // 2
                block = jnp.where(spot % 2 == 0, gat0_ref[half], gat1_ref[half])
            else:
                block = gat0_ref[c]
            x = block[0:states, :]
            leaf_logs = leaf_logs + block[states:states + 1, :]
        else:
            x = tinner_ref[c - leaf_count]
            big = jnp.max(x, axis=0, keepdims=True)
            x = x / big
            logs = logs + jnp.log(big)
        msg = _dot(tp_ref[c], x)
        tmsg_ref[c] = msg
        txw_ref[:, _cols(c, columns)] = x
        p = tpar_ref[c] - leaf_count
        tinner_ref[p] = tinner_ref[p] * msg
    x = tinner_ref[leaf_count - 2]
    big = jnp.max(x, axis=0, keepdims=True)
    logs = logs + jnp.log(big)
    rf = rf_ref[...]
    likelihood = jnp.dot(rf, x / big, precision=PRECISE, preferred_element_type=F32)
    loglik_ref[...] = (jnp.log(likelihood) + logs + leaf_logs) / taxon_count

    eye = (lax.broadcasted_iota(jnp.int32, (states, states), 0)
           == lax.broadcasted_iota(jnp.int32, (states, states), 1))
    rf_col = jnp.sum(jnp.where(eye, rf, 0.0), axis=1, keepdims=True)
    inv = vi_ref[...]
    vt = v_ref[...].T
    basis = basis_ref[...]
    tvw_ref[...] = _dot(inv, txw_ref[...])
    subtree_out = _descend(
        tpar_ref, tkids_ref, toutside_ref, tarr_ref, tmsg_ref, tpt_ref,
        jnp.broadcast_to(rf_col, (states, columns)), pick=g,
    )
    _descend(lpar_ref, lkids_ref, loutside_ref, larr_ref, lmsg_ref, lpt_ref, subtree_out)
    w = w_ref[...]
    weight_total = jnp.sum(w, axis=1, keepdims=True) + jnp.sum(wo_ref[...], axis=1, keepdims=True)
    lanes = max(local_edges, top_edges)
    row = jnp.zeros((1, lanes), F32)
    row = _counts(
        row, 0, w, vt, tarr_ref, tmsg_ref,
        lambda c: _dot(basis * jt_ref[c], tvw_ref[:, _cols(c, columns)]),
    )
    top_ref[...] = row[:, 0:top_edges] / weight_total
    row = jnp.zeros((1, lanes), F32)
    row = _counts(row, 0, w, vt, larr_ref, lmsg_ref, lambda c: lmixed_ref[c])
    local_ref[...] = row[:, 0:local_edges] / weight_total


def join(top_parents, pick, parents, halves, tp, tpt, basis, j_top, vecs, inv, rf_row, w_row,
         w_other, lmsgs, lmixed, lpt, taxon_count, paired):
    gat0, gat1 = halves
    columns = gat0.shape[2]
    top_edges = top_parents.shape[0]
    leaf_count = (top_edges + 2) // 2
    local_edges, states, _ = lmsgs.shape
    local_leaves = (local_edges + 2) // 2
    return pl.pallas_call(
        functools.partial(_join_kernel, taxon_count=taxon_count, paired=paired),
        out_shape=(
            jax.ShapeDtypeStruct((1, local_edges), F32),
            jax.ShapeDtypeStruct((1, top_edges), F32),
            jax.ShapeDtypeStruct((1, columns), F32),
        ),
        in_specs=[SMEM] * 3 + [VMEM] * 14,
        out_specs=(VMEM, VMEM, VMEM),
        scratch_shapes=[
            pltpu.VMEM((leaf_count - 1, states, columns), F32),
            pltpu.VMEM((top_edges, states, columns), F32),
            pltpu.VMEM((states, top_edges * columns), F32),
            pltpu.VMEM((states, top_edges * columns), F32),
            pltpu.VMEM((leaf_count - 1, states, columns), F32),
            pltpu.VMEM((states, top_edges * columns), F32),
            pltpu.VMEM((local_leaves - 1, states, columns), F32),
            pltpu.VMEM((states, local_edges * columns), F32),
            pltpu.SMEM((top_edges + 1,), jnp.int32),
            pltpu.SMEM((local_edges + 1,), jnp.int32),
        ],
        compiler_params=PARAMS,
    )(top_parents, pick, parents, gat0, gat1, tp, tpt, basis, j_top, vecs, inv, rf_row, w_row,
      w_other, lmsgs, lmixed, lpt)


def gather_roots(block, groups, hook):
    buf = block[None]
    step = groups // 2
    while step >= 1:
        other = lax.ppermute(buf, "leaf", [(i, i ^ step) for i in range(groups)])
        if step == 1:
            return buf, other
        if step == max(groups // 8, 1):
            buf = hook(buf)
        buf = jnp.stack([buf, other], axis=1).reshape((-1,) + block.shape)
        step //= 2
    return buf, buf


def on_device(
    tips,
    parents,
    branch_lengths,
    top_parents,
    top_lengths,
    weights,
    eig_vectors,
    eig_inverse,
    eig_values,
    labeled_rates,
    root_freq,
):
    groups = lax.axis_size("leaf")
    sites = lax.axis_size("site")
    member_index = lax.axis_index("leaf")
    taxon_count = tips.shape[0] * groups
    lam_row = eig_values[None, :]
    w_row = weights.astype(F32)[None, :]
    if sites == 2:
        w_other = lax.ppermute(w_row, "site", [(0, 1), (1, 0)])
    else:
        w_other = lax.psum(jnp.sum(w_row), "site") - jnp.sum(w_row)
        w_other = jnp.reshape(w_other, (1, 1))

    root_block, msgs, xw, trl = climb(
        parents, branch_lengths, tips, eig_vectors, eig_inverse, lam_row
    )
    paired = groups & (groups - 1) == 0
    j_local = jax.vmap(lambda t: integrals(eig_values, t))(branch_lengths)
    j_top = jax.vmap(lambda t: integrals(eig_values, t))(top_lengths)
    made = {}

    def hook(buf):
        made["m"] = matrices(
            top_lengths, eig_vectors, eig_inverse, labeled_rates, lam_row, j_local, xw, buf
        )
        return made["m"][3]

    if paired:
        halves = gather_roots(root_block, groups, hook)
        pick = jnp.reshape(member_index, (1,)).astype(jnp.int32)
    else:
        gathered = lax.all_gather(root_block, "leaf", axis=0, tiled=False)
        hook(root_block[None])
        halves = (gathered, gathered)
        pick = jnp.zeros((1,), jnp.int32)
    if "m" not in made:
        hook(root_block[None])
    lmixed, tp, basis, _ = made["m"]
    lpt, tpt = trl, tp
    local_row, top_row, loglik = join(
        top_parents, pick, parents, halves, tp, tpt, basis, j_top, eig_vectors, eig_inverse,
        root_freq[None, :], w_row, w_other, msgs, lmixed, lpt, taxon_count, paired,
    )
    local_sum, top_sum = lax.psum((local_row[0], top_row[0]), "site")
    return (local_sum, top_sum, loglik[0])


def solution(mesh):
    placed = (
        P("leaf", None, "site"),
        P("leaf"),
        P("leaf"),
        P(),
        P(),
        P("site"),
        P(),
        P(),
        P(),
        P(),
        P(),
    )
    return jax.shard_map(
        on_device,
        mesh=mesh,
        in_specs=placed,
        out_specs=(P("leaf"), P(), P("site")),
        check_vma=False,
    )
```

```python
import functools

import jax
import jax.numpy as jnp
from jax import lax
from jax.experimental import pallas as pl
from jax.experimental.pallas import tpu as pltpu
from jax.sharding import PartitionSpec as P

CODONS = 61

PRECISE = lax.Precision.HIGHEST
FAST = lax.Precision.HIGH
F32 = jnp.float32
VMEM_LIMIT = 56 * 1024 * 1024
VMEM = pl.BlockSpec(memory_space=pltpu.VMEM)
SMEM = pl.BlockSpec(memory_space=pltpu.SMEM)


def _dot(a, b):
    return jnp.dot(a, b, precision=FAST, preferred_element_type=F32)


def integrals(eig_values, branch):
    spread = (eig_values[:, None] - eig_values[None, :]) * branch
    near_zero = jnp.abs(spread) < 0.0001
    divisor = jnp.where(near_zero, jnp.ones_like(spread), spread)
    growth = jnp.where(
        near_zero, 1.0 + spread / 2.0 + spread * spread / 6.0, jnp.expm1(spread) / divisor
    )
    return branch * jnp.exp(eig_values[None, :] * branch) * growth


PARAMS = pltpu.CompilerParams(vmem_limit_bytes=VMEM_LIMIT)


def _cols(c, columns):
    return slice(c * columns, (c + 1) * columns)


def _climb_kernel(par_ref, len_ref, leaf_ref, v_ref, vi_ref, lam_ref,
                  root_ref, msg_ref, xw_ref, tr_ref, inner_ref):
    leaf_count = leaf_ref.shape[0]
    edge_count, states, columns = msg_ref.shape
    vecs = v_ref[...]
    inv = vi_ref[...]
    lam = lam_ref[...]
    inner_ref[...] = jnp.ones(inner_ref.shape, F32)
    keep = (lax.broadcasted_iota(jnp.int32, (states, columns), 0) < CODONS).astype(F32)
    logs = jnp.zeros((1, columns), F32)
    for c in range(edge_count):
        if c < leaf_count:
            x = leaf_ref[c] * keep
        else:
            x = inner_ref[c - leaf_count]
            big = jnp.max(x, axis=0, keepdims=True)
            x = x / big
            logs = logs + jnp.log(big)
        trans = _dot(vecs * jnp.exp(lam * len_ref[c]), inv)
        tr_ref[c] = trans
        msg = _dot(trans, x)
        msg_ref[c] = msg
        xw_ref[:, _cols(c, columns)] = x
        p = par_ref[c] - leaf_count
        inner_ref[p] = inner_ref[p] * msg
    x = inner_ref[leaf_count - 2]
    big = jnp.max(x, axis=0, keepdims=True)
    root_ref[0:states, :] = x / big
    root_ref[states:states + 1, :] = logs + jnp.log(big)


def climb(parents, lengths, tips, vecs, inv, lam_row):
    leaf_count, states, columns = tips.shape
    edge_count = parents.shape[0]
    return pl.pallas_call(
        _climb_kernel,
        out_shape=(
            jax.ShapeDtypeStruct((states + 1, columns), F32),
            jax.ShapeDtypeStruct((edge_count, states, columns), F32),
            jax.ShapeDtypeStruct((states, edge_count * columns), F32),
            jax.ShapeDtypeStruct((edge_count, states, states), F32),
        ),
        in_specs=[SMEM, SMEM, VMEM, VMEM, VMEM, VMEM],
        out_specs=(VMEM,) * 4,
        scratch_shapes=[pltpu.VMEM((leaf_count - 1, states, columns), F32)],
        compiler_params=PARAMS,
    )(parents, lengths, tips, vecs, inv, lam_row)


def _matrix_kernel(top_len_ref, v_ref, vi_ref, lab_ref, lam_ref, jl_ref, xw_ref, carry_ref,
                   mixed_ref, tp_ref, basis_ref, carried_ref, vw_ref):
    carried_ref[...] = carry_ref[...]
    local_edges, states, columns = mixed_ref.shape
    top_edges = tp_ref.shape[0]
    vecs = v_ref[...]
    inv = vi_ref[...]
    lam = lam_ref[...]
    basis = _dot(_dot(inv, lab_ref[...]), vecs)
    basis_ref[...] = basis
    vw_ref[...] = _dot(inv, xw_ref[...])
    for c in range(local_edges):
        mixed_ref[c] = _dot(basis * jl_ref[c], vw_ref[:, _cols(c, columns)])
    for c in range(top_edges):
        tp_ref[c] = _dot(vecs * jnp.exp(lam * top_len_ref[c]), inv)


def matrices(top_lengths, vecs, inv, labeled, lam_row, j_all, xw, carry):
    local_edges = j_all.shape[0] - top_lengths.shape[0]
    states = j_all.shape[1]
    columns = xw.shape[1] // local_edges
    top_edges = top_lengths.shape[0]
    sq = (states, states)
    return pl.pallas_call(
        _matrix_kernel,
        out_shape=(
            jax.ShapeDtypeStruct((local_edges, states, columns), F32),
            jax.ShapeDtypeStruct((top_edges,) + sq, F32),
            jax.ShapeDtypeStruct(sq, F32),
            jax.ShapeDtypeStruct(carry.shape, F32),
        ),
        in_specs=[SMEM] + [VMEM] * 7,
        out_specs=(VMEM,) * 4,
        scratch_shapes=[pltpu.VMEM((states, local_edges * columns), F32)],
        compiler_params=PARAMS,
    )(top_lengths, vecs, inv, labeled, lam_row, j_all, xw, carry)


def _lane_put(row, lane, value):
    lanes = lax.broadcasted_iota(jnp.int32, row.shape, 1)
    return jnp.where(lanes == lane, value, row)


def _descend(par_ref, kids_ref, outside_ref, arr_ref, msg_ref, pt_ref, root_out, pick=None):
    edge_count = par_ref.shape[0]
    leaf_count = (edge_count + 2) // 2
    columns = msg_ref.shape[2]
    for n in range(edge_count + 1):
        kids_ref[n] = 0
    for e in range(edge_count):
        p = par_ref[e]
        kids_ref[p] = kids_ref[p] + e
    outside_ref[leaf_count - 2] = root_out

    def arriving_of(c):
        p = par_ref[c]
        s = kids_ref[p] - c
        return outside_ref[p - leaf_count] * msg_ref[s]

    def outward(c, arriving):
        out = lax.dot_general(pt_ref[c], arriving, (((0,), (0,)), ((), ())),
                              precision=FAST, preferred_element_type=F32)
        return out / jnp.max(out, axis=0, keepdims=True)

    for c in range(edge_count - 1, -1, -1):
        arriving = arriving_of(c)
        arr_ref[:, _cols(c, columns)] = arriving
        if c >= leaf_count:
            outside_ref[c - leaf_count] = outward(c, arriving)
    if pick is not None:
        return outward(pick, arriving_of(pick))
    return None


def _counts(row, lane_offset, w, vt, arr_ref, msg_ref, mixed_of):
    edge_count, _, columns = msg_ref.shape
    weighted = _dot(vt, arr_ref[...])
    for c in range(edge_count):
        cols = _cols(c, columns)
        num = jnp.sum(weighted[:, cols] * mixed_of(c), axis=0, keepdims=True)
        den = jnp.sum(arr_ref[:, cols] * msg_ref[c], axis=0, keepdims=True)
        total = jnp.sum(w * num / den, axis=1, keepdims=True)
        row = _lane_put(row, lane_offset + c, total)
    return row


def _join_kernel(tpar_ref, pick_ref, lpar_ref,
                 gat0_ref, gat1_ref, tp_ref, tpt_ref, basis_ref, jt_ref, v_ref, vi_ref, rf_ref,
                 w_ref, wo_ref, lmsg_ref, lmixed_ref, lpt_ref,
                 local_ref, top_ref, loglik_ref,
                 tinner_ref, tmsg_ref, txw_ref, tvw_ref, toutside_ref, tarr_ref,
                 loutside_ref, larr_ref, tkids_ref, lkids_ref, *, taxon_count, paired):
    top_edges = tpar_ref.shape[0]
    leaf_count = (top_edges + 2) // 2
    local_edges = lpar_ref.shape[0]
    states, columns = tmsg_ref.shape[1], tmsg_ref.shape[2]
    g = pick_ref[0]
    tinner_ref[...] = jnp.ones(tinner_ref.shape, F32)
    logs = jnp.zeros((1, columns), F32)
    leaf_logs = jnp.zeros((1, columns), F32)
    for c in range(top_edges):
        if c < leaf_count:
            if paired:
                spot = jnp.bitwise_xor(c, g)
                half = spot // 2
                block = jnp.where(spot % 2 == 0, gat0_ref[half], gat1_ref[half])
            else:
                block = gat0_ref[c]
            x = block[0:states, :]
            leaf_logs = leaf_logs + block[states:states + 1, :]
        else:
            x = tinner_ref[c - leaf_count]
            big = jnp.max(x, axis=0, keepdims=True)
            x = x / big
            logs = logs + jnp.log(big)
        msg = _dot(tp_ref[c], x)
        tmsg_ref[c] = msg
        txw_ref[:, _cols(c, columns)] = x
        p = tpar_ref[c] - leaf_count
        tinner_ref[p] = tinner_ref[p] * msg
    x = tinner_ref[leaf_count - 2]
    big = jnp.max(x, axis=0, keepdims=True)
    logs = logs + jnp.log(big)
    rf = rf_ref[...]
    likelihood = jnp.dot(rf, x / big, precision=PRECISE, preferred_element_type=F32)
    loglik_ref[...] = (jnp.log(likelihood) + logs + leaf_logs) / taxon_count

    eye = (lax.broadcasted_iota(jnp.int32, (states, states), 0)
           == lax.broadcasted_iota(jnp.int32, (states, states), 1))
    rf_col = jnp.sum(jnp.where(eye, rf, 0.0), axis=1, keepdims=True)
    inv = vi_ref[...]
    vt = v_ref[...].T
    basis = basis_ref[...]
    tvw_ref[...] = _dot(inv, txw_ref[...])
    subtree_out = _descend(
        tpar_ref, tkids_ref, toutside_ref, tarr_ref, tmsg_ref, tpt_ref,
        jnp.broadcast_to(rf_col, (states, columns)), pick=g,
    )
    _descend(lpar_ref, lkids_ref, loutside_ref, larr_ref, lmsg_ref, lpt_ref, subtree_out)
    w = w_ref[...]
    weight_total = jnp.sum(w, axis=1, keepdims=True) + jnp.sum(wo_ref[...], axis=1, keepdims=True)
    lanes = max(local_edges, top_edges)
    row = jnp.zeros((1, lanes), F32)
    row = _counts(
        row, 0, w, vt, tarr_ref, tmsg_ref,
        lambda c: _dot(basis * jt_ref[local_edges + c], tvw_ref[:, _cols(c, columns)]),
    )
    top_ref[...] = row[:, 0:top_edges] / weight_total
    row = jnp.zeros((1, lanes), F32)
    row = _counts(row, 0, w, vt, larr_ref, lmsg_ref, lambda c: lmixed_ref[c])
    local_ref[...] = row[:, 0:local_edges] / weight_total


def join(top_parents, pick, parents, halves, tp, tpt, basis, j_top, vecs, inv, rf_row, w_row,
         w_other, lmsgs, lmixed, lpt, taxon_count, paired):
    gat0, gat1 = halves
    columns = gat0.shape[2]
    top_edges = top_parents.shape[0]
    leaf_count = (top_edges + 2) // 2
    local_edges, states, _ = lmsgs.shape
    local_leaves = (local_edges + 2) // 2
    return pl.pallas_call(
        functools.partial(_join_kernel, taxon_count=taxon_count, paired=paired),
        out_shape=(
            jax.ShapeDtypeStruct((1, local_edges), F32),
            jax.ShapeDtypeStruct((1, top_edges), F32),
            jax.ShapeDtypeStruct((1, columns), F32),
        ),
        in_specs=[SMEM] * 3 + [VMEM] * 14,
        out_specs=(VMEM, VMEM, VMEM),
        scratch_shapes=[
            pltpu.VMEM((leaf_count - 1, states, columns), F32),
            pltpu.VMEM((top_edges, states, columns), F32),
            pltpu.VMEM((states, top_edges * columns), F32),
            pltpu.VMEM((states, top_edges * columns), F32),
            pltpu.VMEM((leaf_count - 1, states, columns), F32),
            pltpu.VMEM((states, top_edges * columns), F32),
            pltpu.VMEM((local_leaves - 1, states, columns), F32),
            pltpu.VMEM((states, local_edges * columns), F32),
            pltpu.SMEM((top_edges + 1,), jnp.int32),
            pltpu.SMEM((local_edges + 1,), jnp.int32),
        ],
        compiler_params=PARAMS,
    )(top_parents, pick, parents, gat0, gat1, tp, tpt, basis, j_top, vecs, inv, rf_row, w_row,
      w_other, lmsgs, lmixed, lpt)


def gather_roots(block, groups, hook):
    buf = block[None]
    step = groups // 2
    while step >= 1:
        other = lax.ppermute(buf, "leaf", [(i, i ^ step) for i in range(groups)])
        if step == 1:
            return buf, other
        if step == max(groups // 8, 1):
            buf = hook(buf)
        buf = jnp.stack([buf, other], axis=1).reshape((-1,) + block.shape)
        step //= 2
    return buf, buf


def on_device(
    tips,
    parents,
    branch_lengths,
    top_parents,
    top_lengths,
    weights,
    eig_vectors,
    eig_inverse,
    eig_values,
    labeled_rates,
    root_freq,
):
    groups = lax.axis_size("leaf")
    sites = lax.axis_size("site")
    member_index = lax.axis_index("leaf")
    taxon_count = tips.shape[0] * groups
    lam_row = eig_values[None, :]
    w_row = weights.astype(F32)[None, :]
    if sites == 2:
        w_other = lax.ppermute(w_row, "site", [(0, 1), (1, 0)])
    else:
        w_other = lax.psum(jnp.sum(w_row), "site") - jnp.sum(w_row)
        w_other = jnp.reshape(w_other, (1, 1))

    root_block, msgs, xw, trl = climb(
        parents, branch_lengths, tips, eig_vectors, eig_inverse, lam_row
    )
    paired = groups & (groups - 1) == 0
    j_all = jax.vmap(lambda t: integrals(eig_values, t))(
        jnp.concatenate([branch_lengths, top_lengths])
    )
    made = {}

    def hook(buf):
        made["m"] = matrices(
            top_lengths, eig_vectors, eig_inverse, labeled_rates, lam_row, j_all, xw, buf
        )
        return made["m"][3]

    if paired:
        halves = gather_roots(root_block, groups, hook)
        pick = jnp.reshape(member_index, (1,)).astype(jnp.int32)
    else:
        gathered = lax.all_gather(root_block, "leaf", axis=0, tiled=False)
        hook(root_block[None])
        halves = (gathered, gathered)
        pick = jnp.zeros((1,), jnp.int32)
    if "m" not in made:
        hook(root_block[None])
    lmixed, tp, basis, _ = made["m"]
    lpt, tpt = trl, tp
    local_row, top_row, loglik = join(
        top_parents, pick, parents, halves, tp, tpt, basis, j_all, eig_vectors, eig_inverse,
        root_freq[None, :], w_row, w_other, msgs, lmixed, lpt, taxon_count, paired,
    )
    local_sum, top_sum = lax.psum((local_row[0], top_row[0]), "site")
    return (local_sum, top_sum, loglik[0])


def solution(mesh):
    placed = (
        P("leaf", None, "site"),
        P("leaf"),
        P("leaf"),
        P(),
        P(),
        P("site"),
        P(),
        P(),
        P(),
        P(),
        P(),
    )
    return jax.shard_map(
        on_device,
        mesh=mesh,
        in_specs=placed,
        out_specs=(P("leaf"), P(), P("site")),
        check_vma=False,
    )
```

```python
import functools

import jax
import jax.numpy as jnp
from jax import lax
from jax.experimental import pallas as pl
from jax.experimental.pallas import tpu as pltpu
from jax.sharding import PartitionSpec as P

CODONS = 61

PRECISE = lax.Precision.HIGHEST
FAST = lax.Precision.HIGH
F32 = jnp.float32
VMEM_LIMIT = 56 * 1024 * 1024
VMEM = pl.BlockSpec(memory_space=pltpu.VMEM)
SMEM = pl.BlockSpec(memory_space=pltpu.SMEM)


def _dot(a, b):
    return jnp.dot(a, b, precision=FAST, preferred_element_type=F32)


def integrals(eig_values, branch):
    spread = (eig_values[:, None] - eig_values[None, :]) * branch
    near_zero = jnp.abs(spread) < 0.0001
    divisor = jnp.where(near_zero, jnp.ones_like(spread), spread)
    growth = jnp.where(
        near_zero, 1.0 + spread / 2.0 + spread * spread / 6.0, jnp.expm1(spread) / divisor
    )
    return branch * jnp.exp(eig_values[None, :] * branch) * growth


PARAMS = pltpu.CompilerParams(vmem_limit_bytes=VMEM_LIMIT)


def _cols(c, columns):
    return slice(c * columns, (c + 1) * columns)


def _climb_kernel(par_ref, len_ref, leaf_ref, v_ref, vi_ref, lam_ref,
                  root_ref, msg_ref, xw_ref, tr_ref, inner_ref):
    leaf_count = leaf_ref.shape[0]
    edge_count, states, columns = msg_ref.shape
    vecs = v_ref[...]
    inv = vi_ref[...]
    lam = lam_ref[...]
    inner_ref[...] = jnp.ones(inner_ref.shape, F32)
    keep = (lax.broadcasted_iota(jnp.int32, (states, columns), 0) < CODONS).astype(F32)
    logs = jnp.zeros((1, columns), F32)
    for c in range(edge_count):
        if c < leaf_count:
            x = leaf_ref[c] * keep
        else:
            x = inner_ref[c - leaf_count]
            big = jnp.max(x, axis=0, keepdims=True)
            x = x / big
            logs = logs + jnp.log(big)
        trans = _dot(vecs * jnp.exp(lam * len_ref[c]), inv)
        tr_ref[c] = trans
        msg = _dot(trans, x)
        msg_ref[c] = msg
        xw_ref[:, _cols(c, columns)] = x
        p = par_ref[c] - leaf_count
        inner_ref[p] = inner_ref[p] * msg
    x = inner_ref[leaf_count - 2]
    big = jnp.max(x, axis=0, keepdims=True)
    root_ref[0:states, :] = x / big
    root_ref[states:states + 1, :] = logs + jnp.log(big)


def climb(parents, lengths, tips, vecs, inv, lam_row):
    leaf_count, states, columns = tips.shape
    edge_count = parents.shape[0]
    return pl.pallas_call(
        _climb_kernel,
        out_shape=(
            jax.ShapeDtypeStruct((states + 1, columns), F32),
            jax.ShapeDtypeStruct((edge_count, states, columns), F32),
            jax.ShapeDtypeStruct((states, edge_count * columns), F32),
            jax.ShapeDtypeStruct((edge_count, states, states), F32),
        ),
        in_specs=[SMEM, SMEM, VMEM, VMEM, VMEM, VMEM],
        out_specs=(VMEM,) * 4,
        scratch_shapes=[pltpu.VMEM((leaf_count - 1, states, columns), F32)],
        compiler_params=PARAMS,
    )(parents, lengths, tips, vecs, inv, lam_row)


def _matrix_kernel(top_len_ref, v_ref, vi_ref, lab_ref, lam_ref, jl_ref, xw_ref, carry_ref,
                   mixed_ref, tp_ref, basis_ref, carried_ref, vw_ref):
    carried_ref[...] = carry_ref[...]
    local_edges, states, columns = mixed_ref.shape
    top_edges = tp_ref.shape[0]
    vecs = v_ref[...]
    inv = vi_ref[...]
    lam = lam_ref[...]
    basis = _dot(_dot(inv, lab_ref[...]), vecs)
    basis_ref[...] = basis
    vw_ref[...] = _dot(inv, xw_ref[...])
    for c in range(local_edges):
        mixed_ref[c] = _dot(basis * jl_ref[c], vw_ref[:, _cols(c, columns)])
    for c in range(top_edges):
        tp_ref[c] = _dot(vecs * jnp.exp(lam * top_len_ref[c]), inv)


def matrices(top_lengths, vecs, inv, labeled, lam_row, j_local, xw, carry):
    local_edges, states, _ = j_local.shape
    columns = xw.shape[1] // local_edges
    top_edges = top_lengths.shape[0]
    sq = (states, states)
    return pl.pallas_call(
        _matrix_kernel,
        out_shape=(
            jax.ShapeDtypeStruct((local_edges, states, columns), F32),
            jax.ShapeDtypeStruct((top_edges,) + sq, F32),
            jax.ShapeDtypeStruct(sq, F32),
            jax.ShapeDtypeStruct(carry.shape, F32),
        ),
        in_specs=[SMEM] + [VMEM] * 7,
        out_specs=(VMEM,) * 4,
        scratch_shapes=[pltpu.VMEM((states, local_edges * columns), F32)],
        compiler_params=PARAMS,
    )(top_lengths, vecs, inv, labeled, lam_row, j_local, xw, carry)


def _relay_kernel(a_ref, b_ref, a_out_ref, b_out_ref):
    a_out_ref[...] = a_ref[...]
    b_out_ref[...] = b_ref[...]


def relay(a, b):
    return pl.pallas_call(
        _relay_kernel,
        out_shape=(jax.ShapeDtypeStruct(a.shape, F32), jax.ShapeDtypeStruct(b.shape, F32)),
        in_specs=[VMEM, VMEM],
        out_specs=(VMEM, VMEM),
        compiler_params=PARAMS,
    )(a, b)


def _lane_put(row, lane, value):
    lanes = lax.broadcasted_iota(jnp.int32, row.shape, 1)
    return jnp.where(lanes == lane, value, row)


def _descend(par_ref, kids_ref, outside_ref, arr_ref, msg_ref, pt_ref, root_out, pick=None):
    edge_count = par_ref.shape[0]
    leaf_count = (edge_count + 2) // 2
    columns = msg_ref.shape[2]
    for n in range(edge_count + 1):
        kids_ref[n] = 0
    for e in range(edge_count):
        p = par_ref[e]
        kids_ref[p] = kids_ref[p] + e
    outside_ref[leaf_count - 2] = root_out

    def arriving_of(c):
        p = par_ref[c]
        s = kids_ref[p] - c
        return outside_ref[p - leaf_count] * msg_ref[s]

    def outward(c, arriving):
        out = lax.dot_general(pt_ref[c], arriving, (((0,), (0,)), ((), ())),
                              precision=FAST, preferred_element_type=F32)
        return out / jnp.max(out, axis=0, keepdims=True)

    for c in range(edge_count - 1, -1, -1):
        arriving = arriving_of(c)
        arr_ref[:, _cols(c, columns)] = arriving
        if c >= leaf_count:
            outside_ref[c - leaf_count] = outward(c, arriving)
    if pick is not None:
        return outward(pick, arriving_of(pick))
    return None


def _counts(row, lane_offset, w, vt, arr_ref, msg_ref, mixed_of):
    edge_count, _, columns = msg_ref.shape
    weighted = _dot(vt, arr_ref[...])
    for c in range(edge_count):
        cols = _cols(c, columns)
        num = jnp.sum(weighted[:, cols] * mixed_of(c), axis=0, keepdims=True)
        den = jnp.sum(arr_ref[:, cols] * msg_ref[c], axis=0, keepdims=True)
        total = jnp.sum(w * num / den, axis=1, keepdims=True)
        row = _lane_put(row, lane_offset + c, total)
    return row


def _join_kernel(tpar_ref, pick_ref, lpar_ref,
                 gat0_ref, gat1_ref, tp_ref, tpt_ref, basis_ref, jt_ref, v_ref, vi_ref, rf_ref,
                 w_ref, wo_ref, lmsg_ref, lmixed_ref, lpt_ref,
                 local_ref, top_ref, loglik_ref,
                 tinner_ref, tmsg_ref, txw_ref, tvw_ref, toutside_ref, tarr_ref,
                 loutside_ref, larr_ref, tkids_ref, lkids_ref, *, taxon_count, paired):
    top_edges = tpar_ref.shape[0]
    leaf_count = (top_edges + 2) // 2
    local_edges = lpar_ref.shape[0]
    states, columns = tmsg_ref.shape[1], tmsg_ref.shape[2]
    g = pick_ref[0]
    tinner_ref[...] = jnp.ones(tinner_ref.shape, F32)
    logs = jnp.zeros((1, columns), F32)
    leaf_logs = jnp.zeros((1, columns), F32)
    for c in range(top_edges):
        if c < leaf_count:
            if paired:
                spot = jnp.bitwise_xor(c, g)
                half = spot // 2
                block = jnp.where(spot % 2 == 0, gat0_ref[half], gat1_ref[half])
            else:
                block = gat0_ref[c]
            x = block[0:states, :]
            leaf_logs = leaf_logs + block[states:states + 1, :]
        else:
            x = tinner_ref[c - leaf_count]
            big = jnp.max(x, axis=0, keepdims=True)
            x = x / big
            logs = logs + jnp.log(big)
        msg = _dot(tp_ref[c], x)
        tmsg_ref[c] = msg
        txw_ref[:, _cols(c, columns)] = x
        p = tpar_ref[c] - leaf_count
        tinner_ref[p] = tinner_ref[p] * msg
    x = tinner_ref[leaf_count - 2]
    big = jnp.max(x, axis=0, keepdims=True)
    logs = logs + jnp.log(big)
    rf = rf_ref[...]
    likelihood = jnp.dot(rf, x / big, precision=PRECISE, preferred_element_type=F32)
    loglik_ref[...] = (jnp.log(likelihood) + logs + leaf_logs) / taxon_count

    eye = (lax.broadcasted_iota(jnp.int32, (states, states), 0)
           == lax.broadcasted_iota(jnp.int32, (states, states), 1))
    rf_col = jnp.sum(jnp.where(eye, rf, 0.0), axis=1, keepdims=True)
    inv = vi_ref[...]
    vt = v_ref[...].T
    basis = basis_ref[...]
    tvw_ref[...] = _dot(inv, txw_ref[...])
    subtree_out = _descend(
        tpar_ref, tkids_ref, toutside_ref, tarr_ref, tmsg_ref, tpt_ref,
        jnp.broadcast_to(rf_col, (states, columns)), pick=g,
    )
    _descend(lpar_ref, lkids_ref, loutside_ref, larr_ref, lmsg_ref, lpt_ref, subtree_out)
    w = w_ref[...]
    weight_total = jnp.sum(w, axis=1, keepdims=True) + jnp.sum(wo_ref[...], axis=1, keepdims=True)
    lanes = max(local_edges, top_edges)
    row = jnp.zeros((1, lanes), F32)
    row = _counts(
        row, 0, w, vt, tarr_ref, tmsg_ref,
        lambda c: _dot(basis * jt_ref[c], tvw_ref[:, _cols(c, columns)]),
    )
    top_ref[...] = row[:, 0:top_edges] / weight_total
    row = jnp.zeros((1, lanes), F32)
    row = _counts(row, 0, w, vt, larr_ref, lmsg_ref, lambda c: lmixed_ref[c])
    local_ref[...] = row[:, 0:local_edges] / weight_total


def join(top_parents, pick, parents, halves, tp, tpt, basis, j_top, vecs, inv, rf_row, w_row,
         w_other, lmsgs, lmixed, lpt, taxon_count, paired):
    gat0, gat1 = halves
    columns = gat0.shape[2]
    top_edges = top_parents.shape[0]
    leaf_count = (top_edges + 2) // 2
    local_edges, states, _ = lmsgs.shape
    local_leaves = (local_edges + 2) // 2
    return pl.pallas_call(
        functools.partial(_join_kernel, taxon_count=taxon_count, paired=paired),
        out_shape=(
            jax.ShapeDtypeStruct((1, local_edges), F32),
            jax.ShapeDtypeStruct((1, top_edges), F32),
            jax.ShapeDtypeStruct((1, columns), F32),
        ),
        in_specs=[SMEM] * 3 + [VMEM] * 14,
        out_specs=(VMEM, VMEM, VMEM),
        scratch_shapes=[
            pltpu.VMEM((leaf_count - 1, states, columns), F32),
            pltpu.VMEM((top_edges, states, columns), F32),
            pltpu.VMEM((states, top_edges * columns), F32),
            pltpu.VMEM((states, top_edges * columns), F32),
            pltpu.VMEM((leaf_count - 1, states, columns), F32),
            pltpu.VMEM((states, top_edges * columns), F32),
            pltpu.VMEM((local_leaves - 1, states, columns), F32),
            pltpu.VMEM((states, local_edges * columns), F32),
            pltpu.SMEM((top_edges + 1,), jnp.int32),
            pltpu.SMEM((local_edges + 1,), jnp.int32),
        ],
        compiler_params=PARAMS,
    )(top_parents, pick, parents, gat0, gat1, tp, tpt, basis, j_top, vecs, inv, rf_row, w_row,
      w_other, lmsgs, lmixed, lpt)


def gather_roots(block, groups, hook, early_hook):
    buf = block[None]
    step = groups // 2
    while step >= 1:
        other = lax.ppermute(buf, "leaf", [(i, i ^ step) for i in range(groups)])
        if step == 1:
            return buf, other
        if step == max(groups // 8, 1):
            buf = hook(buf)
        elif step == groups // 4:
            buf = early_hook(buf)
        buf = jnp.stack([buf, other], axis=1).reshape((-1,) + block.shape)
        step //= 2
    return buf, buf


def on_device(
    tips,
    parents,
    branch_lengths,
    top_parents,
    top_lengths,
    weights,
    eig_vectors,
    eig_inverse,
    eig_values,
    labeled_rates,
    root_freq,
):
    groups = lax.axis_size("leaf")
    sites = lax.axis_size("site")
    member_index = lax.axis_index("leaf")
    taxon_count = tips.shape[0] * groups
    lam_row = eig_values[None, :]
    w_row = weights.astype(F32)[None, :]
    if sites == 2:
        w_other = lax.ppermute(w_row, "site", [(0, 1), (1, 0)])
    else:
        w_other = lax.psum(jnp.sum(w_row), "site") - jnp.sum(w_row)
        w_other = jnp.reshape(w_other, (1, 1))

    root_block, msgs, xw, trl = climb(
        parents, branch_lengths, tips, eig_vectors, eig_inverse, lam_row
    )
    paired = groups & (groups - 1) == 0
    j_local = jax.vmap(lambda t: integrals(eig_values, t))(branch_lengths)
    j_top = jax.vmap(lambda t: integrals(eig_values, t))(top_lengths)
    made = {}

    def hook(buf):
        made["m"] = matrices(
            top_lengths, eig_vectors, eig_inverse, labeled_rates, lam_row, j_local, xw, buf
        )
        return made["m"][3]

    def early_hook(buf):
        buf, made["j"] = relay(buf, j_top)
        return buf

    if paired:
        halves = gather_roots(root_block, groups, hook, early_hook)
        pick = jnp.reshape(member_index, (1,)).astype(jnp.int32)
    else:
        gathered = lax.all_gather(root_block, "leaf", axis=0, tiled=False)
        hook(root_block[None])
        halves = (gathered, gathered)
        pick = jnp.zeros((1,), jnp.int32)
    if "m" not in made:
        hook(root_block[None])
    lmixed, tp, basis, _ = made["m"]
    j_top = made.get("j", j_top)
    lpt, tpt = trl, tp
    local_row, top_row, loglik = join(
        top_parents, pick, parents, halves, tp, tpt, basis, j_top, eig_vectors, eig_inverse,
        root_freq[None, :], w_row, w_other, msgs, lmixed, lpt, taxon_count, paired,
    )
    local_sum, top_sum = lax.psum((local_row[0], top_row[0]), "site")
    return (local_sum, top_sum, loglik[0])


def solution(mesh):
    placed = (
        P("leaf", None, "site"),
        P("leaf"),
        P("leaf"),
        P(),
        P(),
        P("site"),
        P(),
        P(),
        P(),
        P(),
        P(),
    )
    return jax.shard_map(
        on_device,
        mesh=mesh,
        in_specs=placed,
        out_specs=(P("leaf"), P(), P("site")),
        check_vma=False,
    )
```
